32 devices in a mesh: lat: 8 (over z, x), lon: 4 (over y, core).
Axes of the slice: x: 2, y: 2, z: 4, core: 2. Of those that a mesh axis runs over, the one named last changes fastest.
Arguments:
- heat_anomaly: float32 [75, 64, 512], P(None, 'lat', 'lon'), may hold values from -6 to 6
- brine_anomaly: float32 [75, 64, 512], P(None, 'lat', 'lon'), may hold values from -6 to 6
- eastward_current: float32 [75, 64, 512], P(None, 'lat', 'lon'), may hold values from -6 to 6
- northward_current: float32 [75, 64, 512], P(None, 'lat', 'lon'), may hold values from -6 to 6
- shoreline_indicator: int32 [64, 512], P('lat', 'lon'), may hold values from 0 to 1, as said below
- bottom_layer_index: int32 [64, 512], P('lat', 'lon'), may hold values from 1 to 75
- boundary_fluxes: float32 [4, 64, 512], P(None, 'lat', 'lon'), may hold values from -6 to 6
Outputs:
- next_temperature: float32 [75, 64, 512], P(None, 'lat', 'lon')
- next_salinity: float32 [75, 64, 512], P(None, 'lat', 'lon')
- next_zonal: float32 [75, 64, 512], P(None, 'lat', 'lon')
- next_merid: float32 [75, 64, 512], P(None, 'lat', 'lon')
The draws below stay inside these ranges and needn't reach their ends.
Inputs may be any that keep to these rules, and one draw needn't show every extreme that they name: `shoreline_indicator`: 1 marks a sea column and 0 a land column. `bottom_layer_index`: the number of wet levels of a sea column; ignored on land.
All inputs are finite; a program needn't handle non-finite values.
Results may differ from the reference program's by a relative error of at most 0.0003.
Values sent between devices are 32-bit elements; how exact they have to be, the bound alone decides.
No kernel may reach another device: no remote copies, remote signals or barrier semaphores. Data moves between devices by JAX's collectives and lax.ppermute only.
A program may use at most 64 MiB of HBM per device.

```python
import jax
import jax.numpy as jnp
from jax import lax

DEPTH_LAYERS = 75
CX = 128
NORTHSOUTH_SIZE = 64
EASTWEST_SIZE = 512
N_LON = 4


def draw_shoreline_indicator(key, part):
    coarse_key, fine_key = jax.random.split(jax.random.fold_in(key, 11))
    coarse = jax.random.randint(coarse_key, (NORTHSOUTH_SIZE // 8, EASTWEST_SIZE // 8), 0, 4)
    fine = jax.random.randint(fine_key, (NORTHSOUTH_SIZE, EASTWEST_SIZE), 0, 10)
    coarse_full = jnp.repeat(jnp.repeat(coarse, 8, axis=0), 8, axis=1)
    return ((coarse_full > 0) & (fine > 0)).astype(jnp.int32)


def touch_ends(result, rng, smallest, largest):
    dims = result.shape
    spot = [jax.random.randint(jax.random.fold_in(rng, axis), (), 0, dims[axis]) for axis in range(len(dims))]
    result = result.at[tuple(spot)].set(smallest)
    longest = dims.index(max(dims))
    spot[longest] = (spot[longest] + 1) % dims[longest]
    return result.at[tuple(spot)].set(largest)


def levels(key, extent, pieces, least, high):
    gain, own = 1.0, jax.random.fold_in(key, 6)
    for position, blocks in pieces:
        heights = jnp.exp(jax.random.uniform(jax.random.fold_in(own, position), (blocks,), jnp.float32, least / len(pieces), high / len(pieces)))
        gain = gain * jnp.repeat(heights, extent[position] // blocks).reshape([-1 if axis == position else 1 for axis in range(len(extent))])
    return gain


def gaussian(key, dims, deviation, limit, pieces=(), held_as=jnp.bfloat16):
    values = jax.random.normal(key, dims, jnp.float32) * deviation
    if len(pieces) > 0:
        values = levels(key, dims, pieces, -0.22, 0.18) * values
    return jnp.clip(values, min=-limit, max=limit).astype(held_as)


def setup_inputs(seed: int = 0) -> dict:
    key_of = jax.random.split(jax.random.key(seed), 8)
    return {
        "heat_anomaly": gaussian(key_of[0], (DEPTH_LAYERS, NORTHSOUTH_SIZE, EASTWEST_SIZE), 1.0, 6.0, ((1, 8), (2, 4)), jnp.float32),
        "brine_anomaly": gaussian(key_of[1], (DEPTH_LAYERS, NORTHSOUTH_SIZE, EASTWEST_SIZE), 1.0, 6.0, ((1, 8), (2, 4)), jnp.float32),
        "eastward_current": gaussian(key_of[2], (DEPTH_LAYERS, NORTHSOUTH_SIZE, EASTWEST_SIZE), 1.0, 6.0, ((1, 8), (2, 4)), jnp.float32),
        "northward_current": gaussian(key_of[3], (DEPTH_LAYERS, NORTHSOUTH_SIZE, EASTWEST_SIZE), 1.0, 6.0, ((1, 8), (2, 4)), jnp.float32),
        "shoreline_indicator": draw_shoreline_indicator(jax.random.fold_in(key_of[7], 71), 0),
        "bottom_layer_index": touch_ends(jax.random.randint(key_of[5], (NORTHSOUTH_SIZE, EASTWEST_SIZE), 1, DEPTH_LAYERS + 1), jax.random.fold_in(key_of[5], 1), 1, DEPTH_LAYERS).astype(jnp.int32),
        "boundary_fluxes": gaussian(key_of[6], (4, NORTHSOUTH_SIZE, EASTWEST_SIZE), 1.0, 6.0, ((1, 8), (2, 4)), jnp.float32),
    }


courant = 0.25
time_step = 0.2
gravity = 0.2
coriolis = 0.5
thermal = 0.6
thermal_sq = 0.1
haline = 0.8
mix_back = 5.0
mix_conv = 60.0
strat_scale = 2.0
momentum_mix = 2.0
bottom_drag = 1.0
surface_gain = 0.5


def layer_thick(layered_profile):
    offsets = jnp.arange(layered_profile, dtype=jnp.float32) + 0.5
    return 0.5 + offsets / layered_profile, offsets / layered_profile


def density(warmth, saltiness, depth_column):
    return -thermal * warmth * (1.0 + thermal_sq * warmth + depth_column) + haline * saltiness


def pressure(rho_cells, thickness):
    layer_load = rho_cells * thickness[:, None, None]
    return jnp.cumsum(layer_load, axis=0) - 0.5 * layer_load


def window(source, first, cell_count, axis_id):
    return lax.slice_in_dim(source, first, first + cell_count, axis=axis_id)


def flux_div(gridded_quantity, velocity, ocean_indicator, axis_id, cell_count):
    face_count = cell_count + 1
    face_vel = 0.5 * (window(velocity, 1, face_count, axis_id) + window(velocity, 2, face_count, axis_id))
    face_vel = face_vel * window(ocean_indicator, 1, face_count, axis_id) * window(ocean_indicator, 2, face_count, axis_id)
    cell_before = window(gridded_quantity, 0, face_count, axis_id)
    cell_here = window(gridded_quantity, 1, face_count, axis_id)
    cell_after = window(gridded_quantity, 2, face_count, axis_id)
    cell_beyond = window(gridded_quantity, 3, face_count, axis_id)
    face_flux = face_vel * 0.5 * (cell_here + cell_after) - (
        jnp.maximum(face_vel, 0.0) * (cell_after - 2.0 * cell_here + cell_before)
        + jnp.minimum(face_vel, 0.0) * (cell_beyond - 2.0 * cell_after + cell_here)) / 6.0
    return window(face_flux, 1, cell_count, axis_id) - window(face_flux, 0, cell_count, axis_id)


def centred(pressure_field, axis_id, cell_count):
    return 0.5 * (window(pressure_field, 3, cell_count, axis_id) - window(pressure_field, 1, cell_count, axis_id))


def wet_from(depth_plane, layered_profile):
    level_ids = jnp.arange(layered_profile, dtype=jnp.float32)[:, None, None]
    return (level_ids < depth_plane[None]).astype(jnp.float32)


def explicit_part(lon_padded, lat_padded, centre, turning_rate):
    layered_profile = centre.shape[0] - 1
    eastwest_sum = centre.shape[2]
    vertical_sum = centre.shape[3]
    thickness, depth_mid = layer_thick(layered_profile)
    depth_column = depth_mid[:, None, None]
    gridded_quantity = centre[:layered_profile]
    ocean_indicator = wet_from(centre[layered_profile, 0], layered_profile)
    lon_values = lon_padded[:layered_profile]
    lon_wet = wet_from(lon_padded[layered_profile, 0], layered_profile)
    lat_values = lat_padded[:layered_profile]
    lat_wet = wet_from(lat_padded[layered_profile, 0], layered_profile)
    div_x = flux_div(lon_values, lon_values[:, 2:3], lon_wet[:, None], 3, vertical_sum)
    div_y = flux_div(lat_values, lat_values[:, 3:4], lat_wet[:, None], 2, eastwest_sum)
    grad_x = centred(pressure(density(lon_values[:, 0], lon_values[:, 1], depth_column) * lon_wet, thickness), 2, vertical_sum)
    grad_y = centred(pressure(density(lat_values[:, 0], lat_values[:, 1], depth_column) * lat_wet, thickness), 1, eastwest_sum)
    advected = gridded_quantity - courant * (div_x + div_y)
    turning = turning_rate[None, :, None]
    zonal_new = advected[:, 2] + time_step * (turning * gridded_quantity[:, 3] - gravity * grad_x)
    merid_new = advected[:, 3] + time_step * (-turning * gridded_quantity[:, 2] - gravity * grad_y)
    stepped = jnp.stack([advected[:, 0], advected[:, 1], zonal_new, merid_new], axis=1) * ocean_indicator[:, None]
    return stepped, ocean_indicator, thickness, depth_column


def build_bands(stepped, ocean_indicator, depth_plane, forcing, thickness, depth_column):
    layered_profile = stepped.shape[0]
    rho_star = density(stepped[:, 0], stepped[:, 1], depth_column)
    spacing = (0.5 * (thickness[1:] + thickness[:-1]))[:, None, None]
    stratified = (rho_star[1:] - rho_star[:-1]) / spacing
    mixing = (mix_back + mix_conv * jax.nn.sigmoid(-stratified / strat_scale)) * ocean_indicator[1:]
    zero_plane = jnp.zeros_like(mixing[:1])
    upper_mix = jnp.concatenate([mixing, zero_plane], axis=0)
    lower_mix = jnp.concatenate([zero_plane, mixing], axis=0)
    channel_mix = jnp.array([1.0, 1.0, momentum_mix, momentum_mix], dtype=jnp.float32)[None, :, None, None]
    channel_drag = jnp.array([0.0, 0.0, 1.0, 1.0], dtype=jnp.float32)[None, :, None, None]
    inverse = (1.0 / thickness)[:, None, None, None]
    lower_band = -lower_mix[:, None] * channel_mix * inverse
    upper_band = -upper_mix[:, None] * channel_mix * inverse
    level_ids = jnp.arange(layered_profile, dtype=jnp.float32)[:, None, None]
    floor_cells = (level_ids == depth_plane[None] - 1.0).astype(jnp.float32)
    centre_band = 1.0 - lower_band - upper_band + bottom_drag * floor_cells[:, None] * channel_drag * inverse
    surface = forcing * ocean_indicator[0][None] * (surface_gain / thickness[0])
    right_side = jnp.concatenate([stepped[:1] + surface[None], stepped[1:]], axis=0)
    return lower_band, centre_band, upper_band, right_side


def thomas(lower_band, centre_band, upper_band, right_side):
    zero_plane = jnp.zeros_like(right_side[0])

    def forward(state_tuple, row_data):
        ratio_prev, scaled_prev = state_tuple
        lower_now, centre_now, upper_now, side_now = row_data
        pivot_now = centre_now - lower_now * ratio_prev
        ratio_now = upper_now / pivot_now
        scaled_now = (side_now - lower_now * scaled_prev) / pivot_now
        return (ratio_now, scaled_now), (ratio_now, scaled_now)

    _, (ratios, scaled) = lax.scan(forward, (zero_plane, zero_plane), (lower_band, centre_band, upper_band, right_side))

    def backward(next_value, row_data):
        ratio_now, scaled_now = row_data
        current = scaled_now - ratio_now * next_value
        return current, current

    _, solved = lax.scan(backward, zero_plane, (ratios, scaled), reverse=True)
    return solved


def reference(heat_anomaly, brine_anomaly, eastward_current, northward_current, shoreline_indicator, bottom_layer_index, boundary_fluxes):
    depth_plane = (shoreline_indicator * bottom_layer_index).astype(jnp.float32)
    ocean_indicator = wet_from(depth_plane, DEPTH_LAYERS)
    gridded_quantity = jnp.stack([heat_anomaly, brine_anomaly, eastward_current, northward_current], axis=1) * ocean_indicator[:, None]
    centre = jnp.concatenate([gridded_quantity, jnp.broadcast_to(depth_plane[None, None], (1, 4, NORTHSOUTH_SIZE, EASTWEST_SIZE))], axis=0)
    lon_padded = jnp.concatenate([centre[..., -2:], centre, centre[..., :2]], axis=3)
    fold_sign = jnp.array([1.0, 1.0, -1.0, -1.0], dtype=jnp.float32)[None, :, None, None]
    ghost = centre[:, :, ::-1][:, :, :2, ::-1] * fold_sign
    lat_padded = jnp.concatenate([jnp.zeros((DEPTH_LAYERS + 1, 4, 2, EASTWEST_SIZE), jnp.float32), centre, ghost], axis=2)
    row_ids = jnp.arange(NORTHSOUTH_SIZE, dtype=jnp.float32)
    turning_rate = coriolis * (2.0 * (row_ids + 0.5) / NORTHSOUTH_SIZE - 1.0)

    def one_block(block_id):
        first = block_id * CX
        lon_block = lax.dynamic_slice_in_dim(lon_padded, first, CX + 4, 3)
        lat_block = lax.dynamic_slice_in_dim(lat_padded, first, CX, 3)
        centre_block = lax.dynamic_slice_in_dim(centre, first, CX, 3)
        forcing_block = lax.dynamic_slice_in_dim(boundary_fluxes, first, CX, 2)
        stepped, wet_block, thickness, depth_column = explicit_part(lon_block, lat_block, centre_block, turning_rate)
        bands = build_bands(stepped, wet_block, centre_block[DEPTH_LAYERS, 0], forcing_block, thickness, depth_column)
        return thomas(*bands)

    blocks = lax.map(one_block, jnp.arange(N_LON, dtype=jnp.int32))
    assembled = jnp.transpose(blocks, (1, 2, 3, 0, 4)).reshape(DEPTH_LAYERS, 4, NORTHSOUTH_SIZE, EASTWEST_SIZE)
    return assembled[:, 0], assembled[:, 1], assembled[:, 2], assembled[:, 3]
```

```python
import jax
import jax.numpy as jnp
from jax import lax
from jax.experimental import pallas as pl
from jax.experimental.pallas import tpu as pltpu
from jax.sharding import PartitionSpec as P

courant = 0.25
time_step = 0.2
gravity = 0.2
coriolis = 0.5
thermal = 0.6
thermal_sq = 0.1
haline = 0.8
mix_back = 5.0
mix_conv = 60.0
strat_scale = 2.0
momentum_mix = 2.0
bottom_drag = 1.0
surface_gain = 0.5


def density(warmth, saltiness, depth_column):
    return -thermal * warmth * (1.0 + thermal_sq * warmth + depth_column) + haline * saltiness


def face_flux(face_vel, before, here, after, beyond):
    return face_vel * 0.5 * (here + after) - (
        jnp.maximum(face_vel, 0.0) * (after - 2.0 * here + before)
        + jnp.minimum(face_vel, 0.0) * (beyond - 2.0 * after + here)
    ) * (1.0 / 6.0)


def step_kernel(
    h_ref, inv_h_ref, zmid_ref, inv_sp_ref,
    f_ref, dep_ref, flux_ref, t_ref, s_ref, u_ref, v_ref, elat_ref, elon_ref,
    o0_ref, o1_ref, o2_ref, o3_ref,
    star_scr, r_scr, rs_scr,
):
    layers = t_ref.shape[0]
    rows, cols = t_ref.shape[1], t_ref.shape[2]
    depth_plane = 4 * layers
    lane = lax.broadcasted_iota(jnp.int32, (rows, cols), 1)
    row = lax.broadcasted_iota(jnp.int32, (rows, cols), 0)

    def xs(v, e, s):
        if s == 1:
            return pltpu.roll(jnp.where(lane == 0, e, v), cols - 1, 1)
        if s == 2:
            return pltpu.roll(jnp.where(lane < 2, e, v), cols - 2, 1)
        if s == -1:
            return pltpu.roll(jnp.where(lane == cols - 1, e, v), 1, 1)
        return pltpu.roll(jnp.where(lane >= cols - 2, e, v), 2, 1)

    def ys(v, e, s):
        if s == 1:
            return pltpu.roll(jnp.where(row == 0, e, v), rows - 1, 0)
        if s == 2:
            return pltpu.roll(jnp.where(row < 2, e, v), rows - 2, 0)
        if s == -1:
            return pltpu.roll(jnp.where(row == rows - 1, e, v), 1, 0)
        return pltpu.roll(jnp.where(row >= rows - 2, e, v), 2, 0)

    dep = dep_ref[...]
    dep_xm = xs(dep, elon_ref[depth_plane], -1)
    dep_xp = xs(dep, elon_ref[depth_plane], 1)
    dep_ym = ys(dep, elat_ref[depth_plane], -1)
    dep_yp = ys(dep, elat_ref[depth_plane], 1)
    turning = f_ref[...]
    zero = jnp.zeros((rows, cols), jnp.float32)

    def explicit(k, carry):
        cum_xm, cum_xp, cum_ym, cum_yp = carry
        kf = k.astype(jnp.float32)
        h = h_ref[k]
        zmid = zmid_ref[k]
        w0 = (kf < dep).astype(jnp.float32)
        wxm = (kf < dep_xm).astype(jnp.float32)
        wxp = (kf < dep_xp).astype(jnp.float32)
        wym = (kf < dep_ym).astype(jnp.float32)
        wyp = (kf < dep_yp).astype(jnp.float32)
        q = [r[k] * w0 for r in (t_ref, s_ref, u_ref, v_ref)]
        ex = [elon_ref[c * layers + k] for c in range(4)]
        ey = [elat_ref[c * layers + k] for c in range(4)]
        xsh = {s: [xs(q[c], ex[c], s) for c in range(4)] for s in (-2, -1, 1, 2)}
        ysh = {s: [ys(q[c], ey[c], s) for c in range(4)] for s in (-2, -1, 1, 2)}
        a_r = 0.5 * (q[2] + xsh[1][2]) * w0 * wxp
        a_l = 0.5 * (xsh[-1][2] + q[2]) * wxm * w0
        b_r = 0.5 * (q[3] + ysh[1][3]) * w0 * wyp
        b_l = 0.5 * (ysh[-1][3] + q[3]) * wym * w0
        adv = []
        for c in range(4):
            div_x = face_flux(a_r, xsh[-1][c], q[c], xsh[1][c], xsh[2][c]) - face_flux(
                a_l, xsh[-2][c], xsh[-1][c], q[c], xsh[1][c]
            )
            div_y = face_flux(b_r, ysh[-1][c], q[c], ysh[1][c], ysh[2][c]) - face_flux(
                b_l, ysh[-2][c], ysh[-1][c], q[c], ysh[1][c]
            )
            adv.append(q[c] - courant * (div_x + div_y))
        load_xm = density(xsh[-1][0], xsh[-1][1], zmid) * wxm * h
        load_xp = density(xsh[1][0], xsh[1][1], zmid) * wxp * h
        load_ym = density(ysh[-1][0], ysh[-1][1], zmid) * wym * h
        load_yp = density(ysh[1][0], ysh[1][1], zmid) * wyp * h
        cum_xm = cum_xm + load_xm
        cum_xp = cum_xp + load_xp
        cum_ym = cum_ym + load_ym
        cum_yp = cum_yp + load_yp
        grad_x = 0.5 * ((cum_xp - 0.5 * load_xp) - (cum_xm - 0.5 * load_xm))
        grad_y = 0.5 * ((cum_yp - 0.5 * load_yp) - (cum_ym - 0.5 * load_ym))
        star0 = adv[0] * w0
        star1 = adv[1] * w0
        star2 = (adv[2] + time_step * (turning * q[3] - gravity * grad_x)) * w0
        star3 = (adv[3] + time_step * (-turning * q[2] - gravity * grad_y)) * w0
        for c, val in enumerate((star0, star1, star2, star3)):
            star_scr[c * layers + k] = val
        rs_scr[k] = density(star0, star1, zmid)
        return (cum_xm, cum_xp, cum_ym, cum_yp)

    lax.fori_loop(0, layers, explicit, (zero, zero, zero, zero), unroll=3)

    surface_scale = surface_gain * inv_h_ref[0]
    w_top = (0.0 < dep).astype(jnp.float32)
    for c in range(4):
        star_scr[c * layers] = star_scr[c * layers] + flux_ref[c] * w_top * surface_scale

    def forward(k, carry):
        mix_prev, r_a, r_b, s0, s1, s2, s3 = carry
        kf = k.astype(jnp.float32)
        inv_h = inv_h_ref[k]
        nxt = jnp.minimum(k + 1, layers - 1)
        stratified = (rs_scr[nxt] - rs_scr[k]) * inv_sp_ref[k]
        sig = 1.0 / (1.0 + jnp.exp(stratified * (1.0 / strat_scale)))
        w_next = (kf + 1.0 < dep).astype(jnp.float32)
        mix = (mix_back + mix_conv * sig) * w_next
        mix = jnp.where(k < layers - 1, mix, 0.0)
        low_a = -mix_prev * inv_h
        up_a = -mix * inv_h
        cen_a = 1.0 - low_a - up_a
        low_b = -mix_prev * momentum_mix * inv_h
        up_b = -mix * momentum_mix * inv_h
        floor = (kf == dep - 1.0).astype(jnp.float32)
        cen_b = 1.0 - low_b - up_b + bottom_drag * floor * inv_h
        inv_a = 1.0 / (cen_a - low_a * r_a)
        inv_b = 1.0 / (cen_b - low_b * r_b)
        r_a = up_a * inv_a
        r_b = up_b * inv_b
        r_scr[k] = r_a
        r_scr[layers + k] = r_b
        s0 = (star_scr[k] - low_a * s0) * inv_a
        s1 = (star_scr[layers + k] - low_a * s1) * inv_a
        s2 = (star_scr[2 * layers + k] - low_b * s2) * inv_b
        s3 = (star_scr[3 * layers + k] - low_b * s3) * inv_b
        star_scr[k] = s0
        star_scr[layers + k] = s1
        star_scr[2 * layers + k] = s2
        star_scr[3 * layers + k] = s3
        return (mix, r_a, r_b, s0, s1, s2, s3)

    lax.fori_loop(0, layers, forward, (zero,) * 7, unroll=3)

    def backward(i, carry):
        x0, x1, x2, x3 = carry
        k = layers - 1 - i
        r_a = r_scr[k]
        r_b = r_scr[layers + k]
        x0 = star_scr[k] - r_a * x0
        x1 = star_scr[layers + k] - r_a * x1
        x2 = star_scr[2 * layers + k] - r_b * x2
        x3 = star_scr[3 * layers + k] - r_b * x3
        o0_ref[k] = x0
        o1_ref[k] = x1
        o2_ref[k] = x2
        o3_ref[k] = x3
        return (x0, x1, x2, x3)

    lax.fori_loop(0, layers, backward, (zero,) * 4, unroll=3)


def on_device(
    heat_anomaly,
    brine_anomaly,
    eastward_current,
    northward_current,
    shoreline_indicator,
    bottom_layer_index,
    boundary_fluxes,
):
    layers, rows, cols = heat_anomaly.shape
    fields = (heat_anomaly, brine_anomaly, eastward_current, northward_current)
    depth_plane = (shoreline_indicator * bottom_layer_index).astype(jnp.float32)
    level_ids = jnp.arange(layers, dtype=jnp.float32)[:, None, None]

    def edge(row_slice, col_slice):
        d = depth_plane[row_slice, col_slice]
        wet = (level_ids < d[None]).astype(jnp.float32)
        parts = [x[:, row_slice, col_slice] * wet for x in fields]
        return jnp.concatenate(parts + [d[None]], axis=0)

    n_lat = lax.axis_size("lat")
    n_lon = lax.axis_size("lon")
    top = edge(slice(rows - 2, rows), slice(None))
    bottom = edge(slice(0, 2), slice(None))
    right = edge(slice(None), slice(cols - 2, cols))
    left = edge(slice(None), slice(0, 2))
    from_south = lax.ppermute(top, "lat", [(i, i + 1) for i in range(n_lat - 1)])
    from_north = lax.ppermute(bottom, "lat", [(i + 1, i) for i in range(n_lat - 1)])
    from_west = lax.ppermute(right, "lon", [(i, (i + 1) % n_lon) for i in range(n_lon)])
    from_east = lax.ppermute(left, "lon", [((i + 1) % n_lon, i) for i in range(n_lon)])
    last = (n_lat - 1) * n_lon
    from_fold = lax.ppermute(
        top, ("lat", "lon"), [(last + x, last + n_lon - 1 - x) for x in range(n_lon)]
    )
    planes = 4 * layers + 1
    fold_sign = jnp.concatenate(
        [jnp.ones((2 * layers,), jnp.float32), -jnp.ones((2 * layers,), jnp.float32),
         jnp.ones((1,), jnp.float32)]
    )[:, None, None]
    ghost = from_fold[:, ::-1, ::-1] * fold_sign
    is_north = lax.axis_index("lat") == n_lat - 1
    north_rows = jnp.where(is_north, ghost, from_north)
    edge_lat = jnp.concatenate(
        [north_rows, jnp.zeros((planes, rows - 4, cols), jnp.float32), from_south], axis=1
    )
    edge_lon = jnp.concatenate(
        [from_east, jnp.zeros((planes, rows, cols - 4), jnp.float32), from_west], axis=2
    )

    row_ids = lax.axis_index("lat") * rows + jnp.arange(rows, dtype=jnp.int32)
    total_rows = rows * n_lat
    turning_rate = coriolis * (2.0 * (row_ids.astype(jnp.float32) + 0.5) / total_rows - 1.0)
    turning_plane = jnp.broadcast_to(turning_rate[:, None], (rows, cols))

    offsets = jnp.arange(layers, dtype=jnp.float32) + 0.5
    thickness = 0.5 + offsets / layers
    zmid = offsets / layers
    inverse = 1.0 / thickness
    spacing = 0.5 * (thickness[1:] + thickness[:-1])
    inv_spacing = jnp.concatenate([1.0 / spacing, jnp.ones((1,), jnp.float32)])

    smem = pl.BlockSpec(memory_space=pltpu.SMEM)
    vmem = pl.BlockSpec(memory_space=pltpu.VMEM)
    plane = jax.ShapeDtypeStruct((layers, rows, cols), jnp.float32)
    outs = pl.pallas_call(
        step_kernel,
        out_shape=(plane,) * 4,
        in_specs=[smem] * 4 + [vmem] * 9,
        out_specs=(vmem,) * 4,
        scratch_shapes=[
            pltpu.VMEM((4 * layers, rows, cols), jnp.float32),
            pltpu.VMEM((2 * layers, rows, cols), jnp.float32),
            pltpu.VMEM((layers, rows, cols), jnp.float32),
        ],
    )(
        thickness, inverse, zmid, inv_spacing,
        turning_plane, depth_plane, boundary_fluxes,
        heat_anomaly, brine_anomaly, eastward_current, northward_current,
        edge_lat, edge_lon,
    )
    return tuple(outs)


def solution(mesh):
    in_specs = (
        P(None, "lat", "lon"),
        P(None, "lat", "lon"),
        P(None, "lat", "lon"),
        P(None, "lat", "lon"),
        P("lat", "lon"),
        P("lat", "lon"),
        P(None, "lat", "lon"),
    )
    out_specs = (
        P(None, "lat", "lon"),
        P(None, "lat", "lon"),
        P(None, "lat", "lon"),
        P(None, "lat", "lon"),
    )
    return jax.shard_map(
        on_device, mesh=mesh, in_specs=in_specs, out_specs=out_specs, check_vma=False
    )
```

```python
import numpy as np
import jax
import jax.numpy as jnp
from jax import lax
from jax.experimental import pallas as pl
from jax.experimental.pallas import tpu as pltpu
from jax.sharding import PartitionSpec as P

courant = 0.25
time_step = 0.2
gravity = 0.2
coriolis = 0.5
thermal = 0.6
thermal_sq = 0.1
haline = 0.8
mix_back = 5.0
mix_conv = 60.0
strat_scale = 2.0
momentum_mix = 2.0
bottom_drag = 1.0
surface_gain = 0.5

GROUP = 15


def density(warmth, saltiness, depth_column):
    return -thermal * warmth * (1.0 + thermal_sq * warmth + depth_column) + haline * saltiness


def face_flux(face_vel, before, here, after, beyond):
    return face_vel * 0.5 * (here + after) - (
        jnp.maximum(face_vel, 0.0) * (after - 2.0 * here + before)
        + jnp.minimum(face_vel, 0.0) * (beyond - 2.0 * after + here)
    ) * (1.0 / 6.0)


def rolled(x, shift, axis):
    shift %= x.shape[axis]
    return x if shift == 0 else pltpu.roll(x, shift, axis)


def pack_kernel(
    last_ref, shore_ref, bottom_ref, t_ref, s_ref, u_ref, v_ref,
    top_ref, bot_ref, fold_ref, right_ref, left_ref,
):
    layers, rows, cols = t_ref.shape
    groups = layers // GROUP
    lane = lax.broadcasted_iota(jnp.int32, (rows, cols), 1)
    row = lax.broadcasted_iota(jnp.int32, (rows, cols), 0)
    dep = (shore_ref[...] * bottom_ref[...]).astype(jnp.float32)
    zero = jnp.zeros((rows, cols), jnp.float32)

    def pack_rows(vals, first):
        out = zero
        for c, val in enumerate(vals):
            out = jnp.where((row >> 1) == c, rolled(val, 2 * c - first, 0), out)
        return out

    def group_body(g, carry):
        right = zero
        left = zero
        for j in range(GROUP):
            k = g * GROUP + j
            w = (k.astype(jnp.float32) < dep).astype(jnp.float32)
            q = [r[k] * w for r in (t_ref, s_ref, u_ref, v_ref)]
            top_ref[k] = pack_rows(q, rows - 2)
            bot_ref[k] = pack_rows(q, 0)
            for c in range(4):
                m = j * 4 + c
                slot = (lane >> 1) == m
                right = jnp.where(slot, rolled(q[c], 2 * m - (cols - 2), 1), right)
                left = jnp.where(slot, rolled(q[c], 2 * m, 1), left)
        right_ref[g] = right
        left_ref[g] = left
        return carry

    lax.fori_loop(0, groups, group_body, 0)
    top_ref[layers] = pack_rows([dep], rows - 2)
    bot_ref[layers] = pack_rows([dep], 0)
    right_ref[groups] = jnp.where(lane < 2, rolled(dep, 2, 1), zero)
    left_ref[groups] = jnp.where(lane < 2, dep, zero)

    @pl.when(last_ref[0] == 1)
    def _():
        sign = jnp.where(row < 4, 1.0, -1.0)
        masks = [(lane & (1 << b)) != 0 for b in range(7)]

        def fold_body(k, carry):
            tile = top_ref[k]
            swapped = jnp.where((row & 1) == 0, rolled(tile, -1, 0), rolled(tile, 1, 0)) * sign
            for b in range(7):
                swapped = jnp.where(
                    masks[b], rolled(swapped, 1 << b, 1), rolled(swapped, -(1 << b), 1)
                )
            fold_ref[k] = swapped
            return carry

        lax.fori_loop(0, layers + 1, fold_body, 0)


def step_kernel(
    lat_ref, h_ref, inv_h_ref, zmid_ref, inv_sp_ref,
    shore_ref, bottom_ref, flux_ref, t_ref, s_ref, u_ref, v_ref,
    south_ref, north_ref, fold_ref, west_ref, east_ref,
    o0_ref, o1_ref, o2_ref, o3_ref,
    star_scr, r_scr, rs_scr,
):
    layers = t_ref.shape[0]
    rows, cols = t_ref.shape[1], t_ref.shape[2]
    groups = layers // GROUP
    lane = lax.broadcasted_iota(jnp.int32, (rows, cols), 1)
    row = lax.broadcasted_iota(jnp.int32, (rows, cols), 0)

    def xs(v, e, s):
        if s == 1:
            return pltpu.roll(jnp.where(lane == 0, e, v), cols - 1, 1)
        if s == 2:
            return pltpu.roll(jnp.where(lane < 2, e, v), cols - 2, 1)
        if s == -1:
            return pltpu.roll(jnp.where(lane == cols - 1, e, v), 1, 1)
        return pltpu.roll(jnp.where(lane >= cols - 2, e, v), 2, 1)

    def ys(v, e, s):
        if s == 1:
            return pltpu.roll(jnp.where(row == 0, e, v), rows - 1, 0)
        if s == 2:
            return pltpu.roll(jnp.where(row < 2, e, v), rows - 2, 0)
        if s == -1:
            return pltpu.roll(jnp.where(row == rows - 1, e, v), 1, 0)
        return pltpu.roll(jnp.where(row >= rows - 2, e, v), 2, 0)

    def lat_edge(tile_n, tile_s, c):
        return jnp.where(row < 4, rolled(tile_n, -2 * c, 0), rolled(tile_s, rows - 2 - 2 * c, 0))

    def lon_edge(tile_e, tile_w, m):
        return jnp.where(lane < 64, rolled(tile_e, -2 * m, 1), rolled(tile_w, cols - 2 - 2 * m, 1))

    dep = (shore_ref[...] * bottom_ref[...]).astype(jnp.float32)
    dep_lat = lat_edge(north_ref[layers] + fold_ref[layers], south_ref[layers], 0)
    dep_lon = lon_edge(east_ref[groups], west_ref[groups], 0)
    dep_xm = xs(dep, dep_lon, -1)
    dep_xp = xs(dep, dep_lon, 1)
    dep_ym = ys(dep, dep_lat, -1)
    dep_yp = ys(dep, dep_lat, 1)
    total_rows = rows * lat_ref[1]
    row_ids = (lat_ref[0] * rows + row).astype(jnp.float32)
    turning = coriolis * (2.0 * (row_ids + 0.5) / total_rows.astype(jnp.float32) - 1.0)
    zero = jnp.zeros((rows, cols), jnp.float32)

    def explicit_group(g, carry):
        tile_e = east_ref[g]
        tile_w = west_ref[g]
        for j in range(GROUP):
            k = g * GROUP + j
            carry = explicit(k, j, tile_e, tile_w, carry)
        return carry

    def explicit(k, j, tile_e, tile_w, carry):
        cum_xm, cum_xp, cum_ym, cum_yp = carry
        kf = k.astype(jnp.float32)
        h = h_ref[k]
        zmid = zmid_ref[k]
        w0 = (kf < dep).astype(jnp.float32)
        wxm = (kf < dep_xm).astype(jnp.float32)
        wxp = (kf < dep_xp).astype(jnp.float32)
        wym = (kf < dep_ym).astype(jnp.float32)
        wyp = (kf < dep_yp).astype(jnp.float32)
        q = [r[k] * w0 for r in (t_ref, s_ref, u_ref, v_ref)]
        tile_n = north_ref[k] + fold_ref[k]
        tile_s = south_ref[k]
        ey = [lat_edge(tile_n, tile_s, c) for c in range(4)]
        ex = [lon_edge(tile_e, tile_w, j * 4 + c) for c in range(4)]
        xsh = {s: [xs(q[c], ex[c], s) for c in range(4)] for s in (-2, -1, 1, 2)}
        ysh = {s: [ys(q[c], ey[c], s) for c in range(4)] for s in (-2, -1, 1, 2)}
        a_r = 0.5 * (q[2] + xsh[1][2]) * w0 * wxp
        a_l = 0.5 * (xsh[-1][2] + q[2]) * wxm * w0
        b_r = 0.5 * (q[3] + ysh[1][3]) * w0 * wyp
        b_l = 0.5 * (ysh[-1][3] + q[3]) * wym * w0
        adv = []
        for c in range(4):
            div_x = face_flux(a_r, xsh[-1][c], q[c], xsh[1][c], xsh[2][c]) - face_flux(
                a_l, xsh[-2][c], xsh[-1][c], q[c], xsh[1][c]
            )
            div_y = face_flux(b_r, ysh[-1][c], q[c], ysh[1][c], ysh[2][c]) - face_flux(
                b_l, ysh[-2][c], ysh[-1][c], q[c], ysh[1][c]
            )
            adv.append(q[c] - courant * (div_x + div_y))
        load_xm = density(xsh[-1][0], xsh[-1][1], zmid) * wxm * h
        load_xp = density(xsh[1][0], xsh[1][1], zmid) * wxp * h
        load_ym = density(ysh[-1][0], ysh[-1][1], zmid) * wym * h
        load_yp = density(ysh[1][0], ysh[1][1], zmid) * wyp * h
        cum_xm = cum_xm + load_xm
        cum_xp = cum_xp + load_xp
        cum_ym = cum_ym + load_ym
        cum_yp = cum_yp + load_yp
        grad_x = 0.5 * ((cum_xp - 0.5 * load_xp) - (cum_xm - 0.5 * load_xm))
        grad_y = 0.5 * ((cum_yp - 0.5 * load_yp) - (cum_ym - 0.5 * load_ym))
        star0 = adv[0] * w0
        star1 = adv[1] * w0
        star2 = (adv[2] + time_step * (turning * q[3] - gravity * grad_x)) * w0
        star3 = (adv[3] + time_step * (-turning * q[2] - gravity * grad_y)) * w0
        for c, val in enumerate((star0, star1, star2, star3)):
            star_scr[c * layers + k] = val
        rs_scr[k] = density(star0, star1, zmid)
        return (cum_xm, cum_xp, cum_ym, cum_yp)

    lax.fori_loop(0, groups, explicit_group, (zero, zero, zero, zero))

    surface_scale = surface_gain * inv_h_ref[0]
    w_top = (0.0 < dep).astype(jnp.float32)
    for c in range(4):
        star_scr[c * layers] = star_scr[c * layers] + flux_ref[c] * w_top * surface_scale

    def forward(k, carry):
        mix_prev, r_a, r_b, s0, s1, s2, s3 = carry
        kf = k.astype(jnp.float32)
        inv_h = inv_h_ref[k]
        nxt = jnp.minimum(k + 1, layers - 1)
        stratified = (rs_scr[nxt] - rs_scr[k]) * inv_sp_ref[k]
        sig = 1.0 / (1.0 + jnp.exp(stratified * (1.0 / strat_scale)))
        w_next = (kf + 1.0 < dep).astype(jnp.float32)
        mix = (mix_back + mix_conv * sig) * w_next
        mix = jnp.where(k < layers - 1, mix, 0.0)
        low_a = -mix_prev * inv_h
        up_a = -mix * inv_h
        cen_a = 1.0 - low_a - up_a
        low_b = -mix_prev * momentum_mix * inv_h
        up_b = -mix * momentum_mix * inv_h
        floor = (kf == dep - 1.0).astype(jnp.float32)
        cen_b = 1.0 - low_b - up_b + bottom_drag * floor * inv_h
        inv_a = 1.0 / (cen_a - low_a * r_a)
        inv_b = 1.0 / (cen_b - low_b * r_b)
        r_a = up_a * inv_a
        r_b = up_b * inv_b
        r_scr[k] = r_a
        r_scr[layers + k] = r_b
        s0 = (star_scr[k] - low_a * s0) * inv_a
        s1 = (star_scr[layers + k] - low_a * s1) * inv_a
        s2 = (star_scr[2 * layers + k] - low_b * s2) * inv_b
        s3 = (star_scr[3 * layers + k] - low_b * s3) * inv_b
        star_scr[k] = s0
        star_scr[layers + k] = s1
        star_scr[2 * layers + k] = s2
        star_scr[3 * layers + k] = s3
        return (mix, r_a, r_b, s0, s1, s2, s3)

    lax.fori_loop(0, layers, forward, (zero,) * 7, unroll=3)

    def backward(i, carry):
        x0, x1, x2, x3 = carry
        k = layers - 1 - i
        r_a = r_scr[k]
        r_b = r_scr[layers + k]
        x0 = star_scr[k] - r_a * x0
        x1 = star_scr[layers + k] - r_a * x1
        x2 = star_scr[2 * layers + k] - r_b * x2
        x3 = star_scr[3 * layers + k] - r_b * x3
        o0_ref[k] = x0
        o1_ref[k] = x1
        o2_ref[k] = x2
        o3_ref[k] = x3
        return (x0, x1, x2, x3)

    lax.fori_loop(0, layers, backward, (zero,) * 4, unroll=3)


def level_tables(layers):
    offsets = np.arange(layers, dtype=np.float32) + np.float32(0.5)
    zmid = offsets / np.float32(layers)
    thickness = np.float32(0.5) + zmid
    inverse = np.float32(1.0) / thickness
    spacing = np.float32(0.5) * (thickness[1:] + thickness[:-1])
    inv_spacing = np.concatenate([np.float32(1.0) / spacing, np.ones((1,), np.float32)])
    return [jnp.asarray(t.astype(np.float32)) for t in (thickness, inverse, zmid, inv_spacing)]


def on_device(
    heat_anomaly,
    brine_anomaly,
    eastward_current,
    northward_current,
    shoreline_indicator,
    bottom_layer_index,
    boundary_fluxes,
):
    layers, rows, cols = heat_anomaly.shape
    fields = (heat_anomaly, brine_anomaly, eastward_current, northward_current)
    groups = layers // GROUP
    n_lat = lax.axis_size("lat")
    n_lon = lax.axis_size("lon")
    lat_idx = lax.axis_index("lat").astype(jnp.int32)
    is_last = (lat_idx == n_lat - 1).astype(jnp.int32).reshape(1)
    lat_info = jnp.stack([lat_idx, jnp.int32(n_lat)])

    smem = pl.BlockSpec(memory_space=pltpu.SMEM)
    vmem = pl.BlockSpec(memory_space=pltpu.VMEM)
    row_tiles = jax.ShapeDtypeStruct((layers + 1, rows, cols), jnp.float32)
    col_tiles = jax.ShapeDtypeStruct((groups + 1, rows, cols), jnp.float32)
    top, bot, fold, right, left = pl.pallas_call(
        pack_kernel,
        out_shape=(row_tiles, row_tiles, row_tiles, col_tiles, col_tiles),
        in_specs=[smem] + [vmem] * 6,
        out_specs=(vmem,) * 5,
    )(is_last, shoreline_indicator, bottom_layer_index, *fields)

    from_south = lax.ppermute(top, "lat", [(i, i + 1) for i in range(n_lat - 1)])
    from_north = lax.ppermute(bot, "lat", [(i + 1, i) for i in range(n_lat - 1)])
    from_west = lax.ppermute(right, "lon", [(i, (i + 1) % n_lon) for i in range(n_lon)])
    from_east = lax.ppermute(left, "lon", [((i + 1) % n_lon, i) for i in range(n_lon)])
    last = (n_lat - 1) * n_lon
    from_fold = lax.ppermute(
        fold, ("lat", "lon"), [(last + x, last + n_lon - 1 - x) for x in range(n_lon)]
    )

    plane = jax.ShapeDtypeStruct((layers, rows, cols), jnp.float32)
    outs = pl.pallas_call(
        step_kernel,
        out_shape=(plane,) * 4,
        in_specs=[smem] * 5 + [vmem] * 12,
        out_specs=(vmem,) * 4,
        scratch_shapes=[
            pltpu.VMEM((4 * layers, rows, cols), jnp.float32),
            pltpu.VMEM((2 * layers, rows, cols), jnp.float32),
            pltpu.VMEM((layers, rows, cols), jnp.float32),
        ],
    )(
        lat_info, *level_tables(layers),
        shoreline_indicator, bottom_layer_index, boundary_fluxes, *fields,
        from_south, from_north, from_fold, from_west, from_east,
    )
    return tuple(outs)


def solution(mesh):
    in_specs = (
        P(None, "lat", "lon"),
        P(None, "lat", "lon"),
        P(None, "lat", "lon"),
        P(None, "lat", "lon"),
        P("lat", "lon"),
        P("lat", "lon"),
        P(None, "lat", "lon"),
    )
    out_specs = (
        P(None, "lat", "lon"),
        P(None, "lat", "lon"),
        P(None, "lat", "lon"),
        P(None, "lat", "lon"),
    )
    return jax.shard_map(
        on_device, mesh=mesh, in_specs=in_specs, out_specs=out_specs, check_vma=False
    )
```

```python
import numpy as np
import jax
import jax.numpy as jnp
from jax import lax
from jax.experimental import pallas as pl
from jax.experimental.pallas import tpu as pltpu
from jax.sharding import PartitionSpec as P

courant = 0.25
time_step = 0.2
gravity = 0.2
coriolis = 0.5
thermal = 0.6
thermal_sq = 0.1
haline = 0.8
mix_back = 5.0
mix_conv = 60.0
strat_scale = 2.0
momentum_mix = 2.0
bottom_drag = 1.0
surface_gain = 0.5

GROUP = 15


def density(warmth, saltiness, depth_column):
    return -thermal * warmth * (1.0 + thermal_sq * warmth + depth_column) + haline * saltiness


def face_flux(face_vel, before, here, after, beyond):
    return face_vel * 0.5 * (here + after) - (
        jnp.maximum(face_vel, 0.0) * (after - 2.0 * here + before)
        + jnp.minimum(face_vel, 0.0) * (beyond - 2.0 * after + here)
    ) * (1.0 / 6.0)


def rolled(x, shift, axis):
    shift %= x.shape[axis]
    return x if shift == 0 else pltpu.roll(x, shift, axis)


def pack_kernel(
    last_ref, shore_ref, bottom_ref, t_ref, s_ref, u_ref, v_ref,
    top_ref, bot_ref, fold_ref, right_ref, left_ref,
):
    layers, rows, cols = t_ref.shape
    groups = layers // GROUP
    lane = lax.broadcasted_iota(jnp.int32, (rows, cols), 1)
    row = lax.broadcasted_iota(jnp.int32, (rows, cols), 0)
    dep = (shore_ref[...] * bottom_ref[...]).astype(jnp.float32)
    zero = jnp.zeros((rows, cols), jnp.float32)

    def pack_rows(vals, first):
        out = zero
        for c, val in enumerate(vals):
            out = jnp.where((row >> 1) == c, rolled(val, 2 * c - first, 0), out)
        return out

    def group_body(g, carry):
        right = zero
        left = zero
        for j in range(GROUP):
            k = g * GROUP + j
            w = (k.astype(jnp.float32) < dep).astype(jnp.float32)
            q = [r[k] * w for r in (t_ref, s_ref, u_ref, v_ref)]
            top_ref[k] = pack_rows(q, rows - 2)
            bot_ref[k] = pack_rows(q, 0)
            for c in range(4):
                m = j * 4 + c
                slot = (lane >> 1) == m
                right = jnp.where(slot, rolled(q[c], 2 * m - (cols - 2), 1), right)
                left = jnp.where(slot, rolled(q[c], 2 * m, 1), left)
        right_ref[g] = right
        left_ref[g] = left
        return carry

    lax.fori_loop(0, groups, group_body, 0)
    top_ref[layers] = pack_rows([dep], rows - 2)
    bot_ref[layers] = pack_rows([dep], 0)
    right_ref[groups] = jnp.where(lane < 2, rolled(dep, 2, 1), zero)
    left_ref[groups] = jnp.where(lane < 2, dep, zero)

    @pl.when(last_ref[0] == 1)
    def _():
        tiles = top_ref[...].reshape((layers + 1) * rows, cols)
        tile_row = lax.broadcasted_iota(jnp.int32, tiles.shape, 0) % rows
        sign = jnp.where(tile_row < 4, 1.0, -1.0)
        swapped = jnp.where(
            (tile_row & 1) == 0, rolled(tiles, -1, 0), rolled(tiles, 1, 0)
        ) * sign
        src_lane = lax.broadcasted_iota(jnp.int32, (cols, cols), 0)
        dst_lane = lax.broadcasted_iota(jnp.int32, (cols, cols), 1)
        reverse = (src_lane + dst_lane == cols - 1).astype(jnp.float32)
        flipped = jnp.dot(
            swapped, reverse, precision=lax.Precision.HIGHEST,
            preferred_element_type=jnp.float32,
        )
        fold_ref[...] = flipped.reshape(layers + 1, rows, cols)


def step_kernel(
    lat_ref, h_ref, inv_h_ref, zmid_ref, inv_sp_ref,
    shore_ref, bottom_ref, flux_ref, t_ref, s_ref, u_ref, v_ref,
    south_ref, north_ref, fold_ref, west_ref, east_ref,
    o0_ref, o1_ref, o2_ref, o3_ref,
    star_scr, r_scr, rs_scr,
):
    layers = t_ref.shape[0]
    rows, cols = t_ref.shape[1], t_ref.shape[2]
    groups = layers // GROUP
    lane = lax.broadcasted_iota(jnp.int32, (rows, cols), 1)
    row = lax.broadcasted_iota(jnp.int32, (rows, cols), 0)

    def xs(v, e, s):
        if s == 1:
            return pltpu.roll(jnp.where(lane == 0, e, v), cols - 1, 1)
        if s == 2:
            return pltpu.roll(jnp.where(lane < 2, e, v), cols - 2, 1)
        if s == -1:
            return pltpu.roll(jnp.where(lane == cols - 1, e, v), 1, 1)
        return pltpu.roll(jnp.where(lane >= cols - 2, e, v), 2, 1)

    def ys(v, e, s):
        if s == 1:
            return pltpu.roll(jnp.where(row == 0, e, v), rows - 1, 0)
        if s == 2:
            return pltpu.roll(jnp.where(row < 2, e, v), rows - 2, 0)
        if s == -1:
            return pltpu.roll(jnp.where(row == rows - 1, e, v), 1, 0)
        return pltpu.roll(jnp.where(row >= rows - 2, e, v), 2, 0)

    def lat_edge(tile_n, tile_s, c):
        return jnp.where(row < 4, rolled(tile_n, -2 * c, 0), rolled(tile_s, rows - 2 - 2 * c, 0))

    def lon_edge(tile_e, tile_w, m):
        return jnp.where(lane < 64, rolled(tile_e, -2 * m, 1), rolled(tile_w, cols - 2 - 2 * m, 1))

    dep = (shore_ref[...] * bottom_ref[...]).astype(jnp.float32)
    dep_lat = lat_edge(north_ref[layers] + fold_ref[layers], south_ref[layers], 0)
    dep_lon = lon_edge(east_ref[groups], west_ref[groups], 0)
    dep_xm = xs(dep, dep_lon, -1)
    dep_xp = xs(dep, dep_lon, 1)
    dep_ym = ys(dep, dep_lat, -1)
    dep_yp = ys(dep, dep_lat, 1)
    total_rows = rows * lat_ref[1]
    row_ids = (lat_ref[0] * rows + row).astype(jnp.float32)
    turning = coriolis * (2.0 * (row_ids + 0.5) / total_rows.astype(jnp.float32) - 1.0)
    zero = jnp.zeros((rows, cols), jnp.float32)

    def explicit_group(g, carry):
        tile_e = east_ref[g]
        tile_w = west_ref[g]
        for j in range(GROUP):
            k = g * GROUP + j
            carry = explicit(k, j, tile_e, tile_w, carry)
        return carry

    def explicit(k, j, tile_e, tile_w, carry):
        cum_xm, cum_xp, cum_ym, cum_yp = carry
        kf = k.astype(jnp.float32)
        h = h_ref[k]
        zmid = zmid_ref[k]
        w0 = (kf < dep).astype(jnp.float32)
        wxm = (kf < dep_xm).astype(jnp.float32)
        wxp = (kf < dep_xp).astype(jnp.float32)
        wym = (kf < dep_ym).astype(jnp.float32)
        wyp = (kf < dep_yp).astype(jnp.float32)
        q = [r[k] * w0 for r in (t_ref, s_ref, u_ref, v_ref)]
        tile_n = north_ref[k] + fold_ref[k]
        tile_s = south_ref[k]
        ey = [lat_edge(tile_n, tile_s, c) for c in range(4)]
        ex = [lon_edge(tile_e, tile_w, j * 4 + c) for c in range(4)]
        xsh = {s: [xs(q[c], ex[c], s) for c in range(4)] for s in (-2, -1, 1, 2)}
        ysh = {s: [ys(q[c], ey[c], s) for c in range(4)] for s in (-2, -1, 1, 2)}
        a_r = 0.5 * (q[2] + xsh[1][2]) * w0 * wxp
        a_l = 0.5 * (xsh[-1][2] + q[2]) * wxm * w0
        b_r = 0.5 * (q[3] + ysh[1][3]) * w0 * wyp
        b_l = 0.5 * (ysh[-1][3] + q[3]) * wym * w0
        adv = []
        for c in range(4):
            div_x = face_flux(a_r, xsh[-1][c], q[c], xsh[1][c], xsh[2][c]) - face_flux(
                a_l, xsh[-2][c], xsh[-1][c], q[c], xsh[1][c]
            )
            div_y = face_flux(b_r, ysh[-1][c], q[c], ysh[1][c], ysh[2][c]) - face_flux(
                b_l, ysh[-2][c], ysh[-1][c], q[c], ysh[1][c]
            )
            adv.append(q[c] - courant * (div_x + div_y))
        load_xm = density(xsh[-1][0], xsh[-1][1], zmid) * wxm * h
        load_xp = density(xsh[1][0], xsh[1][1], zmid) * wxp * h
        load_ym = density(ysh[-1][0], ysh[-1][1], zmid) * wym * h
        load_yp = density(ysh[1][0], ysh[1][1], zmid) * wyp * h
        cum_xm = cum_xm + load_xm
        cum_xp = cum_xp + load_xp
        cum_ym = cum_ym + load_ym
        cum_yp = cum_yp + load_yp
        grad_x = 0.5 * ((cum_xp - 0.5 * load_xp) - (cum_xm - 0.5 * load_xm))
        grad_y = 0.5 * ((cum_yp - 0.5 * load_yp) - (cum_ym - 0.5 * load_ym))
        star0 = adv[0] * w0
        star1 = adv[1] * w0
        star2 = (adv[2] + time_step * (turning * q[3] - gravity * grad_x)) * w0
        star3 = (adv[3] + time_step * (-turning * q[2] - gravity * grad_y)) * w0
        for c, val in enumerate((star0, star1, star2, star3)):
            star_scr[c * layers + k] = val
        rs_scr[k] = density(star0, star1, zmid)
        return (cum_xm, cum_xp, cum_ym, cum_yp)

    lax.fori_loop(0, groups, explicit_group, (zero, zero, zero, zero))

    surface_scale = surface_gain * inv_h_ref[0]
    w_top = (0.0 < dep).astype(jnp.float32)
    for c in range(4):
        star_scr[c * layers] = star_scr[c * layers] + flux_ref[c] * w_top * surface_scale

    def forward(k, carry):
        mix_prev, r_a, r_b, s0, s1, s2, s3 = carry
        kf = k.astype(jnp.float32)
        inv_h = inv_h_ref[k]
        nxt = jnp.minimum(k + 1, layers - 1)
        stratified = (rs_scr[nxt] - rs_scr[k]) * inv_sp_ref[k]
        sig = 1.0 / (1.0 + jnp.exp(stratified * (1.0 / strat_scale)))
        w_next = (kf + 1.0 < dep).astype(jnp.float32)
        mix = (mix_back + mix_conv * sig) * w_next
        mix = jnp.where(k < layers - 1, mix, 0.0)
        low_a = -mix_prev * inv_h
        up_a = -mix * inv_h
        cen_a = 1.0 - low_a - up_a
        low_b = -mix_prev * momentum_mix * inv_h
        up_b = -mix * momentum_mix * inv_h
        floor = (kf == dep - 1.0).astype(jnp.float32)
        cen_b = 1.0 - low_b - up_b + bottom_drag * floor * inv_h
        inv_a = 1.0 / (cen_a - low_a * r_a)
        inv_b = 1.0 / (cen_b - low_b * r_b)
        r_a = up_a * inv_a
        r_b = up_b * inv_b
        r_scr[k] = r_a
        r_scr[layers + k] = r_b
        s0 = (star_scr[k] - low_a * s0) * inv_a
        s1 = (star_scr[layers + k] - low_a * s1) * inv_a
        s2 = (star_scr[2 * layers + k] - low_b * s2) * inv_b
        s3 = (star_scr[3 * layers + k] - low_b * s3) * inv_b
        star_scr[k] = s0
        star_scr[layers + k] = s1
        star_scr[2 * layers + k] = s2
        star_scr[3 * layers + k] = s3
        return (mix, r_a, r_b, s0, s1, s2, s3)

    lax.fori_loop(0, layers, forward, (zero,) * 7, unroll=3)

    def backward(i, carry):
        x0, x1, x2, x3 = carry
        k = layers - 1 - i
        r_a = r_scr[k]
        r_b = r_scr[layers + k]
        x0 = star_scr[k] - r_a * x0
        x1 = star_scr[layers + k] - r_a * x1
        x2 = star_scr[2 * layers + k] - r_b * x2
        x3 = star_scr[3 * layers + k] - r_b * x3
        o0_ref[k] = x0
        o1_ref[k] = x1
        o2_ref[k] = x2
        o3_ref[k] = x3
        return (x0, x1, x2, x3)

    lax.fori_loop(0, layers, backward, (zero,) * 4, unroll=3)


def level_tables(layers):
    offsets = np.arange(layers, dtype=np.float32) + np.float32(0.5)
    zmid = offsets / np.float32(layers)
    thickness = np.float32(0.5) + zmid
    inverse = np.float32(1.0) / thickness
    spacing = np.float32(0.5) * (thickness[1:] + thickness[:-1])
    inv_spacing = np.concatenate([np.float32(1.0) / spacing, np.ones((1,), np.float32)])
    return [jnp.asarray(t.astype(np.float32)) for t in (thickness, inverse, zmid, inv_spacing)]


def on_device(
    heat_anomaly,
    brine_anomaly,
    eastward_current,
    northward_current,
    shoreline_indicator,
    bottom_layer_index,
    boundary_fluxes,
):
    layers, rows, cols = heat_anomaly.shape
    fields = (heat_anomaly, brine_anomaly, eastward_current, northward_current)
    groups = layers // GROUP
    n_lat = lax.axis_size("lat")
    n_lon = lax.axis_size("lon")
    lat_idx = lax.axis_index("lat").astype(jnp.int32)
    is_last = (lat_idx == n_lat - 1).astype(jnp.int32).reshape(1)
    lat_info = jnp.stack([lat_idx, jnp.int32(n_lat)])

    smem = pl.BlockSpec(memory_space=pltpu.SMEM)
    vmem = pl.BlockSpec(memory_space=pltpu.VMEM)
    row_tiles = jax.ShapeDtypeStruct((layers + 1, rows, cols), jnp.float32)
    col_tiles = jax.ShapeDtypeStruct((groups + 1, rows, cols), jnp.float32)
    top, bot, fold, right, left = pl.pallas_call(
        pack_kernel,
        out_shape=(row_tiles, row_tiles, row_tiles, col_tiles, col_tiles),
        in_specs=[smem] + [vmem] * 6,
        out_specs=(vmem,) * 5,
    )(is_last, shoreline_indicator, bottom_layer_index, *fields)

    from_south = lax.ppermute(top, "lat", [(i, i + 1) for i in range(n_lat - 1)])
    from_north = lax.ppermute(bot, "lat", [(i + 1, i) for i in range(n_lat - 1)])
    from_west = lax.ppermute(right, "lon", [(i, (i + 1) % n_lon) for i in range(n_lon)])
    from_east = lax.ppermute(left, "lon", [((i + 1) % n_lon, i) for i in range(n_lon)])
    last = (n_lat - 1) * n_lon
    from_fold = lax.ppermute(
        fold, ("lat", "lon"), [(last + x, last + n_lon - 1 - x) for x in range(n_lon)]
    )

    plane = jax.ShapeDtypeStruct((layers, rows, cols), jnp.float32)
    outs = pl.pallas_call(
        step_kernel,
        out_shape=(plane,) * 4,
        in_specs=[smem] * 5 + [vmem] * 12,
        out_specs=(vmem,) * 4,
        scratch_shapes=[
            pltpu.VMEM((4 * layers, rows, cols), jnp.float32),
            pltpu.VMEM((2 * layers, rows, cols), jnp.float32),
            pltpu.VMEM((layers, rows, cols), jnp.float32),
        ],
    )(
        lat_info, *level_tables(layers),
        shoreline_indicator, bottom_layer_index, boundary_fluxes, *fields,
        from_south, from_north, from_fold, from_west, from_east,
    )
    return tuple(outs)


def solution(mesh):
    in_specs = (
        P(None, "lat", "lon"),
        P(None, "lat", "lon"),
        P(None, "lat", "lon"),
        P(None, "lat", "lon"),
        P("lat", "lon"),
        P("lat", "lon"),
        P(None, "lat", "lon"),
    )
    out_specs = (
        P(None, "lat", "lon"),
        P(None, "lat", "lon"),
        P(None, "lat", "lon"),
        P(None, "lat", "lon"),
    )
    return jax.shard_map(
        on_device, mesh=mesh, in_specs=in_specs, out_specs=out_specs, check_vma=False
    )
```

```python
import numpy as np
import jax
import jax.numpy as jnp
from jax import lax
from jax.experimental import pallas as pl
from jax.experimental.pallas import tpu as pltpu
from jax.sharding import PartitionSpec as P

courant = 0.25
time_step = 0.2
gravity = 0.2
coriolis = 0.5
thermal = 0.6
thermal_sq = 0.1
haline = 0.8
mix_back = 5.0
mix_conv = 60.0
strat_scale = 2.0
momentum_mix = 2.0
bottom_drag = 1.0
surface_gain = 0.5

GROUP = 15


def density(warmth, saltiness, depth_column):
    return -thermal * warmth * (1.0 + thermal_sq * warmth + depth_column) + haline * saltiness


def face_flux(face_vel, before, here, after, beyond):
    return face_vel * 0.5 * (here + after) - (
        jnp.maximum(face_vel, 0.0) * (after - 2.0 * here + before)
        + jnp.minimum(face_vel, 0.0) * (beyond - 2.0 * after + here)
    ) * (1.0 / 6.0)


def rolled(x, shift, axis):
    shift %= x.shape[axis]
    return x if shift == 0 else pltpu.roll(x, shift, axis)


def pack_lat_kernel(shore_ref, bottom_ref, t_ref, s_ref, u_ref, v_ref, top_ref, bot_ref):
    layers, rows, cols = t_ref.shape
    row = lax.broadcasted_iota(jnp.int32, (rows, cols), 0)
    dep = (shore_ref[...] * bottom_ref[...]).astype(jnp.float32)
    zero = jnp.zeros((rows, cols), jnp.float32)

    def pack_rows(vals, first):
        out = zero
        for c, val in enumerate(vals):
            out = jnp.where((row >> 1) == c, rolled(val, 2 * c - first, 0), out)
        return out

    def level_body(k, carry):
        w = (k.astype(jnp.float32) < dep).astype(jnp.float32)
        q = [r[k] * w for r in (t_ref, s_ref, u_ref, v_ref)]
        top_ref[k] = pack_rows(q, rows - 2)
        bot_ref[k] = pack_rows(q, 0)
        return carry

    lax.fori_loop(0, layers, level_body, 0, unroll=5)
    top_ref[layers] = pack_rows([dep], rows - 2)
    bot_ref[layers] = pack_rows([dep], 0)


def pack_fold_kernel(last_ref, top_ref, fold_ref):
    tiles_n, rows, cols = top_ref.shape

    @pl.when(last_ref[0] == 1)
    def _():
        tiles = top_ref[...].reshape(tiles_n * rows, cols)
        tile_row = lax.broadcasted_iota(jnp.int32, tiles.shape, 0) % rows
        sign = jnp.where(tile_row < 4, 1.0, -1.0)
        swapped = jnp.where(
            (tile_row & 1) == 0, rolled(tiles, -1, 0), rolled(tiles, 1, 0)
        ) * sign
        src_lane = lax.broadcasted_iota(jnp.int32, (cols, cols), 0)
        dst_lane = lax.broadcasted_iota(jnp.int32, (cols, cols), 1)
        reverse = (src_lane + dst_lane == cols - 1).astype(jnp.float32)
        flipped = jnp.dot(
            swapped, reverse, precision=lax.Precision.HIGHEST,
            preferred_element_type=jnp.float32,
        )
        fold_ref[...] = flipped.reshape(tiles_n, rows, cols)


def pack_lon_kernel(shore_ref, bottom_ref, t_ref, s_ref, u_ref, v_ref, right_ref, left_ref):
    layers, rows, cols = t_ref.shape
    groups = layers // GROUP
    lane = lax.broadcasted_iota(jnp.int32, (rows, cols), 1)
    dep = (shore_ref[...] * bottom_ref[...]).astype(jnp.float32)
    zero = jnp.zeros((rows, cols), jnp.float32)

    def group_body(g, carry):
        right = zero
        left = zero
        for j in range(GROUP):
            k = g * GROUP + j
            w = (k.astype(jnp.float32) < dep).astype(jnp.float32)
            q = [r[k] * w for r in (t_ref, s_ref, u_ref, v_ref)]
            for c in range(4):
                m = j * 4 + c
                slot = (lane >> 1) == m
                right = jnp.where(slot, rolled(q[c], 2 * m - (cols - 2), 1), right)
                left = jnp.where(slot, rolled(q[c], 2 * m, 1), left)
        right_ref[g] = right
        left_ref[g] = left
        return carry

    lax.fori_loop(0, groups, group_body, 0)
    right_ref[groups] = jnp.where(lane < 2, rolled(dep, 2, 1), zero)
    left_ref[groups] = jnp.where(lane < 2, dep, zero)


def step_kernel(
    lat_ref, h_ref, inv_h_ref, zmid_ref, inv_sp_ref,
    shore_ref, bottom_ref, flux_ref, t_ref, s_ref, u_ref, v_ref,
    south_ref, north_ref, fold_ref, west_ref, east_ref,
    o0_ref, o1_ref, o2_ref, o3_ref,
    star_scr, r_scr, rs_scr,
):
    layers = t_ref.shape[0]
    rows, cols = t_ref.shape[1], t_ref.shape[2]
    groups = layers // GROUP
    lane = lax.broadcasted_iota(jnp.int32, (rows, cols), 1)
    row = lax.broadcasted_iota(jnp.int32, (rows, cols), 0)

    def xs(v, e, s):
        if s == 1:
            return pltpu.roll(jnp.where(lane == 0, e, v), cols - 1, 1)
        if s == 2:
            return pltpu.roll(jnp.where(lane < 2, e, v), cols - 2, 1)
        if s == -1:
            return pltpu.roll(jnp.where(lane == cols - 1, e, v), 1, 1)
        return pltpu.roll(jnp.where(lane >= cols - 2, e, v), 2, 1)

    def ys(v, e, s):
        if s == 1:
            return pltpu.roll(jnp.where(row == 0, e, v), rows - 1, 0)
        if s == 2:
            return pltpu.roll(jnp.where(row < 2, e, v), rows - 2, 0)
        if s == -1:
            return pltpu.roll(jnp.where(row == rows - 1, e, v), 1, 0)
        return pltpu.roll(jnp.where(row >= rows - 2, e, v), 2, 0)

    def lat_edge(tile_n, tile_s, c):
        return jnp.where(row < 4, rolled(tile_n, -2 * c, 0), rolled(tile_s, rows - 2 - 2 * c, 0))

    def lon_edge(tile_e, tile_w, m):
        return jnp.where(lane < 64, rolled(tile_e, -2 * m, 1), rolled(tile_w, cols - 2 - 2 * m, 1))

    dep = (shore_ref[...] * bottom_ref[...]).astype(jnp.float32)
    dep_lat = lat_edge(north_ref[layers] + fold_ref[layers], south_ref[layers], 0)
    dep_lon = lon_edge(east_ref[groups], west_ref[groups], 0)
    dep_xm = xs(dep, dep_lon, -1)
    dep_xp = xs(dep, dep_lon, 1)
    dep_ym = ys(dep, dep_lat, -1)
    dep_yp = ys(dep, dep_lat, 1)
    total_rows = rows * lat_ref[1]
    row_ids = (lat_ref[0] * rows + row).astype(jnp.float32)
    turning = coriolis * (2.0 * (row_ids + 0.5) / total_rows.astype(jnp.float32) - 1.0)
    zero = jnp.zeros((rows, cols), jnp.float32)

    def explicit_group(g, carry):
        tile_e = east_ref[g]
        tile_w = west_ref[g]
        for j in range(GROUP):
            k = g * GROUP + j
            carry = explicit(k, j, tile_e, tile_w, carry)
        return carry

    def explicit(k, j, tile_e, tile_w, carry):
        cum_xm, cum_xp, cum_ym, cum_yp = carry
        kf = k.astype(jnp.float32)
        h = h_ref[k]
        zmid = zmid_ref[k]
        w0 = (kf < dep).astype(jnp.float32)
        wxm = (kf < dep_xm).astype(jnp.float32)
        wxp = (kf < dep_xp).astype(jnp.float32)
        wym = (kf < dep_ym).astype(jnp.float32)
        wyp = (kf < dep_yp).astype(jnp.float32)
        q = [r[k] * w0 for r in (t_ref, s_ref, u_ref, v_ref)]
        tile_n = north_ref[k] + fold_ref[k]
        tile_s = south_ref[k]
        ey = [lat_edge(tile_n, tile_s, c) for c in range(4)]
        ex = [lon_edge(tile_e, tile_w, j * 4 + c) for c in range(4)]
        xsh = {s: [xs(q[c], ex[c], s) for c in range(4)] for s in (-2, -1, 1, 2)}
        ysh = {s: [ys(q[c], ey[c], s) for c in range(4)] for s in (-2, -1, 1, 2)}
        a_r = 0.5 * (q[2] + xsh[1][2]) * w0 * wxp
        a_l = 0.5 * (xsh[-1][2] + q[2]) * wxm * w0
        b_r = 0.5 * (q[3] + ysh[1][3]) * w0 * wyp
        b_l = 0.5 * (ysh[-1][3] + q[3]) * wym * w0
        adv = []
        for c in range(4):
            div_x = face_flux(a_r, xsh[-1][c], q[c], xsh[1][c], xsh[2][c]) - face_flux(
                a_l, xsh[-2][c], xsh[-1][c], q[c], xsh[1][c]
            )
            div_y = face_flux(b_r, ysh[-1][c], q[c], ysh[1][c], ysh[2][c]) - face_flux(
                b_l, ysh[-2][c], ysh[-1][c], q[c], ysh[1][c]
            )
            adv.append(q[c] - courant * (div_x + div_y))
        load_xm = density(xsh[-1][0], xsh[-1][1], zmid) * wxm * h
        load_xp = density(xsh[1][0], xsh[1][1], zmid) * wxp * h
        load_ym = density(ysh[-1][0], ysh[-1][1], zmid) * wym * h
        load_yp = density(ysh[1][0], ysh[1][1], zmid) * wyp * h
        cum_xm = cum_xm + load_xm
        cum_xp = cum_xp + load_xp
        cum_ym = cum_ym + load_ym
        cum_yp = cum_yp + load_yp
        grad_x = 0.5 * ((cum_xp - 0.5 * load_xp) - (cum_xm - 0.5 * load_xm))
        grad_y = 0.5 * ((cum_yp - 0.5 * load_yp) - (cum_ym - 0.5 * load_ym))
        star0 = adv[0] * w0
        star1 = adv[1] * w0
        star2 = (adv[2] + time_step * (turning * q[3] - gravity * grad_x)) * w0
        star3 = (adv[3] + time_step * (-turning * q[2] - gravity * grad_y)) * w0
        for c, val in enumerate((star0, star1, star2, star3)):
            star_scr[c * layers + k] = val
        rs_scr[k] = density(star0, star1, zmid)
        return (cum_xm, cum_xp, cum_ym, cum_yp)

    lax.fori_loop(0, groups, explicit_group, (zero, zero, zero, zero))

    surface_scale = surface_gain * inv_h_ref[0]
    w_top = (0.0 < dep).astype(jnp.float32)
    for c in range(4):
        star_scr[c * layers] = star_scr[c * layers] + flux_ref[c] * w_top * surface_scale

    def forward(k, carry):
        mix_prev, r_a, r_b, s0, s1, s2, s3 = carry
        kf = k.astype(jnp.float32)
        inv_h = inv_h_ref[k]
        nxt = jnp.minimum(k + 1, layers - 1)
        stratified = (rs_scr[nxt] - rs_scr[k]) * inv_sp_ref[k]
        sig = 1.0 / (1.0 + jnp.exp(stratified * (1.0 / strat_scale)))
        w_next = (kf + 1.0 < dep).astype(jnp.float32)
        mix = (mix_back + mix_conv * sig) * w_next
        mix = jnp.where(k < layers - 1, mix, 0.0)
        low_a = -mix_prev * inv_h
        up_a = -mix * inv_h
        cen_a = 1.0 - low_a - up_a
        low_b = -mix_prev * momentum_mix * inv_h
        up_b = -mix * momentum_mix * inv_h
        floor = (kf == dep - 1.0).astype(jnp.float32)
        cen_b = 1.0 - low_b - up_b + bottom_drag * floor * inv_h
        inv_a = 1.0 / (cen_a - low_a * r_a)
        inv_b = 1.0 / (cen_b - low_b * r_b)
        r_a = up_a * inv_a
        r_b = up_b * inv_b
        r_scr[k] = r_a
        r_scr[layers + k] = r_b
        s0 = (star_scr[k] - low_a * s0) * inv_a
        s1 = (star_scr[layers + k] - low_a * s1) * inv_a
        s2 = (star_scr[2 * layers + k] - low_b * s2) * inv_b
        s3 = (star_scr[3 * layers + k] - low_b * s3) * inv_b
        star_scr[k] = s0
        star_scr[layers + k] = s1
        star_scr[2 * layers + k] = s2
        star_scr[3 * layers + k] = s3
        return (mix, r_a, r_b, s0, s1, s2, s3)

    lax.fori_loop(0, layers, forward, (zero,) * 7, unroll=3)

    def backward(i, carry):
        x0, x1, x2, x3 = carry
        k = layers - 1 - i
        r_a = r_scr[k]
        r_b = r_scr[layers + k]
        x0 = star_scr[k] - r_a * x0
        x1 = star_scr[layers + k] - r_a * x1
        x2 = star_scr[2 * layers + k] - r_b * x2
        x3 = star_scr[3 * layers + k] - r_b * x3
        o0_ref[k] = x0
        o1_ref[k] = x1
        o2_ref[k] = x2
        o3_ref[k] = x3
        return (x0, x1, x2, x3)

    lax.fori_loop(0, layers, backward, (zero,) * 4, unroll=3)


def level_tables(layers):
    offsets = np.arange(layers, dtype=np.float32) + np.float32(0.5)
    zmid = offsets / np.float32(layers)
    thickness = np.float32(0.5) + zmid
    inverse = np.float32(1.0) / thickness
    spacing = np.float32(0.5) * (thickness[1:] + thickness[:-1])
    inv_spacing = np.concatenate([np.float32(1.0) / spacing, np.ones((1,), np.float32)])
    return [jnp.asarray(t.astype(np.float32)) for t in (thickness, inverse, zmid, inv_spacing)]


def on_device(
    heat_anomaly,
    brine_anomaly,
    eastward_current,
    northward_current,
    shoreline_indicator,
    bottom_layer_index,
    boundary_fluxes,
):
    layers, rows, cols = heat_anomaly.shape
    fields = (heat_anomaly, brine_anomaly, eastward_current, northward_current)
    groups = layers // GROUP
    n_lat = lax.axis_size("lat")
    n_lon = lax.axis_size("lon")
    lat_idx = lax.axis_index("lat").astype(jnp.int32)
    is_last = (lat_idx == n_lat - 1).astype(jnp.int32).reshape(1)
    lat_info = jnp.stack([lat_idx, jnp.int32(n_lat)])

    smem = pl.BlockSpec(memory_space=pltpu.SMEM)
    vmem = pl.BlockSpec(memory_space=pltpu.VMEM)
    row_tiles = jax.ShapeDtypeStruct((layers + 1, rows, cols), jnp.float32)
    col_tiles = jax.ShapeDtypeStruct((groups + 1, rows, cols), jnp.float32)
    top, bot = pl.pallas_call(
        pack_lat_kernel,
        out_shape=(row_tiles, row_tiles),
        in_specs=[vmem] * 6,
        out_specs=(vmem,) * 2,
    )(shoreline_indicator, bottom_layer_index, *fields)
    from_south = lax.ppermute(top, "lat", [(i, i + 1) for i in range(n_lat - 1)])
    from_north = lax.ppermute(bot, "lat", [(i + 1, i) for i in range(n_lat - 1)])
    fold = pl.pallas_call(
        pack_fold_kernel,
        out_shape=row_tiles,
        in_specs=[smem, vmem],
        out_specs=vmem,
    )(is_last, top)
    last = (n_lat - 1) * n_lon
    from_fold = lax.ppermute(
        fold, ("lat", "lon"), [(last + x, last + n_lon - 1 - x) for x in range(n_lon)]
    )
    right, left = pl.pallas_call(
        pack_lon_kernel,
        out_shape=(col_tiles, col_tiles),
        in_specs=[vmem] * 6,
        out_specs=(vmem,) * 2,
    )(shoreline_indicator, bottom_layer_index, *fields)
    from_west = lax.ppermute(right, "lon", [(i, (i + 1) % n_lon) for i in range(n_lon)])
    from_east = lax.ppermute(left, "lon", [((i + 1) % n_lon, i) for i in range(n_lon)])

    plane = jax.ShapeDtypeStruct((layers, rows, cols), jnp.float32)
    outs = pl.pallas_call(
        step_kernel,
        out_shape=(plane,) * 4,
        in_specs=[smem] * 5 + [vmem] * 12,
        out_specs=(vmem,) * 4,
        scratch_shapes=[
            pltpu.VMEM((4 * layers, rows, cols), jnp.float32),
            pltpu.VMEM((2 * layers, rows, cols), jnp.float32),
            pltpu.VMEM((layers, rows, cols), jnp.float32),
        ],
    )(
        lat_info, *level_tables(layers),
        shoreline_indicator, bottom_layer_index, boundary_fluxes, *fields,
        from_south, from_north, from_fold, from_west, from_east,
    )
    return tuple(outs)


def solution(mesh):
    in_specs = (
        P(None, "lat", "lon"),
        P(None, "lat", "lon"),
        P(None, "lat", "lon"),
        P(None, "lat", "lon"),
        P("lat", "lon"),
        P("lat", "lon"),
        P(None, "lat", "lon"),
    )
    out_specs = (
        P(None, "lat", "lon"),
        P(None, "lat", "lon"),
        P(None, "lat", "lon"),
        P(None, "lat", "lon"),
    )
    return jax.shard_map(
        on_device, mesh=mesh, in_specs=in_specs, out_specs=out_specs, check_vma=False
    )
```

```python
import numpy as np
import jax
import jax.numpy as jnp
from jax import lax
from jax.experimental import pallas as pl
from jax.experimental.pallas import tpu as pltpu
from jax.sharding import PartitionSpec as P

courant = 0.25
time_step = 0.2
gravity = 0.2
coriolis = 0.5
thermal = 0.6
thermal_sq = 0.1
haline = 0.8
mix_back = 5.0
mix_conv = 60.0
strat_scale = 2.0
momentum_mix = 2.0
bottom_drag = 1.0
surface_gain = 0.5

GROUP = 15


def density(warmth, saltiness, depth_column):
    return -thermal * warmth * (1.0 + thermal_sq * warmth + depth_column) + haline * saltiness


def face_flux(face_vel, before, here, after, beyond):
    return face_vel * 0.5 * (here + after) - (
        jnp.maximum(face_vel, 0.0) * (after - 2.0 * here + before)
        + jnp.minimum(face_vel, 0.0) * (beyond - 2.0 * after + here)
    ) * (1.0 / 6.0)


def rolled(x, shift, axis):
    shift %= x.shape[axis]
    return x if shift == 0 else pltpu.roll(x, shift, axis)


def pack_kernel(
    last_ref, shore_ref, bottom_ref, t_ref, s_ref, u_ref, v_ref,
    top_ref, bot_ref, fold_ref, right_ref, left_ref,
):
    layers, rows, cols = t_ref.shape
    groups = layers // GROUP
    lane = lax.broadcasted_iota(jnp.int32, (rows, cols), 1)
    row = lax.broadcasted_iota(jnp.int32, (rows, cols), 0)
    dep = (shore_ref[...] * bottom_ref[...]).astype(jnp.float32)
    zero = jnp.zeros((rows, cols), jnp.float32)

    def pack_rows(vals, first):
        out = zero
        for c, val in enumerate(vals):
            out = jnp.where((row >> 1) == c, rolled(val, 2 * c - first, 0), out)
        return out

    def group_body(g, carry):
        right = zero
        left = zero
        for j in range(GROUP):
            k = g * GROUP + j
            w = (k.astype(jnp.float32) < dep).astype(jnp.float32)
            q = [r[k] * w for r in (t_ref, s_ref, u_ref, v_ref)]
            top_ref[k] = pack_rows(q, rows - 2)
            bot_ref[k] = pack_rows(q, 0)
            for c in range(4):
                m = j * 4 + c
                slot = (lane >> 1) == m
                right = jnp.where(slot, rolled(q[c], 2 * m - (cols - 2), 1), right)
                left = jnp.where(slot, rolled(q[c], 2 * m, 1), left)
        right_ref[g] = right
        left_ref[g] = left
        return carry

    lax.fori_loop(0, groups, group_body, 0)
    top_ref[layers] = pack_rows([dep], rows - 2)
    bot_ref[layers] = pack_rows([dep], 0)
    right_ref[groups] = jnp.where(lane < 2, rolled(dep, 2, 1), zero)
    left_ref[groups] = jnp.where(lane < 2, dep, zero)

    @pl.when(last_ref[0] == 1)
    def _():
        tiles = top_ref[...].reshape((layers + 1) * rows, cols)
        tile_row = lax.broadcasted_iota(jnp.int32, tiles.shape, 0) % rows
        sign = jnp.where(tile_row < 4, 1.0, -1.0)
        swapped = jnp.where(
            (tile_row & 1) == 0, rolled(tiles, -1, 0), rolled(tiles, 1, 0)
        ) * sign
        src_lane = lax.broadcasted_iota(jnp.int32, (cols, cols), 0)
        dst_lane = lax.broadcasted_iota(jnp.int32, (cols, cols), 1)
        reverse = (src_lane + dst_lane == cols - 1).astype(jnp.float32)
        flipped = jnp.dot(
            swapped, reverse, precision=lax.Precision.HIGHEST,
            preferred_element_type=jnp.float32,
        )
        fold_ref[...] = flipped.reshape(layers + 1, rows, cols)


def xpart_kernel(
    h_ref, zmid_ref, shore_ref, bottom_ref, t_ref, s_ref, u_ref, v_ref, west_ref, east_ref,
    divx_ref, gradx_ref,
):
    layers, rows, cols = t_ref.shape
    groups = layers // GROUP
    lane = lax.broadcasted_iota(jnp.int32, (rows, cols), 1)

    def xs(v, e, s):
        if s == 1:
            return pltpu.roll(jnp.where(lane == 0, e, v), cols - 1, 1)
        if s == 2:
            return pltpu.roll(jnp.where(lane < 2, e, v), cols - 2, 1)
        if s == -1:
            return pltpu.roll(jnp.where(lane == cols - 1, e, v), 1, 1)
        return pltpu.roll(jnp.where(lane >= cols - 2, e, v), 2, 1)

    def lon_edge(tile_e, tile_w, m):
        return jnp.where(lane < 64, rolled(tile_e, -2 * m, 1), rolled(tile_w, cols - 2 - 2 * m, 1))

    dep = (shore_ref[...] * bottom_ref[...]).astype(jnp.float32)
    dep_lon = lon_edge(east_ref[groups], west_ref[groups], 0)
    dep_xm = xs(dep, dep_lon, -1)
    dep_xp = xs(dep, dep_lon, 1)
    zero = jnp.zeros((rows, cols), jnp.float32)

    def group_body(g, carry):
        tile_e = east_ref[g]
        tile_w = west_ref[g]
        for j in range(GROUP):
            cum_xm, cum_xp = carry
            k = g * GROUP + j
            kf = k.astype(jnp.float32)
            h = h_ref[k]
            zmid = zmid_ref[k]
            w0 = (kf < dep).astype(jnp.float32)
            wxm = (kf < dep_xm).astype(jnp.float32)
            wxp = (kf < dep_xp).astype(jnp.float32)
            q = [r[k] * w0 for r in (t_ref, s_ref, u_ref, v_ref)]
            ex = [lon_edge(tile_e, tile_w, j * 4 + c) for c in range(4)]
            xsh = {s: [xs(q[c], ex[c], s) for c in range(4)] for s in (-2, -1, 1, 2)}
            a_r = 0.5 * (q[2] + xsh[1][2]) * w0 * wxp
            a_l = 0.5 * (xsh[-1][2] + q[2]) * wxm * w0
            for c in range(4):
                divx_ref[c * layers + k] = face_flux(
                    a_r, xsh[-1][c], q[c], xsh[1][c], xsh[2][c]
                ) - face_flux(a_l, xsh[-2][c], xsh[-1][c], q[c], xsh[1][c])
            load_xm = density(xsh[-1][0], xsh[-1][1], zmid) * wxm * h
            load_xp = density(xsh[1][0], xsh[1][1], zmid) * wxp * h
            cum_xm = cum_xm + load_xm
            cum_xp = cum_xp + load_xp
            gradx_ref[k] = 0.5 * ((cum_xp - 0.5 * load_xp) - (cum_xm - 0.5 * load_xm))
            carry = (cum_xm, cum_xp)
        return carry

    lax.fori_loop(0, groups, group_body, (zero, zero))


def step_kernel(
    lat_ref, h_ref, inv_h_ref, zmid_ref, inv_sp_ref,
    shore_ref, bottom_ref, flux_ref, t_ref, s_ref, u_ref, v_ref,
    south_ref, north_ref, fold_ref, divx_ref, gradx_ref,
    o0_ref, o1_ref, o2_ref, o3_ref,
    star_scr, r_scr, rs_scr,
):
    layers = t_ref.shape[0]
    rows, cols = t_ref.shape[1], t_ref.shape[2]
    groups = layers // GROUP
    lane = lax.broadcasted_iota(jnp.int32, (rows, cols), 1)
    row = lax.broadcasted_iota(jnp.int32, (rows, cols), 0)

    def ys(v, e, s):
        if s == 1:
            return pltpu.roll(jnp.where(row == 0, e, v), rows - 1, 0)
        if s == 2:
            return pltpu.roll(jnp.where(row < 2, e, v), rows - 2, 0)
        if s == -1:
            return pltpu.roll(jnp.where(row == rows - 1, e, v), 1, 0)
        return pltpu.roll(jnp.where(row >= rows - 2, e, v), 2, 0)

    def lat_edge(tile_n, tile_s, c):
        return jnp.where(row < 4, rolled(tile_n, -2 * c, 0), rolled(tile_s, rows - 2 - 2 * c, 0))

    dep = (shore_ref[...] * bottom_ref[...]).astype(jnp.float32)
    dep_lat = lat_edge(north_ref[layers] + fold_ref[layers], south_ref[layers], 0)
    dep_ym = ys(dep, dep_lat, -1)
    dep_yp = ys(dep, dep_lat, 1)
    total_rows = rows * lat_ref[1]
    row_ids = (lat_ref[0] * rows + row).astype(jnp.float32)
    turning = coriolis * (2.0 * (row_ids + 0.5) / total_rows.astype(jnp.float32) - 1.0)
    zero = jnp.zeros((rows, cols), jnp.float32)

    def explicit(k, carry):
        cum_ym, cum_yp = carry
        kf = k.astype(jnp.float32)
        h = h_ref[k]
        zmid = zmid_ref[k]
        w0 = (kf < dep).astype(jnp.float32)
        wym = (kf < dep_ym).astype(jnp.float32)
        wyp = (kf < dep_yp).astype(jnp.float32)
        q = [r[k] * w0 for r in (t_ref, s_ref, u_ref, v_ref)]
        tile_n = north_ref[k] + fold_ref[k]
        tile_s = south_ref[k]
        ey = [lat_edge(tile_n, tile_s, c) for c in range(4)]
        ysh = {s: [ys(q[c], ey[c], s) for c in range(4)] for s in (-2, -1, 1, 2)}
        b_r = 0.5 * (q[3] + ysh[1][3]) * w0 * wyp
        b_l = 0.5 * (ysh[-1][3] + q[3]) * wym * w0
        adv = []
        for c in range(4):
            div_y = face_flux(b_r, ysh[-1][c], q[c], ysh[1][c], ysh[2][c]) - face_flux(
                b_l, ysh[-2][c], ysh[-1][c], q[c], ysh[1][c]
            )
            adv.append(q[c] - courant * (divx_ref[c * layers + k] + div_y))
        load_ym = density(ysh[-1][0], ysh[-1][1], zmid) * wym * h
        load_yp = density(ysh[1][0], ysh[1][1], zmid) * wyp * h
        cum_ym = cum_ym + load_ym
        cum_yp = cum_yp + load_yp
        grad_x = gradx_ref[k]
        grad_y = 0.5 * ((cum_yp - 0.5 * load_yp) - (cum_ym - 0.5 * load_ym))
        star0 = adv[0] * w0
        star1 = adv[1] * w0
        star2 = (adv[2] + time_step * (turning * q[3] - gravity * grad_x)) * w0
        star3 = (adv[3] + time_step * (-turning * q[2] - gravity * grad_y)) * w0
        for c, val in enumerate((star0, star1, star2, star3)):
            star_scr[c * layers + k] = val
        rs_scr[k] = density(star0, star1, zmid)
        return (cum_ym, cum_yp)

    lax.fori_loop(0, layers, explicit, (zero, zero), unroll=3)

    surface_scale = surface_gain * inv_h_ref[0]
    w_top = (0.0 < dep).astype(jnp.float32)
    for c in range(4):
        star_scr[c * layers] = star_scr[c * layers] + flux_ref[c] * w_top * surface_scale

    def forward(k, carry):
        mix_prev, r_a, r_b, s0, s1, s2, s3 = carry
        kf = k.astype(jnp.float32)
        inv_h = inv_h_ref[k]
        nxt = jnp.minimum(k + 1, layers - 1)
        stratified = (rs_scr[nxt] - rs_scr[k]) * inv_sp_ref[k]
        sig = 1.0 / (1.0 + jnp.exp(stratified * (1.0 / strat_scale)))
        w_next = (kf + 1.0 < dep).astype(jnp.float32)
        mix = (mix_back + mix_conv * sig) * w_next
        mix = jnp.where(k < layers - 1, mix, 0.0)
        low_a = -mix_prev * inv_h
        up_a = -mix * inv_h
        cen_a = 1.0 - low_a - up_a
        low_b = -mix_prev * momentum_mix * inv_h
        up_b = -mix * momentum_mix * inv_h
        floor = (kf == dep - 1.0).astype(jnp.float32)
        cen_b = 1.0 - low_b - up_b + bottom_drag * floor * inv_h
        inv_a = 1.0 / (cen_a - low_a * r_a)
        inv_b = 1.0 / (cen_b - low_b * r_b)
        r_a = up_a * inv_a
        r_b = up_b * inv_b
        r_scr[k] = r_a
        r_scr[layers + k] = r_b
        s0 = (star_scr[k] - low_a * s0) * inv_a
        s1 = (star_scr[layers + k] - low_a * s1) * inv_a
        s2 = (star_scr[2 * layers + k] - low_b * s2) * inv_b
        s3 = (star_scr[3 * layers + k] - low_b * s3) * inv_b
        star_scr[k] = s0
        star_scr[layers + k] = s1
        star_scr[2 * layers + k] = s2
        star_scr[3 * layers + k] = s3
        return (mix, r_a, r_b, s0, s1, s2, s3)

    lax.fori_loop(0, layers, forward, (zero,) * 7, unroll=3)

    def backward(i, carry):
        x0, x1, x2, x3 = carry
        k = layers - 1 - i
        r_a = r_scr[k]
        r_b = r_scr[layers + k]
        x0 = star_scr[k] - r_a * x0
        x1 = star_scr[layers + k] - r_a * x1
        x2 = star_scr[2 * layers + k] - r_b * x2
        x3 = star_scr[3 * layers + k] - r_b * x3
        o0_ref[k] = x0
        o1_ref[k] = x1
        o2_ref[k] = x2
        o3_ref[k] = x3
        return (x0, x1, x2, x3)

    lax.fori_loop(0, layers, backward, (zero,) * 4, unroll=3)


def level_tables(layers):
    offsets = np.arange(layers, dtype=np.float32) + np.float32(0.5)
    zmid = offsets / np.float32(layers)
    thickness = np.float32(0.5) + zmid
    inverse = np.float32(1.0) / thickness
    spacing = np.float32(0.5) * (thickness[1:] + thickness[:-1])
    inv_spacing = np.concatenate([np.float32(1.0) / spacing, np.ones((1,), np.float32)])
    return [jnp.asarray(t.astype(np.float32)) for t in (thickness, inverse, zmid, inv_spacing)]


def on_device(
    heat_anomaly,
    brine_anomaly,
    eastward_current,
    northward_current,
    shoreline_indicator,
    bottom_layer_index,
    boundary_fluxes,
):
    layers, rows, cols = heat_anomaly.shape
    fields = (heat_anomaly, brine_anomaly, eastward_current, northward_current)
    groups = layers // GROUP
    n_lat = lax.axis_size("lat")
    n_lon = lax.axis_size("lon")
    lat_idx = lax.axis_index("lat").astype(jnp.int32)
    is_last = (lat_idx == n_lat - 1).astype(jnp.int32).reshape(1)
    lat_info = jnp.stack([lat_idx, jnp.int32(n_lat)])

    smem = pl.BlockSpec(memory_space=pltpu.SMEM)
    vmem = pl.BlockSpec(memory_space=pltpu.VMEM)
    row_tiles = jax.ShapeDtypeStruct((layers + 1, rows, cols), jnp.float32)
    col_tiles = jax.ShapeDtypeStruct((groups + 1, rows, cols), jnp.float32)
    top, bot, fold, right, left = pl.pallas_call(
        pack_kernel,
        out_shape=(row_tiles, row_tiles, row_tiles, col_tiles, col_tiles),
        in_specs=[smem] + [vmem] * 6,
        out_specs=(vmem,) * 5,
    )(is_last, shoreline_indicator, bottom_layer_index, *fields)

    from_south = lax.ppermute(top, "lat", [(i, i + 1) for i in range(n_lat - 1)])
    from_north = lax.ppermute(bot, "lat", [(i + 1, i) for i in range(n_lat - 1)])
    from_west = lax.ppermute(right, "lon", [(i, (i + 1) % n_lon) for i in range(n_lon)])
    from_east = lax.ppermute(left, "lon", [((i + 1) % n_lon, i) for i in range(n_lon)])
    last = (n_lat - 1) * n_lon
    from_fold = lax.ppermute(
        fold, ("lat", "lon"), [(last + x, last + n_lon - 1 - x) for x in range(n_lon)]
    )

    plane = jax.ShapeDtypeStruct((layers, rows, cols), jnp.float32)
    tables = level_tables(layers)
    divx, gradx = pl.pallas_call(
        xpart_kernel,
        out_shape=(jax.ShapeDtypeStruct((4 * layers, rows, cols), jnp.float32), plane),
        in_specs=[smem] * 2 + [vmem] * 8,
        out_specs=(vmem,) * 2,
    )(tables[0], tables[2], shoreline_indicator, bottom_layer_index, *fields, from_west, from_east)
    outs = pl.pallas_call(
        step_kernel,
        out_shape=(plane,) * 4,
        in_specs=[smem] * 5 + [vmem] * 12,
        out_specs=(vmem,) * 4,
        scratch_shapes=[
            pltpu.VMEM((4 * layers, rows, cols), jnp.float32),
            pltpu.VMEM((2 * layers, rows, cols), jnp.float32),
            pltpu.VMEM((layers, rows, cols), jnp.float32),
        ],
    )(
        lat_info, *tables,
        shoreline_indicator, bottom_layer_index, boundary_fluxes, *fields,
        from_south, from_north, from_fold, divx, gradx,
    )
    return tuple(outs)


def solution(mesh):
    in_specs = (
        P(None, "lat", "lon"),
        P(None, "lat", "lon"),
        P(None, "lat", "lon"),
        P(None, "lat", "lon"),
        P("lat", "lon"),
        P("lat", "lon"),
        P(None, "lat", "lon"),
    )
    out_specs = (
        P(None, "lat", "lon"),
        P(None, "lat", "lon"),
        P(None, "lat", "lon"),
        P(None, "lat", "lon"),
    )
    return jax.shard_map(
        on_device, mesh=mesh, in_specs=in_specs, out_specs=out_specs, check_vma=False
    )
```

```python
import numpy as np
import jax
import jax.numpy as jnp
from jax import lax
from jax.experimental import pallas as pl
from jax.experimental.pallas import tpu as pltpu
from jax.sharding import PartitionSpec as P

courant = 0.25
time_step = 0.2
gravity = 0.2
coriolis = 0.5
thermal = 0.6
thermal_sq = 0.1
haline = 0.8
mix_back = 5.0
mix_conv = 60.0
strat_scale = 2.0
momentum_mix = 2.0
bottom_drag = 1.0
surface_gain = 0.5

GROUP = 15


def density(warmth, saltiness, depth_column):
    return -thermal * warmth * (1.0 + thermal_sq * warmth + depth_column) + haline * saltiness


def face_flux(face_vel, before, here, after, beyond):
    return face_vel * 0.5 * (here + after) - (
        jnp.maximum(face_vel, 0.0) * (after - 2.0 * here + before)
        + jnp.minimum(face_vel, 0.0) * (beyond - 2.0 * after + here)
    ) * (1.0 / 6.0)


def rolled(x, shift, axis):
    shift %= x.shape[axis]
    return x if shift == 0 else pltpu.roll(x, shift, axis)


def pack_kernel(
    last_ref, shore_ref, bottom_ref, t_ref, s_ref, u_ref, v_ref,
    top_ref, bot_ref, fold_ref, right_ref, left_ref,
):
    layers, rows, cols = t_ref.shape
    groups = layers // GROUP
    lane = lax.broadcasted_iota(jnp.int32, (rows, cols), 1)
    row = lax.broadcasted_iota(jnp.int32, (rows, cols), 0)
    dep = (shore_ref[...] * bottom_ref[...]).astype(jnp.float32)
    zero = jnp.zeros((rows, cols), jnp.float32)

    def pack_rows(vals, first):
        out = zero
        for c, val in enumerate(vals):
            out = jnp.where((row >> 1) == c, rolled(val, 2 * c - first, 0), out)
        return out

    def group_body(g, carry):
        right = zero
        left = zero
        for j in range(GROUP):
            k = g * GROUP + j
            w = (k.astype(jnp.float32) < dep).astype(jnp.float32)
            q = [r[k] * w for r in (t_ref, s_ref, u_ref, v_ref)]
            top_ref[k] = pack_rows(q, rows - 2)
            bot_ref[k] = pack_rows(q, 0)
            for c in range(4):
                m = j * 4 + c
                slot = (lane >> 1) == m
                right = jnp.where(slot, rolled(q[c], 2 * m - (cols - 2), 1), right)
                left = jnp.where(slot, rolled(q[c], 2 * m, 1), left)
        right_ref[g] = right
        left_ref[g] = left
        return carry

    lax.fori_loop(0, groups, group_body, 0)
    top_ref[layers] = pack_rows([dep], rows - 2)
    bot_ref[layers] = pack_rows([dep], 0)
    right_ref[groups] = jnp.where(lane < 2, rolled(dep, 2, 1), zero)
    left_ref[groups] = jnp.where(lane < 2, dep, zero)

    @pl.when(last_ref[0] == 1)
    def _():
        tiles = top_ref[...].reshape((layers + 1) * rows, cols)
        tile_row = lax.broadcasted_iota(jnp.int32, tiles.shape, 0) % rows
        sign = jnp.where(tile_row < 4, 1.0, -1.0)
        swapped = jnp.where(
            (tile_row & 1) == 0, rolled(tiles, -1, 0), rolled(tiles, 1, 0)
        ) * sign
        src_lane = lax.broadcasted_iota(jnp.int32, (cols, cols), 0)
        dst_lane = lax.broadcasted_iota(jnp.int32, (cols, cols), 1)
        reverse = (src_lane + dst_lane == cols - 1).astype(jnp.float32)
        flipped = jnp.dot(
            swapped, reverse, precision=lax.Precision.HIGHEST,
            preferred_element_type=jnp.float32,
        )
        fold_ref[...] = flipped.reshape(layers + 1, rows, cols)


def xpart_kernel(
    h_ref, zmid_ref, shore_ref, bottom_ref, t_ref, s_ref, u_ref, v_ref, west_ref, east_ref,
    divx_ref, gradx_ref,
):
    layers, rows, cols = t_ref.shape
    groups = layers // GROUP
    lane = lax.broadcasted_iota(jnp.int32, (rows, cols), 1)

    def xs(v, e, s):
        if s == 1:
            return pltpu.roll(jnp.where(lane == 0, e, v), cols - 1, 1)
        if s == 2:
            return pltpu.roll(jnp.where(lane < 2, e, v), cols - 2, 1)
        if s == -1:
            return pltpu.roll(jnp.where(lane == cols - 1, e, v), 1, 1)
        return pltpu.roll(jnp.where(lane >= cols - 2, e, v), 2, 1)

    def lon_edge(tile_e, tile_w, m):
        return jnp.where(lane < 64, rolled(tile_e, -2 * m, 1), rolled(tile_w, cols - 2 - 2 * m, 1))

    dep = (shore_ref[...] * bottom_ref[...]).astype(jnp.float32)
    dep_lon = lon_edge(east_ref[groups], west_ref[groups], 0)
    dep_xm = xs(dep, dep_lon, -1)
    dep_xp = xs(dep, dep_lon, 1)
    zero = jnp.zeros((rows, cols), jnp.float32)

    def group_body(g, carry):
        tile_e = east_ref[g]
        tile_w = west_ref[g]
        for j in range(GROUP):
            cum_xm, cum_xp = carry
            k = g * GROUP + j
            kf = k.astype(jnp.float32)
            h = h_ref[k]
            zmid = zmid_ref[k]
            w0 = (kf < dep).astype(jnp.float32)
            wxm = (kf < dep_xm).astype(jnp.float32)
            wxp = (kf < dep_xp).astype(jnp.float32)
            q = [r[k] * w0 for r in (t_ref, s_ref, u_ref, v_ref)]
            ex = [lon_edge(tile_e, tile_w, j * 4 + c) for c in range(4)]
            xsh = {s: [xs(q[c], ex[c], s) for c in range(4)] for s in (-2, -1, 1, 2)}
            a_r = 0.5 * (q[2] + xsh[1][2]) * w0 * wxp
            a_l = 0.5 * (xsh[-1][2] + q[2]) * wxm * w0
            for c in range(4):
                divx_ref[c * layers + k] = face_flux(
                    a_r, xsh[-1][c], q[c], xsh[1][c], xsh[2][c]
                ) - face_flux(a_l, xsh[-2][c], xsh[-1][c], q[c], xsh[1][c])
            load_xm = density(xsh[-1][0], xsh[-1][1], zmid) * wxm * h
            load_xp = density(xsh[1][0], xsh[1][1], zmid) * wxp * h
            cum_xm = cum_xm + load_xm
            cum_xp = cum_xp + load_xp
            gradx_ref[k] = 0.5 * ((cum_xp - 0.5 * load_xp) - (cum_xm - 0.5 * load_xm))
            carry = (cum_xm, cum_xp)
        return carry

    lax.fori_loop(0, groups, group_body, (zero, zero))


def step_kernel(
    lat_ref, h_ref, inv_h_ref, zmid_ref, inv_sp_ref,
    shore_ref, bottom_ref, flux_ref, t_ref, s_ref, u_ref, v_ref,
    south_ref, north_ref, fold_ref, divx_ref, gradx_ref,
    o0_ref, o1_ref, o2_ref, o3_ref,
    star_scr, r_scr, rs_scr,
):
    layers = t_ref.shape[0]
    rows, cols = t_ref.shape[1], t_ref.shape[2]
    groups = layers // GROUP
    lane = lax.broadcasted_iota(jnp.int32, (rows, cols), 1)
    row = lax.broadcasted_iota(jnp.int32, (rows, cols), 0)

    def ys(v, e, s):
        if s == 1:
            return pltpu.roll(jnp.where(row == 0, e, v), rows - 1, 0)
        if s == 2:
            return pltpu.roll(jnp.where(row < 2, e, v), rows - 2, 0)
        if s == -1:
            return pltpu.roll(jnp.where(row == rows - 1, e, v), 1, 0)
        return pltpu.roll(jnp.where(row >= rows - 2, e, v), 2, 0)

    def lat_edge(tile_n, tile_s, c):
        return jnp.where(row < 4, rolled(tile_n, -2 * c, 0), rolled(tile_s, rows - 2 - 2 * c, 0))

    dep = (shore_ref[...] * bottom_ref[...]).astype(jnp.float32)
    dep_lat = lat_edge(north_ref[layers] + fold_ref[layers], south_ref[layers], 0)
    dep_ym = ys(dep, dep_lat, -1)
    dep_yp = ys(dep, dep_lat, 1)
    total_rows = rows * lat_ref[1]
    row_ids = (lat_ref[0] * rows + row).astype(jnp.float32)
    turning = coriolis * (2.0 * (row_ids + 0.5) / total_rows.astype(jnp.float32) - 1.0)
    zero = jnp.zeros((rows, cols), jnp.float32)

    def explicit(k, carry):
        cum_ym, cum_yp = carry
        kf = k.astype(jnp.float32)
        h = h_ref[k]
        zmid = zmid_ref[k]
        w0 = (kf < dep).astype(jnp.float32)
        wym = (kf < dep_ym).astype(jnp.float32)
        wyp = (kf < dep_yp).astype(jnp.float32)
        q = [r[k] * w0 for r in (t_ref, s_ref, u_ref, v_ref)]
        tile_n = north_ref[k] + fold_ref[k]
        tile_s = south_ref[k]
        ey = [lat_edge(tile_n, tile_s, c) for c in range(4)]
        ysh = {s: [ys(q[c], ey[c], s) for c in range(4)] for s in (-2, -1, 1, 2)}
        b_r = 0.5 * (q[3] + ysh[1][3]) * w0 * wyp
        b_l = 0.5 * (ysh[-1][3] + q[3]) * wym * w0
        adv = []
        for c in range(4):
            div_y = face_flux(b_r, ysh[-1][c], q[c], ysh[1][c], ysh[2][c]) - face_flux(
                b_l, ysh[-2][c], ysh[-1][c], q[c], ysh[1][c]
            )
            adv.append(q[c] - courant * (divx_ref[c * layers + k] + div_y))
        load_ym = density(ysh[-1][0], ysh[-1][1], zmid) * wym * h
        load_yp = density(ysh[1][0], ysh[1][1], zmid) * wyp * h
        cum_ym = cum_ym + load_ym
        cum_yp = cum_yp + load_yp
        grad_x = gradx_ref[k]
        grad_y = 0.5 * ((cum_yp - 0.5 * load_yp) - (cum_ym - 0.5 * load_ym))
        star0 = adv[0] * w0
        star1 = adv[1] * w0
        star2 = (adv[2] + time_step * (turning * q[3] - gravity * grad_x)) * w0
        star3 = (adv[3] + time_step * (-turning * q[2] - gravity * grad_y)) * w0
        for c, val in enumerate((star0, star1, star2, star3)):
            star_scr[c * layers + k] = val
        rs_scr[k] = density(star0, star1, zmid)
        return (cum_ym, cum_yp)

    lax.fori_loop(0, layers, explicit, (zero, zero), unroll=3)

    surface_scale = surface_gain * inv_h_ref[0]
    w_top = (0.0 < dep).astype(jnp.float32)
    for c in range(4):
        star_scr[c * layers] = star_scr[c * layers] + flux_ref[c] * w_top * surface_scale

    def forward(k, carry):
        mix_prev, r_a, r_b, s0, s1, s2, s3 = carry
        kf = k.astype(jnp.float32)
        inv_h = inv_h_ref[k]
        nxt = jnp.minimum(k + 1, layers - 1)
        stratified = (rs_scr[nxt] - rs_scr[k]) * inv_sp_ref[k]
        sig = 1.0 / (1.0 + jnp.exp(stratified * (1.0 / strat_scale)))
        w_next = (kf + 1.0 < dep).astype(jnp.float32)
        mix = (mix_back + mix_conv * sig) * w_next
        mix = jnp.where(k < layers - 1, mix, 0.0)
        low_a = -mix_prev * inv_h
        up_a = -mix * inv_h
        cen_a = 1.0 - low_a - up_a
        low_b = -mix_prev * momentum_mix * inv_h
        up_b = -mix * momentum_mix * inv_h
        floor = (kf == dep - 1.0).astype(jnp.float32)
        cen_b = 1.0 - low_b - up_b + bottom_drag * floor * inv_h
        inv_a = 1.0 / (cen_a - low_a * r_a)
        inv_b = 1.0 / (cen_b - low_b * r_b)
        r_a = up_a * inv_a
        r_b = up_b * inv_b
        r_scr[k] = r_a
        r_scr[layers + k] = r_b
        s0 = (star_scr[k] - low_a * s0) * inv_a
        s1 = (star_scr[layers + k] - low_a * s1) * inv_a
        s2 = (star_scr[2 * layers + k] - low_b * s2) * inv_b
        s3 = (star_scr[3 * layers + k] - low_b * s3) * inv_b
        star_scr[k] = s0
        star_scr[layers + k] = s1
        star_scr[2 * layers + k] = s2
        star_scr[3 * layers + k] = s3
        return (mix, r_a, r_b, s0, s1, s2, s3)

    lax.fori_loop(0, layers, forward, (zero,) * 7, unroll=3)

    def backward(i, carry):
        x0, x1, x2, x3 = carry
        k = layers - 1 - i
        r_a = r_scr[k]
        r_b = r_scr[layers + k]
        x0 = star_scr[k] - r_a * x0
        x1 = star_scr[layers + k] - r_a * x1
        x2 = star_scr[2 * layers + k] - r_b * x2
        x3 = star_scr[3 * layers + k] - r_b * x3
        o0_ref[k] = x0
        o1_ref[k] = x1
        o2_ref[k] = x2
        o3_ref[k] = x3
        return (x0, x1, x2, x3)

    lax.fori_loop(0, layers, backward, (zero,) * 4, unroll=3)


def level_tables(layers):
    offsets = np.arange(layers, dtype=np.float32) + np.float32(0.5)
    zmid = offsets / np.float32(layers)
    thickness = np.float32(0.5) + zmid
    inverse = np.float32(1.0) / thickness
    spacing = np.float32(0.5) * (thickness[1:] + thickness[:-1])
    inv_spacing = np.concatenate([np.float32(1.0) / spacing, np.ones((1,), np.float32)])
    return [jnp.asarray(t.astype(np.float32)) for t in (thickness, inverse, zmid, inv_spacing)]


def on_device(
    heat_anomaly,
    brine_anomaly,
    eastward_current,
    northward_current,
    shoreline_indicator,
    bottom_layer_index,
    boundary_fluxes,
):
    layers, rows, cols = heat_anomaly.shape
    fields = (heat_anomaly, brine_anomaly, eastward_current, northward_current)
    groups = layers // GROUP
    n_lat = lax.axis_size("lat")
    n_lon = lax.axis_size("lon")
    lat_idx = lax.axis_index("lat").astype(jnp.int32)
    is_last = (lat_idx == n_lat - 1).astype(jnp.int32).reshape(1)
    lat_info = jnp.stack([lat_idx, jnp.int32(n_lat)])

    smem = pl.BlockSpec(memory_space=pltpu.SMEM)
    vmem = pl.BlockSpec(memory_space=pltpu.VMEM)
    row_tiles = jax.ShapeDtypeStruct((layers + 1, rows, cols), jnp.float32)
    col_tiles = jax.ShapeDtypeStruct((groups + 1, rows, cols), jnp.float32)
    top, bot, fold, right, left = pl.pallas_call(
        pack_kernel,
        out_shape=(row_tiles, row_tiles, row_tiles, col_tiles, col_tiles),
        in_specs=[smem] + [vmem] * 6,
        out_specs=(vmem,) * 5,
    )(is_last, shoreline_indicator, bottom_layer_index, *fields)

    from_south = lax.ppermute(top, "lat", [(i, i + 1) for i in range(n_lat - 1)])
    from_north = lax.ppermute(bot, "lat", [(i + 1, i) for i in range(n_lat - 1)])
    from_west = lax.ppermute(right, "lon", [(i, (i + 1) % n_lon) for i in range(n_lon)])
    from_east = lax.ppermute(left, "lon", [((i + 1) % n_lon, i) for i in range(n_lon)])
    last = (n_lat - 1) * n_lon
    fold, from_west, from_east = lax.optimization_barrier((fold, from_west, from_east))
    from_fold = lax.ppermute(
        fold, ("lat", "lon"), [(last + x, last + n_lon - 1 - x) for x in range(n_lon)]
    )

    plane = jax.ShapeDtypeStruct((layers, rows, cols), jnp.float32)
    tables = level_tables(layers)
    divx, gradx = pl.pallas_call(
        xpart_kernel,
        out_shape=(jax.ShapeDtypeStruct((4 * layers, rows, cols), jnp.float32), plane),
        in_specs=[smem] * 2 + [vmem] * 8,
        out_specs=(vmem,) * 2,
    )(tables[0], tables[2], shoreline_indicator, bottom_layer_index, *fields, from_west, from_east)
    outs = pl.pallas_call(
        step_kernel,
        out_shape=(plane,) * 4,
        in_specs=[smem] * 5 + [vmem] * 12,
        out_specs=(vmem,) * 4,
        scratch_shapes=[
            pltpu.VMEM((4 * layers, rows, cols), jnp.float32),
            pltpu.VMEM((2 * layers, rows, cols), jnp.float32),
            pltpu.VMEM((layers, rows, cols), jnp.float32),
        ],
    )(
        lat_info, *tables,
        shoreline_indicator, bottom_layer_index, boundary_fluxes, *fields,
        from_south, from_north, from_fold, divx, gradx,
    )
    return tuple(outs)


def solution(mesh):
    in_specs = (
        P(None, "lat", "lon"),
        P(None, "lat", "lon"),
        P(None, "lat", "lon"),
        P(None, "lat", "lon"),
        P("lat", "lon"),
        P("lat", "lon"),
        P(None, "lat", "lon"),
    )
    out_specs = (
        P(None, "lat", "lon"),
        P(None, "lat", "lon"),
        P(None, "lat", "lon"),
        P(None, "lat", "lon"),
    )
    return jax.shard_map(
        on_device, mesh=mesh, in_specs=in_specs, out_specs=out_specs, check_vma=False
    )
```

```python
import numpy as np
import jax
import jax.numpy as jnp
from jax import lax
from jax.experimental import pallas as pl
from jax.experimental.pallas import tpu as pltpu
from jax.sharding import PartitionSpec as P

courant = 0.25
time_step = 0.2
gravity = 0.2
coriolis = 0.5
thermal = 0.6
thermal_sq = 0.1
haline = 0.8
mix_back = 5.0
mix_conv = 60.0
strat_scale = 2.0
momentum_mix = 2.0
bottom_drag = 1.0
surface_gain = 0.5

GROUP = 15


def density(warmth, saltiness, depth_column):
    return -thermal * warmth * (1.0 + thermal_sq * warmth + depth_column) + haline * saltiness


def face_flux(face_vel, before, here, after, beyond):
    return face_vel * 0.5 * (here + after) - (
        jnp.maximum(face_vel, 0.0) * (after - 2.0 * here + before)
        + jnp.minimum(face_vel, 0.0) * (beyond - 2.0 * after + here)
    ) * (1.0 / 6.0)


def rolled(x, shift, axis):
    shift %= x.shape[axis]
    return x if shift == 0 else pltpu.roll(x, shift, axis)


def pack_kernel(
    last_ref, shore_ref, bottom_ref, t_ref, s_ref, u_ref, v_ref,
    top_ref, bot_ref, fold_ref, right_ref, left_ref,
):
    layers, rows, cols = t_ref.shape
    groups = layers // GROUP
    lane = lax.broadcasted_iota(jnp.int32, (rows, cols), 1)
    row = lax.broadcasted_iota(jnp.int32, (rows, cols), 0)
    dep = (shore_ref[...] * bottom_ref[...]).astype(jnp.float32)
    zero = jnp.zeros((rows, cols), jnp.float32)

    def pack_rows(vals, first):
        out = zero
        for c, val in enumerate(vals):
            out = jnp.where((row >> 1) == c, rolled(val, 2 * c - first, 0), out)
        return out

    def group_body(g, carry):
        right = zero
        left = zero
        for j in range(GROUP):
            k = g * GROUP + j
            w = (k.astype(jnp.float32) < dep).astype(jnp.float32)
            q = [r[k] * w for r in (t_ref, s_ref, u_ref, v_ref)]
            top_ref[k] = pack_rows(q, rows - 2)
            bot_ref[k] = pack_rows(q, 0)
            for c in range(4):
                m = j * 4 + c
                slot = (lane >> 1) == m
                right = jnp.where(slot, rolled(q[c], 2 * m - (cols - 2), 1), right)
                left = jnp.where(slot, rolled(q[c], 2 * m, 1), left)
        right_ref[g] = right
        left_ref[g] = left
        return carry

    lax.fori_loop(0, groups, group_body, 0)
    top_ref[layers] = pack_rows([dep], rows - 2)
    bot_ref[layers] = pack_rows([dep], 0)
    right_ref[groups] = jnp.where(lane < 2, rolled(dep, 2, 1), zero)
    left_ref[groups] = jnp.where(lane < 2, dep, zero)

    @pl.when(last_ref[0] == 1)
    def _():
        tiles = top_ref[...].reshape((layers + 1) * rows, cols)
        tile_row = lax.broadcasted_iota(jnp.int32, tiles.shape, 0) % rows
        sign = jnp.where(tile_row < 4, 1.0, -1.0)
        swapped = jnp.where(
            (tile_row & 1) == 0, rolled(tiles, -1, 0), rolled(tiles, 1, 0)
        ) * sign
        src_lane = lax.broadcasted_iota(jnp.int32, (cols, cols), 0)
        dst_lane = lax.broadcasted_iota(jnp.int32, (cols, cols), 1)
        reverse = (src_lane + dst_lane == cols - 1).astype(jnp.float32)
        flipped = jnp.dot(
            swapped, reverse, precision=lax.Precision.HIGHEST,
            preferred_element_type=jnp.float32,
        )
        fold_ref[...] = flipped.reshape(layers + 1, rows, cols)


def xpart_kernel(
    h_ref, zmid_ref, shore_ref, bottom_ref, t_ref, s_ref, u_ref, v_ref, west_ref, east_ref,
    divx_ref, gradx_ref,
):
    layers, rows, cols = t_ref.shape
    groups = layers // GROUP
    lane = lax.broadcasted_iota(jnp.int32, (rows, cols), 1)

    def xs(v, e, s):
        if s == 1:
            return pltpu.roll(jnp.where(lane == 0, e, v), cols - 1, 1)
        if s == 2:
            return pltpu.roll(jnp.where(lane < 2, e, v), cols - 2, 1)
        if s == -1:
            return pltpu.roll(jnp.where(lane == cols - 1, e, v), 1, 1)
        return pltpu.roll(jnp.where(lane >= cols - 2, e, v), 2, 1)

    def lon_edge(tile_e, tile_w, m):
        return jnp.where(lane < 64, rolled(tile_e, -2 * m, 1), rolled(tile_w, cols - 2 - 2 * m, 1))

    dep = (shore_ref[...] * bottom_ref[...]).astype(jnp.float32)
    dep_lon = lon_edge(east_ref[groups], west_ref[groups], 0)
    dep_xm = xs(dep, dep_lon, -1)
    dep_xp = xs(dep, dep_lon, 1)
    zero = jnp.zeros((rows, cols), jnp.float32)

    def group_body(g, carry):
        tile_e = east_ref[g]
        tile_w = west_ref[g]
        for j in range(GROUP):
            cum_xm, cum_xp = carry
            k = g * GROUP + j
            kf = k.astype(jnp.float32)
            h = h_ref[k]
            zmid = zmid_ref[k]
            w0 = (kf < dep).astype(jnp.float32)
            wxm = (kf < dep_xm).astype(jnp.float32)
            wxp = (kf < dep_xp).astype(jnp.float32)
            q = [r[k] * w0 for r in (t_ref, s_ref, u_ref, v_ref)]
            ex = [lon_edge(tile_e, tile_w, j * 4 + c) for c in range(4)]
            xsh = {s: [xs(q[c], ex[c], s) for c in range(4)] for s in (-2, -1, 1, 2)}
            a_r = 0.5 * (q[2] + xsh[1][2]) * w0 * wxp
            a_l = 0.5 * (xsh[-1][2] + q[2]) * wxm * w0
            for c in range(4):
                divx_ref[c * layers + k] = face_flux(
                    a_r, xsh[-1][c], q[c], xsh[1][c], xsh[2][c]
                ) - face_flux(a_l, xsh[-2][c], xsh[-1][c], q[c], xsh[1][c])
            load_xm = density(xsh[-1][0], xsh[-1][1], zmid) * wxm * h
            load_xp = density(xsh[1][0], xsh[1][1], zmid) * wxp * h
            cum_xm = cum_xm + load_xm
            cum_xp = cum_xp + load_xp
            gradx_ref[k] = 0.5 * ((cum_xp - 0.5 * load_xp) - (cum_xm - 0.5 * load_xm))
            carry = (cum_xm, cum_xp)
        return carry

    lax.fori_loop(0, groups, group_body, (zero, zero))


def step_kernel(
    lat_ref, h_ref, inv_h_ref, zmid_ref, inv_sp_ref,
    shore_ref, bottom_ref, flux_ref, t_hbm, s_hbm, u_hbm, v_hbm,
    south_ref, north_ref, fold_ref, divx_hbm, gradx_hbm,
    o0_ref, o1_ref, o2_ref, o3_ref,
    star_scr, r_scr, rs_scr,
    t_ref, s_ref, u_ref, v_ref, divx_ref, gradx_ref, sems,
):
    layers = t_ref.shape[0]
    rows, cols = t_ref.shape[1], t_ref.shape[2]
    groups = layers // GROUP

    def chunk_copies(g):
        span = pl.ds(g * GROUP, GROUP)
        pairs = [(src.at[span], dst.at[span]) for src, dst in (
            (t_hbm, t_ref), (s_hbm, s_ref), (u_hbm, u_ref), (v_hbm, v_ref),
            (gradx_hbm, gradx_ref),
        )]
        for c in range(4):
            plane_span = pl.ds(c * layers + g * GROUP, GROUP)
            pairs.append((divx_hbm.at[plane_span], divx_ref.at[plane_span]))
        return [
            pltpu.make_async_copy(src, dst, sems.at[g, i]) for i, (src, dst) in enumerate(pairs)
        ]

    for g in range(groups):
        for copy in chunk_copies(g):
            copy.start()
    lane = lax.broadcasted_iota(jnp.int32, (rows, cols), 1)
    row = lax.broadcasted_iota(jnp.int32, (rows, cols), 0)

    def ys(v, e, s):
        if s == 1:
            return pltpu.roll(jnp.where(row == 0, e, v), rows - 1, 0)
        if s == 2:
            return pltpu.roll(jnp.where(row < 2, e, v), rows - 2, 0)
        if s == -1:
            return pltpu.roll(jnp.where(row == rows - 1, e, v), 1, 0)
        return pltpu.roll(jnp.where(row >= rows - 2, e, v), 2, 0)

    def lat_edge(tile_n, tile_s, c):
        return jnp.where(row < 4, rolled(tile_n, -2 * c, 0), rolled(tile_s, rows - 2 - 2 * c, 0))

    dep = (shore_ref[...] * bottom_ref[...]).astype(jnp.float32)
    dep_lat = lat_edge(north_ref[layers] + fold_ref[layers], south_ref[layers], 0)
    dep_ym = ys(dep, dep_lat, -1)
    dep_yp = ys(dep, dep_lat, 1)
    total_rows = rows * lat_ref[1]
    row_ids = (lat_ref[0] * rows + row).astype(jnp.float32)
    turning = coriolis * (2.0 * (row_ids + 0.5) / total_rows.astype(jnp.float32) - 1.0)
    zero = jnp.zeros((rows, cols), jnp.float32)

    def explicit(k, carry):
        cum_ym, cum_yp = carry
        kf = k.astype(jnp.float32)
        h = h_ref[k]
        zmid = zmid_ref[k]
        w0 = (kf < dep).astype(jnp.float32)
        wym = (kf < dep_ym).astype(jnp.float32)
        wyp = (kf < dep_yp).astype(jnp.float32)
        q = [r[k] * w0 for r in (t_ref, s_ref, u_ref, v_ref)]
        tile_n = north_ref[k] + fold_ref[k]
        tile_s = south_ref[k]
        ey = [lat_edge(tile_n, tile_s, c) for c in range(4)]
        ysh = {s: [ys(q[c], ey[c], s) for c in range(4)] for s in (-2, -1, 1, 2)}
        b_r = 0.5 * (q[3] + ysh[1][3]) * w0 * wyp
        b_l = 0.5 * (ysh[-1][3] + q[3]) * wym * w0
        adv = []
        for c in range(4):
            div_y = face_flux(b_r, ysh[-1][c], q[c], ysh[1][c], ysh[2][c]) - face_flux(
                b_l, ysh[-2][c], ysh[-1][c], q[c], ysh[1][c]
            )
            adv.append(q[c] - courant * (divx_ref[c * layers + k] + div_y))
        load_ym = density(ysh[-1][0], ysh[-1][1], zmid) * wym * h
        load_yp = density(ysh[1][0], ysh[1][1], zmid) * wyp * h
        cum_ym = cum_ym + load_ym
        cum_yp = cum_yp + load_yp
        grad_x = gradx_ref[k]
        grad_y = 0.5 * ((cum_yp - 0.5 * load_yp) - (cum_ym - 0.5 * load_ym))
        star0 = adv[0] * w0
        star1 = adv[1] * w0
        star2 = (adv[2] + time_step * (turning * q[3] - gravity * grad_x)) * w0
        star3 = (adv[3] + time_step * (-turning * q[2] - gravity * grad_y)) * w0
        for c, val in enumerate((star0, star1, star2, star3)):
            star_scr[c * layers + k] = val
        rs_scr[k] = density(star0, star1, zmid)
        return (cum_ym, cum_yp)

    carry = (zero, zero)
    for g in range(groups):
        for copy in chunk_copies(g):
            copy.wait()
        carry = lax.fori_loop(g * GROUP, (g + 1) * GROUP, explicit, carry, unroll=3)

    surface_scale = surface_gain * inv_h_ref[0]
    w_top = (0.0 < dep).astype(jnp.float32)
    for c in range(4):
        star_scr[c * layers] = star_scr[c * layers] + flux_ref[c] * w_top * surface_scale

    def forward(k, carry):
        mix_prev, r_a, r_b, s0, s1, s2, s3 = carry
        kf = k.astype(jnp.float32)
        inv_h = inv_h_ref[k]
        nxt = jnp.minimum(k + 1, layers - 1)
        stratified = (rs_scr[nxt] - rs_scr[k]) * inv_sp_ref[k]
        sig = 1.0 / (1.0 + jnp.exp(stratified * (1.0 / strat_scale)))
        w_next = (kf + 1.0 < dep).astype(jnp.float32)
        mix = (mix_back + mix_conv * sig) * w_next
        mix = jnp.where(k < layers - 1, mix, 0.0)
        low_a = -mix_prev * inv_h
        up_a = -mix * inv_h
        cen_a = 1.0 - low_a - up_a
        low_b = -mix_prev * momentum_mix * inv_h
        up_b = -mix * momentum_mix * inv_h
        floor = (kf == dep - 1.0).astype(jnp.float32)
        cen_b = 1.0 - low_b - up_b + bottom_drag * floor * inv_h
        inv_a = 1.0 / (cen_a - low_a * r_a)
        inv_b = 1.0 / (cen_b - low_b * r_b)
        r_a = up_a * inv_a
        r_b = up_b * inv_b
        r_scr[k] = r_a
        r_scr[layers + k] = r_b
        s0 = (star_scr[k] - low_a * s0) * inv_a
        s1 = (star_scr[layers + k] - low_a * s1) * inv_a
        s2 = (star_scr[2 * layers + k] - low_b * s2) * inv_b
        s3 = (star_scr[3 * layers + k] - low_b * s3) * inv_b
        star_scr[k] = s0
        star_scr[layers + k] = s1
        star_scr[2 * layers + k] = s2
        star_scr[3 * layers + k] = s3
        return (mix, r_a, r_b, s0, s1, s2, s3)

    lax.fori_loop(0, layers, forward, (zero,) * 7, unroll=3)

    def backward(i, carry):
        x0, x1, x2, x3 = carry
        k = layers - 1 - i
        r_a = r_scr[k]
        r_b = r_scr[layers + k]
        x0 = star_scr[k] - r_a * x0
        x1 = star_scr[layers + k] - r_a * x1
        x2 = star_scr[2 * layers + k] - r_b * x2
        x3 = star_scr[3 * layers + k] - r_b * x3
        o0_ref[k] = x0
        o1_ref[k] = x1
        o2_ref[k] = x2
        o3_ref[k] = x3
        return (x0, x1, x2, x3)

    lax.fori_loop(0, layers, backward, (zero,) * 4, unroll=3)


def level_tables(layers):
    offsets = np.arange(layers, dtype=np.float32) + np.float32(0.5)
    zmid = offsets / np.float32(layers)
    thickness = np.float32(0.5) + zmid
    inverse = np.float32(1.0) / thickness
    spacing = np.float32(0.5) * (thickness[1:] + thickness[:-1])
    inv_spacing = np.concatenate([np.float32(1.0) / spacing, np.ones((1,), np.float32)])
    return [jnp.asarray(t.astype(np.float32)) for t in (thickness, inverse, zmid, inv_spacing)]


def on_device(
    heat_anomaly,
    brine_anomaly,
    eastward_current,
    northward_current,
    shoreline_indicator,
    bottom_layer_index,
    boundary_fluxes,
):
    layers, rows, cols = heat_anomaly.shape
    fields = (heat_anomaly, brine_anomaly, eastward_current, northward_current)
    groups = layers // GROUP
    n_lat = lax.axis_size("lat")
    n_lon = lax.axis_size("lon")
    lat_idx = lax.axis_index("lat").astype(jnp.int32)
    is_last = (lat_idx == n_lat - 1).astype(jnp.int32).reshape(1)
    lat_info = jnp.stack([lat_idx, jnp.int32(n_lat)])

    smem = pl.BlockSpec(memory_space=pltpu.SMEM)
    vmem = pl.BlockSpec(memory_space=pltpu.VMEM)
    anywhere = pl.BlockSpec(memory_space=pl.ANY)
    row_tiles = jax.ShapeDtypeStruct((layers + 1, rows, cols), jnp.float32)
    col_tiles = jax.ShapeDtypeStruct((groups + 1, rows, cols), jnp.float32)
    top, bot, fold, right, left = pl.pallas_call(
        pack_kernel,
        out_shape=(row_tiles, row_tiles, row_tiles, col_tiles, col_tiles),
        in_specs=[smem] + [vmem] * 6,
        out_specs=(vmem,) * 5,
    )(is_last, shoreline_indicator, bottom_layer_index, *fields)

    from_south = lax.ppermute(top, "lat", [(i, i + 1) for i in range(n_lat - 1)])
    from_north = lax.ppermute(bot, "lat", [(i + 1, i) for i in range(n_lat - 1)])
    from_west = lax.ppermute(right, "lon", [(i, (i + 1) % n_lon) for i in range(n_lon)])
    from_east = lax.ppermute(left, "lon", [((i + 1) % n_lon, i) for i in range(n_lon)])
    last = (n_lat - 1) * n_lon
    fold, from_west, from_east = lax.optimization_barrier((fold, from_west, from_east))
    from_fold = lax.ppermute(
        fold, ("lat", "lon"), [(last + x, last + n_lon - 1 - x) for x in range(n_lon)]
    )

    plane = jax.ShapeDtypeStruct((layers, rows, cols), jnp.float32)
    tables = level_tables(layers)
    divx, gradx = pl.pallas_call(
        xpart_kernel,
        out_shape=(jax.ShapeDtypeStruct((4 * layers, rows, cols), jnp.float32), plane),
        in_specs=[smem] * 2 + [vmem] * 8,
        out_specs=(vmem,) * 2,
    )(tables[0], tables[2], shoreline_indicator, bottom_layer_index, *fields, from_west, from_east)
    outs = pl.pallas_call(
        step_kernel,
        out_shape=(plane,) * 4,
        in_specs=[smem] * 5 + [vmem] * 3 + [anywhere] * 4 + [vmem] * 3 + [anywhere] * 2,
        out_specs=(vmem,) * 4,
        scratch_shapes=[
            pltpu.VMEM((4 * layers, rows, cols), jnp.float32),
            pltpu.VMEM((2 * layers, rows, cols), jnp.float32),
            pltpu.VMEM((layers, rows, cols), jnp.float32),
        ] + [pltpu.VMEM((layers, rows, cols), jnp.float32)] * 4 + [
            pltpu.VMEM((4 * layers, rows, cols), jnp.float32),
            pltpu.VMEM((layers, rows, cols), jnp.float32),
            pltpu.SemaphoreType.DMA((groups, 9)),
        ],
    )(
        lat_info, *tables,
        shoreline_indicator, bottom_layer_index, boundary_fluxes, *fields,
        from_south, from_north, from_fold, divx, gradx,
    )
    return tuple(outs)


def solution(mesh):
    in_specs = (
        P(None, "lat", "lon"),
        P(None, "lat", "lon"),
        P(None, "lat", "lon"),
        P(None, "lat", "lon"),
        P("lat", "lon"),
        P("lat", "lon"),
        P(None, "lat", "lon"),
    )
    out_specs = (
        P(None, "lat", "lon"),
        P(None, "lat", "lon"),
        P(None, "lat", "lon"),
        P(None, "lat", "lon"),
    )
    return jax.shard_map(
        on_device, mesh=mesh, in_specs=in_specs, out_specs=out_specs, check_vma=False
    )
```

```python
import numpy as np
import jax
import jax.numpy as jnp
from jax import lax
from jax.experimental import pallas as pl
from jax.experimental.pallas import tpu as pltpu
from jax.sharding import PartitionSpec as P

courant = 0.25
time_step = 0.2
gravity = 0.2
coriolis = 0.5
thermal = 0.6
thermal_sq = 0.1
haline = 0.8
mix_back = 5.0
mix_conv = 60.0
strat_scale = 2.0
momentum_mix = 2.0
bottom_drag = 1.0
surface_gain = 0.5

GROUP = 15


def density(warmth, saltiness, depth_column):
    return -thermal * warmth * (1.0 + thermal_sq * warmth + depth_column) + haline * saltiness


def face_flux(face_vel, before, here, after, beyond):
    return face_vel * 0.5 * (here + after) - (
        jnp.maximum(face_vel, 0.0) * (after - 2.0 * here + before)
        + jnp.minimum(face_vel, 0.0) * (beyond - 2.0 * after + here)
    ) * (1.0 / 6.0)


def rolled(x, shift, axis):
    shift %= x.shape[axis]
    return x if shift == 0 else pltpu.roll(x, shift, axis)


def pack_kernel(
    last_ref, shore_ref, bottom_ref, t_ref, s_ref, u_ref, v_ref,
    top_ref, bot_ref, fold_ref, right_ref, left_ref,
):
    layers, rows, cols = t_ref.shape
    groups = layers // GROUP
    lane = lax.broadcasted_iota(jnp.int32, (rows, cols), 1)
    row = lax.broadcasted_iota(jnp.int32, (rows, cols), 0)
    dep = (shore_ref[...] * bottom_ref[...]).astype(jnp.float32)
    zero = jnp.zeros((rows, cols), jnp.float32)

    def pack_rows(vals, first):
        out = zero
        for c, val in enumerate(vals):
            out = jnp.where((row >> 1) == c, rolled(val, 2 * c - first, 0), out)
        return out

    def group_body(g, carry):
        right = zero
        left = zero
        for j in range(GROUP):
            k = g * GROUP + j
            w = (k.astype(jnp.float32) < dep).astype(jnp.float32)
            q = [r[k] * w for r in (t_ref, s_ref, u_ref, v_ref)]
            top_ref[k] = pack_rows(q, rows - 2)
            bot_ref[k] = pack_rows(q, 0)
            for c in range(4):
                m = j * 4 + c
                slot = (lane >> 1) == m
                right = jnp.where(slot, rolled(q[c], 2 * m - (cols - 2), 1), right)
                left = jnp.where(slot, rolled(q[c], 2 * m, 1), left)
        right_ref[g] = right
        left_ref[g] = left
        return carry

    lax.fori_loop(0, groups, group_body, 0)
    top_ref[layers] = pack_rows([dep], rows - 2)
    bot_ref[layers] = pack_rows([dep], 0)
    right_ref[groups] = jnp.where(lane < 2, rolled(dep, 2, 1), zero)
    left_ref[groups] = jnp.where(lane < 2, dep, zero)

    @pl.when(last_ref[0] == 1)
    def _():
        tiles = top_ref[...].reshape((layers + 1) * rows, cols)
        tile_row = lax.broadcasted_iota(jnp.int32, tiles.shape, 0) % rows
        sign = jnp.where(tile_row < 4, 1.0, -1.0)
        swapped = jnp.where(
            (tile_row & 1) == 0, rolled(tiles, -1, 0), rolled(tiles, 1, 0)
        ) * sign
        src_lane = lax.broadcasted_iota(jnp.int32, (cols, cols), 0)
        dst_lane = lax.broadcasted_iota(jnp.int32, (cols, cols), 1)
        reverse = (src_lane + dst_lane == cols - 1).astype(jnp.float32)
        flipped = jnp.dot(
            swapped, reverse, precision=lax.Precision.HIGHEST,
            preferred_element_type=jnp.float32,
        )
        fold_ref[...] = flipped.reshape(layers + 1, rows, cols)


def xpart_kernel(
    h_ref, zmid_ref, shore_ref, bottom_ref, t_ref, s_ref, u_ref, v_ref, west_ref, east_ref,
    divx_ref, gradx_ref,
):
    layers, rows, cols = t_ref.shape
    groups = layers // GROUP
    lane = lax.broadcasted_iota(jnp.int32, (rows, cols), 1)

    def xs(v, e, s):
        if s == 1:
            return pltpu.roll(jnp.where(lane == 0, e, v), cols - 1, 1)
        if s == 2:
            return pltpu.roll(jnp.where(lane < 2, e, v), cols - 2, 1)
        if s == -1:
            return pltpu.roll(jnp.where(lane == cols - 1, e, v), 1, 1)
        return pltpu.roll(jnp.where(lane >= cols - 2, e, v), 2, 1)

    def lon_edge(tile_e, tile_w, m):
        return jnp.where(lane < 64, rolled(tile_e, -2 * m, 1), rolled(tile_w, cols - 2 - 2 * m, 1))

    dep = (shore_ref[...] * bottom_ref[...]).astype(jnp.float32)
    dep_lon = lon_edge(east_ref[groups], west_ref[groups], 0)
    dep_xm = xs(dep, dep_lon, -1)
    dep_xp = xs(dep, dep_lon, 1)
    zero = jnp.zeros((rows, cols), jnp.float32)

    def group_body(g, carry):
        tile_e = east_ref[g]
        tile_w = west_ref[g]
        for j in range(GROUP):
            cum_xm, cum_xp = carry
            k = g * GROUP + j
            kf = k.astype(jnp.float32)
            h = h_ref[k]
            zmid = zmid_ref[k]
            w0 = (kf < dep).astype(jnp.float32)
            wxm = (kf < dep_xm).astype(jnp.float32)
            wxp = (kf < dep_xp).astype(jnp.float32)
            q = [r[k] * w0 for r in (t_ref, s_ref, u_ref, v_ref)]
            ex = [lon_edge(tile_e, tile_w, j * 4 + c) for c in range(4)]
            xsh = {s: [xs(q[c], ex[c], s) for c in range(4)] for s in (-2, -1, 1, 2)}
            a_r = 0.5 * (q[2] + xsh[1][2]) * w0 * wxp
            a_l = 0.5 * (xsh[-1][2] + q[2]) * wxm * w0
            for c in range(4):
                divx_ref[c * layers + k] = face_flux(
                    a_r, xsh[-1][c], q[c], xsh[1][c], xsh[2][c]
                ) - face_flux(a_l, xsh[-2][c], xsh[-1][c], q[c], xsh[1][c])
            load_xm = density(xsh[-1][0], xsh[-1][1], zmid) * wxm * h
            load_xp = density(xsh[1][0], xsh[1][1], zmid) * wxp * h
            cum_xm = cum_xm + load_xm
            cum_xp = cum_xp + load_xp
            gradx_ref[k] = 0.5 * ((cum_xp - 0.5 * load_xp) - (cum_xm - 0.5 * load_xm))
            carry = (cum_xm, cum_xp)
        return carry

    lax.fori_loop(0, groups, group_body, (zero, zero))


def step_kernel(
    lat_ref, h_ref, inv_h_ref, zmid_ref, inv_sp_ref,
    shore_ref, bottom_ref, flux_ref, t_ref, s_ref, u_ref, v_ref,
    south_ref, north_ref, fold_ref, divx_ref, gradx_ref,
    o0_ref, o1_ref, o2_ref, o3_ref,
    star_scr, r_scr, rs_scr,
):
    layers = t_ref.shape[0]
    rows, cols = t_ref.shape[1], t_ref.shape[2]
    groups = layers // GROUP
    lane = lax.broadcasted_iota(jnp.int32, (rows, cols), 1)
    row = lax.broadcasted_iota(jnp.int32, (rows, cols), 0)

    def ys(v, e, s):
        if s == 1:
            return pltpu.roll(jnp.where(row == 0, e, v), rows - 1, 0)
        if s == 2:
            return pltpu.roll(jnp.where(row < 2, e, v), rows - 2, 0)
        if s == -1:
            return pltpu.roll(jnp.where(row == rows - 1, e, v), 1, 0)
        return pltpu.roll(jnp.where(row >= rows - 2, e, v), 2, 0)

    def lat_edge(tile_n, tile_s, c):
        return jnp.where(row < 4, rolled(tile_n, -2 * c, 0), rolled(tile_s, rows - 2 - 2 * c, 0))

    dep = (shore_ref[...] * bottom_ref[...]).astype(jnp.float32)
    dep_lat = lat_edge(north_ref[layers] + fold_ref[layers], south_ref[layers], 0)
    dep_ym = ys(dep, dep_lat, -1)
    dep_yp = ys(dep, dep_lat, 1)
    total_rows = rows * lat_ref[1]
    row_ids = (lat_ref[0] * rows + row).astype(jnp.float32)
    turning = coriolis * (2.0 * (row_ids + 0.5) / total_rows.astype(jnp.float32) - 1.0)
    zero = jnp.zeros((rows, cols), jnp.float32)

    def explicit(k, carry):
        cum_ym, cum_yp = carry
        kf = k.astype(jnp.float32)
        h = h_ref[k]
        zmid = zmid_ref[k]
        w0 = (kf < dep).astype(jnp.float32)
        wym = (kf < dep_ym).astype(jnp.float32)
        wyp = (kf < dep_yp).astype(jnp.float32)
        q = [r[k] * w0 for r in (t_ref, s_ref, u_ref, v_ref)]
        tile_n = north_ref[k] + fold_ref[k]
        tile_s = south_ref[k]
        ey = [lat_edge(tile_n, tile_s, c) for c in range(4)]
        ysh = {s: [ys(q[c], ey[c], s) for c in range(4)] for s in (-2, -1, 1, 2)}
        b_r = 0.5 * (q[3] + ysh[1][3]) * w0 * wyp
        b_l = 0.5 * (ysh[-1][3] + q[3]) * wym * w0
        adv = []
        for c in range(4):
            div_y = face_flux(b_r, ysh[-1][c], q[c], ysh[1][c], ysh[2][c]) - face_flux(
                b_l, ysh[-2][c], ysh[-1][c], q[c], ysh[1][c]
            )
            adv.append(q[c] - courant * (divx_ref[c * layers + k] + div_y))
        load_ym = density(ysh[-1][0], ysh[-1][1], zmid) * wym * h
        load_yp = density(ysh[1][0], ysh[1][1], zmid) * wyp * h
        cum_ym = cum_ym + load_ym
        cum_yp = cum_yp + load_yp
        grad_x = gradx_ref[k]
        grad_y = 0.5 * ((cum_yp - 0.5 * load_yp) - (cum_ym - 0.5 * load_ym))
        star0 = adv[0] * w0
        star1 = adv[1] * w0
        star2 = (adv[2] + time_step * (turning * q[3] - gravity * grad_x)) * w0
        star3 = (adv[3] + time_step * (-turning * q[2] - gravity * grad_y)) * w0
        for c, val in enumerate((star0, star1, star2, star3)):
            star_scr[c * layers + k] = val
        rs_scr[k] = density(star0, star1, zmid)
        return (cum_ym, cum_yp)

    lag = 2
    carry_e = lax.fori_loop(0, lag, explicit, (zero, zero))

    surface_scale = surface_gain * inv_h_ref[0]
    w_top = (0.0 < dep).astype(jnp.float32)
    for c in range(4):
        star_scr[c * layers] = star_scr[c * layers] + flux_ref[c] * w_top * surface_scale

    def forward(k, carry):
        mix_prev, r_a, r_b, s0, s1, s2, s3 = carry
        kf = k.astype(jnp.float32)
        inv_h = inv_h_ref[k]
        nxt = jnp.minimum(k + 1, layers - 1)
        stratified = (rs_scr[nxt] - rs_scr[k]) * inv_sp_ref[k]
        sig = 1.0 / (1.0 + jnp.exp(stratified * (1.0 / strat_scale)))
        w_next = (kf + 1.0 < dep).astype(jnp.float32)
        mix = (mix_back + mix_conv * sig) * w_next
        mix = jnp.where(k < layers - 1, mix, 0.0)
        low_a = -mix_prev * inv_h
        up_a = -mix * inv_h
        cen_a = 1.0 - low_a - up_a
        low_b = -mix_prev * momentum_mix * inv_h
        up_b = -mix * momentum_mix * inv_h
        floor = (kf == dep - 1.0).astype(jnp.float32)
        cen_b = 1.0 - low_b - up_b + bottom_drag * floor * inv_h
        inv_a = 1.0 / (cen_a - low_a * r_a)
        inv_b = 1.0 / (cen_b - low_b * r_b)
        r_a = up_a * inv_a
        r_b = up_b * inv_b
        r_scr[k] = r_a
        r_scr[layers + k] = r_b
        s0 = (star_scr[k] - low_a * s0) * inv_a
        s1 = (star_scr[layers + k] - low_a * s1) * inv_a
        s2 = (star_scr[2 * layers + k] - low_b * s2) * inv_b
        s3 = (star_scr[3 * layers + k] - low_b * s3) * inv_b
        star_scr[k] = s0
        star_scr[layers + k] = s1
        star_scr[2 * layers + k] = s2
        star_scr[3 * layers + k] = s3
        return (mix, r_a, r_b, s0, s1, s2, s3)

    def fused(k, carry):
        carry_e, carry_f = carry
        return (explicit(k, carry_e), forward(k - lag, carry_f))

    _, carry_f = lax.fori_loop(lag, layers, fused, (carry_e, (zero,) * 7), unroll=3)
    lax.fori_loop(layers - lag, layers, forward, carry_f)

    def backward(i, carry):
        x0, x1, x2, x3 = carry
        k = layers - 1 - i
        r_a = r_scr[k]
        r_b = r_scr[layers + k]
        x0 = star_scr[k] - r_a * x0
        x1 = star_scr[layers + k] - r_a * x1
        x2 = star_scr[2 * layers + k] - r_b * x2
        x3 = star_scr[3 * layers + k] - r_b * x3
        o0_ref[k] = x0
        o1_ref[k] = x1
        o2_ref[k] = x2
        o3_ref[k] = x3
        return (x0, x1, x2, x3)

    lax.fori_loop(0, layers, backward, (zero,) * 4, unroll=3)


def level_tables(layers):
    offsets = np.arange(layers, dtype=np.float32) + np.float32(0.5)
    zmid = offsets / np.float32(layers)
    thickness = np.float32(0.5) + zmid
    inverse = np.float32(1.0) / thickness
    spacing = np.float32(0.5) * (thickness[1:] + thickness[:-1])
    inv_spacing = np.concatenate([np.float32(1.0) / spacing, np.ones((1,), np.float32)])
    return [jnp.asarray(t.astype(np.float32)) for t in (thickness, inverse, zmid, inv_spacing)]


def on_device(
    heat_anomaly,
    brine_anomaly,
    eastward_current,
    northward_current,
    shoreline_indicator,
    bottom_layer_index,
    boundary_fluxes,
):
    layers, rows, cols = heat_anomaly.shape
    fields = (heat_anomaly, brine_anomaly, eastward_current, northward_current)
    groups = layers // GROUP
    n_lat = lax.axis_size("lat")
    n_lon = lax.axis_size("lon")
    lat_idx = lax.axis_index("lat").astype(jnp.int32)
    is_last = (lat_idx == n_lat - 1).astype(jnp.int32).reshape(1)
    lat_info = jnp.stack([lat_idx, jnp.int32(n_lat)])

    smem = pl.BlockSpec(memory_space=pltpu.SMEM)
    vmem = pl.BlockSpec(memory_space=pltpu.VMEM)
    row_tiles = jax.ShapeDtypeStruct((layers + 1, rows, cols), jnp.float32)
    col_tiles = jax.ShapeDtypeStruct((groups + 1, rows, cols), jnp.float32)
    top, bot, fold, right, left = pl.pallas_call(
        pack_kernel,
        out_shape=(row_tiles, row_tiles, row_tiles, col_tiles, col_tiles),
        in_specs=[smem] + [vmem] * 6,
        out_specs=(vmem,) * 5,
    )(is_last, shoreline_indicator, bottom_layer_index, *fields)

    from_south = lax.ppermute(top, "lat", [(i, i + 1) for i in range(n_lat - 1)])
    from_north = lax.ppermute(bot, "lat", [(i + 1, i) for i in range(n_lat - 1)])
    from_west = lax.ppermute(right, "lon", [(i, (i + 1) % n_lon) for i in range(n_lon)])
    from_east = lax.ppermute(left, "lon", [((i + 1) % n_lon, i) for i in range(n_lon)])
    last = (n_lat - 1) * n_lon
    fold, from_west, from_east = lax.optimization_barrier((fold, from_west, from_east))
    from_fold = lax.ppermute(
        fold, ("lat", "lon"), [(last + x, last + n_lon - 1 - x) for x in range(n_lon)]
    )

    plane = jax.ShapeDtypeStruct((layers, rows, cols), jnp.float32)
    tables = level_tables(layers)
    divx, gradx = pl.pallas_call(
        xpart_kernel,
        out_shape=(jax.ShapeDtypeStruct((4 * layers, rows, cols), jnp.float32), plane),
        in_specs=[smem] * 2 + [vmem] * 8,
        out_specs=(vmem,) * 2,
    )(tables[0], tables[2], shoreline_indicator, bottom_layer_index, *fields, from_west, from_east)
    outs = pl.pallas_call(
        step_kernel,
        out_shape=(plane,) * 4,
        in_specs=[smem] * 5 + [vmem] * 12,
        out_specs=(vmem,) * 4,
        scratch_shapes=[
            pltpu.VMEM((4 * layers, rows, cols), jnp.float32),
            pltpu.VMEM((2 * layers, rows, cols), jnp.float32),
            pltpu.VMEM((layers, rows, cols), jnp.float32),
        ],
    )(
        lat_info, *tables,
        shoreline_indicator, bottom_layer_index, boundary_fluxes, *fields,
        from_south, from_north, from_fold, divx, gradx,
    )
    return tuple(outs)


def solution(mesh):
    in_specs = (
        P(None, "lat", "lon"),
        P(None, "lat", "lon"),
        P(None, "lat", "lon"),
        P(None, "lat", "lon"),
        P("lat", "lon"),
        P("lat", "lon"),
        P(None, "lat", "lon"),
    )
    out_specs = (
        P(None, "lat", "lon"),
        P(None, "lat", "lon"),
        P(None, "lat", "lon"),
        P(None, "lat", "lon"),
    )
    return jax.shard_map(
        on_device, mesh=mesh, in_specs=in_specs, out_specs=out_specs, check_vma=False
    )
```

```python
import numpy as np
import jax
import jax.numpy as jnp
from jax import lax
from jax.experimental import pallas as pl
from jax.experimental.pallas import tpu as pltpu
from jax.sharding import PartitionSpec as P

courant = 0.25
time_step = 0.2
gravity = 0.2
coriolis = 0.5
thermal = 0.6
thermal_sq = 0.1
haline = 0.8
mix_back = 5.0
mix_conv = 60.0
strat_scale = 2.0
momentum_mix = 2.0
bottom_drag = 1.0
surface_gain = 0.5

GROUP = 15


def density(warmth, saltiness, depth_column):
    return -thermal * warmth * (1.0 + thermal_sq * warmth + depth_column) + haline * saltiness


def face_weights(face_vel):
    return (
        0.5 * face_vel,
        jnp.maximum(face_vel, 0.0) * (1.0 / 6.0),
        jnp.minimum(face_vel, 0.0) * (1.0 / 6.0),
    )


def flux_divergence(right_w, left_w, m2, m1, q0, p1, p2):
    half_r, pos_r, neg_r = right_w
    half_l, pos_l, neg_l = left_w
    step_r = p1 - q0
    step_l = q0 - m1
    curv_0 = step_r - step_l
    curv_p = (p2 - p1) - step_r
    curv_m = step_l - (m1 - m2)
    flux_r = half_r * (q0 + p1) - (pos_r * curv_0 + neg_r * curv_p)
    flux_l = half_l * (m1 + q0) - (pos_l * curv_m + neg_l * curv_0)
    return flux_r - flux_l


def rolled(x, shift, axis):
    shift %= x.shape[axis]
    return x if shift == 0 else pltpu.roll(x, shift, axis)


def pack_kernel(
    last_ref, shore_ref, bottom_ref, t_ref, s_ref, u_ref, v_ref,
    top_ref, bot_ref, right_ref, left_ref,
):
    layers, rows, cols = t_ref.shape
    groups = layers // GROUP
    lane = lax.broadcasted_iota(jnp.int32, (rows, cols), 1)
    row = lax.broadcasted_iota(jnp.int32, (rows, cols), 0)
    dep = (shore_ref[...] * bottom_ref[...]).astype(jnp.float32)
    zero = jnp.zeros((rows, cols), jnp.float32)

    def pack_rows(vals, first):
        out = zero
        for c, val in enumerate(vals):
            out = jnp.where((row >> 1) == c, rolled(val, 2 * c - first, 0), out)
        return out

    def group_body(g, carry):
        right = zero
        left = zero
        for j in range(GROUP):
            k = g * GROUP + j
            w = (k.astype(jnp.float32) < dep).astype(jnp.float32)
            q = [r[k] * w for r in (t_ref, s_ref, u_ref, v_ref)]
            top_ref[k] = pack_rows(q, rows - 2)
            bot_ref[k] = pack_rows(q, 0)
            for c in range(4):
                m = j * 4 + c
                slot = (lane >> 1) == m
                right = jnp.where(slot, rolled(q[c], 2 * m - (cols - 2), 1), right)
                left = jnp.where(slot, rolled(q[c], 2 * m, 1), left)
        right_ref[g] = right
        left_ref[g] = left
        return carry

    lax.fori_loop(0, groups, group_body, 0)
    top_ref[layers] = pack_rows([dep], rows - 2)
    bot_ref[layers] = pack_rows([dep], 0)
    right_ref[groups] = jnp.where(lane < 2, rolled(dep, 2, 1), zero)
    left_ref[groups] = jnp.where(lane < 2, dep, zero)

    @pl.when(last_ref[0] == 1)
    def _():
        tiles = top_ref[...].reshape((layers + 1) * rows, cols)
        tile_row = lax.broadcasted_iota(jnp.int32, tiles.shape, 0) % rows
        sign = jnp.where(tile_row < 4, 1.0, -1.0)
        swapped = jnp.where(
            (tile_row & 1) == 0, rolled(tiles, -1, 0), rolled(tiles, 1, 0)
        ) * sign
        src_lane = lax.broadcasted_iota(jnp.int32, (cols, cols), 0)
        dst_lane = lax.broadcasted_iota(jnp.int32, (cols, cols), 1)
        reverse = (src_lane + dst_lane == cols - 1).astype(jnp.float32)
        flipped = jnp.dot(
            swapped, reverse, precision=lax.Precision.HIGHEST,
            preferred_element_type=jnp.float32,
        )
        top_ref[...] = flipped.reshape(layers + 1, rows, cols)


def xpart_kernel(
    h_ref, zmid_ref, shore_ref, bottom_ref, t_ref, s_ref, u_ref, v_ref, west_ref, east_ref,
    divx_ref, gradx_ref,
):
    layers, rows, cols = t_ref.shape
    groups = layers // GROUP
    lane = lax.broadcasted_iota(jnp.int32, (rows, cols), 1)

    def xs(v, e, s):
        if s == 1:
            return pltpu.roll(jnp.where(lane == 0, e, v), cols - 1, 1)
        if s == 2:
            return pltpu.roll(jnp.where(lane < 2, e, v), cols - 2, 1)
        if s == -1:
            return pltpu.roll(jnp.where(lane == cols - 1, e, v), 1, 1)
        return pltpu.roll(jnp.where(lane >= cols - 2, e, v), 2, 1)

    def lon_edge(tile_e, tile_w, m):
        return jnp.where(lane < 64, rolled(tile_e, -2 * m, 1), rolled(tile_w, cols - 2 - 2 * m, 1))

    dep = (shore_ref[...] * bottom_ref[...]).astype(jnp.float32)
    dep_lon = lon_edge(east_ref[groups], west_ref[groups], 0)
    dep_xm = xs(dep, dep_lon, -1)
    dep_xp = xs(dep, dep_lon, 1)
    zero = jnp.zeros((rows, cols), jnp.float32)

    def group_body(g, carry):
        tile_e = east_ref[g]
        tile_w = west_ref[g]
        for j in range(GROUP):
            cum_xm, cum_xp = carry
            k = g * GROUP + j
            kf = k.astype(jnp.float32)
            h = h_ref[k]
            zmid = zmid_ref[k]
            w0 = (kf < dep).astype(jnp.float32)
            wxm = (kf < dep_xm).astype(jnp.float32)
            wxp = (kf < dep_xp).astype(jnp.float32)
            q = [r[k] * w0 for r in (t_ref, s_ref, u_ref, v_ref)]
            ex = [lon_edge(tile_e, tile_w, j * 4 + c) for c in range(4)]
            xsh = {s: [xs(q[c], ex[c], s) for c in range(4)] for s in (-2, -1, 1, 2)}
            a_r = 0.5 * (q[2] + xsh[1][2]) * w0 * wxp
            a_l = 0.5 * (xsh[-1][2] + q[2]) * wxm * w0
            w_r = face_weights(a_r)
            w_l = face_weights(a_l)
            for c in range(4):
                divx_ref[c * layers + k] = q[c] - courant * flux_divergence(
                    w_r, w_l, xsh[-2][c], xsh[-1][c], q[c], xsh[1][c], xsh[2][c]
                )
            load_xm = density(xsh[-1][0], xsh[-1][1], zmid) * wxm * h
            load_xp = density(xsh[1][0], xsh[1][1], zmid) * wxp * h
            cum_xm = cum_xm + load_xm
            cum_xp = cum_xp + load_xp
            gradx_ref[k] = 0.5 * ((cum_xp - 0.5 * load_xp) - (cum_xm - 0.5 * load_xm))
            carry = (cum_xm, cum_xp)
        return carry

    lax.fori_loop(0, groups, group_body, (zero, zero))


def step_kernel(
    lat_ref, h_ref, inv_h_ref, zmid_ref, inv_sp_ref,
    shore_ref, bottom_ref, flux_ref, t_ref, s_ref, u_ref, v_ref,
    south_ref, north_ref, fold_ref, divx_ref, gradx_ref,
    o0_ref, o1_ref, o2_ref, o3_ref,
    star_scr, r_scr, rs_scr,
):
    layers = t_ref.shape[0]
    rows, cols = t_ref.shape[1], t_ref.shape[2]
    groups = layers // GROUP
    lane = lax.broadcasted_iota(jnp.int32, (rows, cols), 1)
    row = lax.broadcasted_iota(jnp.int32, (rows, cols), 0)

    def ys(v, e, s):
        if s == 1:
            return pltpu.roll(jnp.where(row == 0, e, v), rows - 1, 0)
        if s == 2:
            return pltpu.roll(jnp.where(row < 2, e, v), rows - 2, 0)
        if s == -1:
            return pltpu.roll(jnp.where(row == rows - 1, e, v), 1, 0)
        return pltpu.roll(jnp.where(row >= rows - 2, e, v), 2, 0)

    def lat_edge(tile_n, tile_s, c):
        return jnp.where(row < 4, rolled(tile_n, -2 * c, 0), rolled(tile_s, rows - 2 - 2 * c, 0))

    dep = (shore_ref[...] * bottom_ref[...]).astype(jnp.float32)
    dep_lat = lat_edge(north_ref[layers] + fold_ref[layers], south_ref[layers], 0)
    dep_ym = ys(dep, dep_lat, -1)
    dep_yp = ys(dep, dep_lat, 1)
    total_rows = rows * lat_ref[1]
    row_ids = (lat_ref[0] * rows + row).astype(jnp.float32)
    turning = coriolis * (2.0 * (row_ids + 0.5) / total_rows.astype(jnp.float32) - 1.0)
    zero = jnp.zeros((rows, cols), jnp.float32)

    def explicit(k, carry):
        cum_ym, cum_yp = carry
        kf = k.astype(jnp.float32)
        h = h_ref[k]
        zmid = zmid_ref[k]
        w0 = (kf < dep).astype(jnp.float32)
        wym = (kf < dep_ym).astype(jnp.float32)
        wyp = (kf < dep_yp).astype(jnp.float32)
        q = [r[k] * w0 for r in (t_ref, s_ref, u_ref, v_ref)]
        tile_n = north_ref[k] + fold_ref[k]
        tile_s = south_ref[k]
        ey = [lat_edge(tile_n, tile_s, c) for c in range(4)]
        ysh = {s: [ys(q[c], ey[c], s) for c in range(4)] for s in (-2, -1, 1, 2)}
        b_r = 0.5 * (q[3] + ysh[1][3]) * w0 * wyp
        b_l = 0.5 * (ysh[-1][3] + q[3]) * wym * w0
        w_r = face_weights(b_r)
        w_l = face_weights(b_l)
        adv = []
        for c in range(4):
            div_y = flux_divergence(w_r, w_l, ysh[-2][c], ysh[-1][c], q[c], ysh[1][c], ysh[2][c])
            adv.append(divx_ref[c * layers + k] - courant * div_y)
        load_ym = density(ysh[-1][0], ysh[-1][1], zmid) * wym * h
        load_yp = density(ysh[1][0], ysh[1][1], zmid) * wyp * h
        cum_ym = cum_ym + load_ym
        cum_yp = cum_yp + load_yp
        grad_x = gradx_ref[k]
        grad_y = 0.5 * ((cum_yp - 0.5 * load_yp) - (cum_ym - 0.5 * load_ym))
        star0 = adv[0] * w0
        star1 = adv[1] * w0
        star2 = (adv[2] + time_step * (turning * q[3] - gravity * grad_x)) * w0
        star3 = (adv[3] + time_step * (-turning * q[2] - gravity * grad_y)) * w0
        for c, val in enumerate((star0, star1, star2, star3)):
            star_scr[c * layers + k] = val
        rs_scr[k] = density(star0, star1, zmid)
        return (cum_ym, cum_yp)

    lag = 2
    carry_e = lax.fori_loop(0, lag, explicit, (zero, zero))

    surface_scale = surface_gain * inv_h_ref[0]
    w_top = (0.0 < dep).astype(jnp.float32)
    for c in range(4):
        star_scr[c * layers] = star_scr[c * layers] + flux_ref[c] * w_top * surface_scale

    def forward(k, carry):
        mix_prev, r_a, r_b, s0, s1, s2, s3 = carry
        kf = k.astype(jnp.float32)
        inv_h = inv_h_ref[k]
        nxt = jnp.minimum(k + 1, layers - 1)
        stratified = (rs_scr[nxt] - rs_scr[k]) * inv_sp_ref[k]
        sig = 1.0 / (1.0 + jnp.exp(stratified * (1.0 / strat_scale)))
        w_next = (kf + 1.0 < dep).astype(jnp.float32)
        mix = (mix_back + mix_conv * sig) * w_next
        mix = jnp.where(k < layers - 1, mix, 0.0)
        low_a = -mix_prev * inv_h
        up_a = -mix * inv_h
        cen_a = 1.0 - low_a - up_a
        low_b = -mix_prev * momentum_mix * inv_h
        up_b = -mix * momentum_mix * inv_h
        floor = (kf == dep - 1.0).astype(jnp.float32)
        cen_b = 1.0 - low_b - up_b + bottom_drag * floor * inv_h
        inv_a = 1.0 / (cen_a - low_a * r_a)
        inv_b = 1.0 / (cen_b - low_b * r_b)
        r_a = up_a * inv_a
        r_b = up_b * inv_b
        r_scr[k] = r_a
        r_scr[layers + k] = r_b
        s0 = (star_scr[k] - low_a * s0) * inv_a
        s1 = (star_scr[layers + k] - low_a * s1) * inv_a
        s2 = (star_scr[2 * layers + k] - low_b * s2) * inv_b
        s3 = (star_scr[3 * layers + k] - low_b * s3) * inv_b
        star_scr[k] = s0
        star_scr[layers + k] = s1
        star_scr[2 * layers + k] = s2
        star_scr[3 * layers + k] = s3
        return (mix, r_a, r_b, s0, s1, s2, s3)

    def fused(k, carry):
        carry_e, carry_f = carry
        return (explicit(k, carry_e), forward(k - lag, carry_f))

    _, carry_f = lax.fori_loop(lag, layers, fused, (carry_e, (zero,) * 7), unroll=3)
    lax.fori_loop(layers - lag, layers, forward, carry_f)

    def backward(i, carry):
        x0, x1, x2, x3 = carry
        k = layers - 1 - i
        r_a = r_scr[k]
        r_b = r_scr[layers + k]
        x0 = star_scr[k] - r_a * x0
        x1 = star_scr[layers + k] - r_a * x1
        x2 = star_scr[2 * layers + k] - r_b * x2
        x3 = star_scr[3 * layers + k] - r_b * x3
        o0_ref[k] = x0
        o1_ref[k] = x1
        o2_ref[k] = x2
        o3_ref[k] = x3
        return (x0, x1, x2, x3)

    lax.fori_loop(0, layers, backward, (zero,) * 4, unroll=3)


def level_tables(layers):
    offsets = np.arange(layers, dtype=np.float32) + np.float32(0.5)
    zmid = offsets / np.float32(layers)
    thickness = np.float32(0.5) + zmid
    inverse = np.float32(1.0) / thickness
    spacing = np.float32(0.5) * (thickness[1:] + thickness[:-1])
    inv_spacing = np.concatenate([np.float32(1.0) / spacing, np.ones((1,), np.float32)])
    return [jnp.asarray(t.astype(np.float32)) for t in (thickness, inverse, zmid, inv_spacing)]


def on_device(
    heat_anomaly,
    brine_anomaly,
    eastward_current,
    northward_current,
    shoreline_indicator,
    bottom_layer_index,
    boundary_fluxes,
):
    layers, rows, cols = heat_anomaly.shape
    fields = (heat_anomaly, brine_anomaly, eastward_current, northward_current)
    groups = layers // GROUP
    n_lat = lax.axis_size("lat")
    n_lon = lax.axis_size("lon")
    lat_idx = lax.axis_index("lat").astype(jnp.int32)
    is_last = (lat_idx == n_lat - 1).astype(jnp.int32).reshape(1)
    lat_info = jnp.stack([lat_idx, jnp.int32(n_lat)])

    smem = pl.BlockSpec(memory_space=pltpu.SMEM)
    vmem = pl.BlockSpec(memory_space=pltpu.VMEM)
    row_tiles = jax.ShapeDtypeStruct((layers + 1, rows, cols), jnp.float32)
    col_tiles = jax.ShapeDtypeStruct((groups + 1, rows, cols), jnp.float32)
    top, bot, right, left = pl.pallas_call(
        pack_kernel,
        out_shape=(row_tiles, row_tiles, col_tiles, col_tiles),
        in_specs=[smem] + [vmem] * 6,
        out_specs=(vmem,) * 4,
    )(is_last, shoreline_indicator, bottom_layer_index, *fields)

    from_south = lax.ppermute(top, "lat", [(i, i + 1) for i in range(n_lat - 1)])
    from_north = lax.ppermute(bot, "lat", [(i + 1, i) for i in range(n_lat - 1)])
    from_west = lax.ppermute(right, "lon", [(i, (i + 1) % n_lon) for i in range(n_lon)])
    from_east = lax.ppermute(left, "lon", [((i + 1) % n_lon, i) for i in range(n_lon)])
    last = (n_lat - 1) * n_lon
    fold, from_west, from_east = lax.optimization_barrier((top, from_west, from_east))
    from_fold = lax.ppermute(
        fold, ("lat", "lon"), [(last + x, last + n_lon - 1 - x) for x in range(n_lon)]
    )

    plane = jax.ShapeDtypeStruct((layers, rows, cols), jnp.float32)
    tables = level_tables(layers)
    divx, gradx = pl.pallas_call(
        xpart_kernel,
        out_shape=(jax.ShapeDtypeStruct((4 * layers, rows, cols), jnp.float32), plane),
        in_specs=[smem] * 2 + [vmem] * 8,
        out_specs=(vmem,) * 2,
    )(tables[0], tables[2], shoreline_indicator, bottom_layer_index, *fields, from_west, from_east)
    outs = pl.pallas_call(
        step_kernel,
        out_shape=(plane,) * 4,
        in_specs=[smem] * 5 + [vmem] * 12,
        out_specs=(vmem,) * 4,
        scratch_shapes=[
            pltpu.VMEM((4 * layers, rows, cols), jnp.float32),
            pltpu.VMEM((2 * layers, rows, cols), jnp.float32),
            pltpu.VMEM((layers, rows, cols), jnp.float32),
        ],
    )(
        lat_info, *tables,
        shoreline_indicator, bottom_layer_index, boundary_fluxes, *fields,
        from_south, from_north, from_fold, divx, gradx,
    )
    return tuple(outs)


def solution(mesh):
    in_specs = (
        P(None, "lat", "lon"),
        P(None, "lat", "lon"),
        P(None, "lat", "lon"),
        P(None, "lat", "lon"),
        P("lat", "lon"),
        P("lat", "lon"),
        P(None, "lat", "lon"),
    )
    out_specs = (
        P(None, "lat", "lon"),
        P(None, "lat", "lon"),
        P(None, "lat", "lon"),
        P(None, "lat", "lon"),
    )
    return jax.shard_map(
        on_device, mesh=mesh, in_specs=in_specs, out_specs=out_specs, check_vma=False
    )
```

```python
import numpy as np
import jax
import jax.numpy as jnp
from jax import lax
from jax.experimental import pallas as pl
from jax.experimental.pallas import tpu as pltpu
from jax.sharding import PartitionSpec as P

courant = 0.25
time_step = 0.2
gravity = 0.2
coriolis = 0.5
thermal = 0.6
thermal_sq = 0.1
haline = 0.8
mix_back = 5.0
mix_conv = 60.0
strat_scale = 2.0
momentum_mix = 2.0
bottom_drag = 1.0
surface_gain = 0.5

GROUP = 15


def density(warmth, saltiness, depth_column):
    return -thermal * warmth * (1.0 + thermal_sq * warmth + depth_column) + haline * saltiness


def face_weights(face_vel):
    return (
        0.5 * face_vel,
        jnp.maximum(face_vel, 0.0) * (1.0 / 6.0),
        jnp.minimum(face_vel, 0.0) * (1.0 / 6.0),
    )


def flux_divergence(right_w, left_w, m2, m1, q0, p1, p2):
    half_r, pos_r, neg_r = right_w
    half_l, pos_l, neg_l = left_w
    step_r = p1 - q0
    step_l = q0 - m1
    curv_0 = step_r - step_l
    curv_p = (p2 - p1) - step_r
    curv_m = step_l - (m1 - m2)
    flux_r = half_r * (q0 + p1) - (pos_r * curv_0 + neg_r * curv_p)
    flux_l = half_l * (m1 + q0) - (pos_l * curv_m + neg_l * curv_0)
    return flux_r - flux_l


def rolled(x, shift, axis):
    shift %= x.shape[axis]
    return x if shift == 0 else pltpu.roll(x, shift, axis)


def pack_kernel(
    last_ref, shore_ref, bottom_ref, t_ref, s_ref, u_ref, v_ref,
    top_ref, bot_ref, right_ref, left_ref,
):
    layers, rows, cols = t_ref.shape
    groups = layers // GROUP
    lane = lax.broadcasted_iota(jnp.int32, (rows, cols), 1)
    row = lax.broadcasted_iota(jnp.int32, (rows, cols), 0)
    dep = (shore_ref[...] * bottom_ref[...]).astype(jnp.float32)
    zero = jnp.zeros((rows, cols), jnp.float32)

    def pack_rows(vals, first):
        out = zero
        for c, val in enumerate(vals):
            out = jnp.where((row >> 1) == c, rolled(val, 2 * c - first, 0), out)
        return out

    def group_body(g, carry):
        right = zero
        left = zero
        for j in range(GROUP):
            k = g * GROUP + j
            w = (k.astype(jnp.float32) < dep).astype(jnp.float32)
            q = [r[k] * w for r in (t_ref, s_ref, u_ref, v_ref)]
            top_ref[k] = pack_rows(q, rows - 2)
            bot_ref[k] = pack_rows(q, 0)
            for c in range(4):
                m = j * 4 + c
                slot = (lane >> 1) == m
                right = jnp.where(slot, rolled(q[c], 2 * m - (cols - 2), 1), right)
                left = jnp.where(slot, rolled(q[c], 2 * m, 1), left)
        right_ref[g] = right
        left_ref[g] = left
        return carry

    lax.fori_loop(0, groups, group_body, 0)
    top_ref[layers] = pack_rows([dep], rows - 2)
    bot_ref[layers] = pack_rows([dep], 0)
    right_ref[groups] = jnp.where(lane < 2, rolled(dep, 2, 1), zero)
    left_ref[groups] = jnp.where(lane < 2, dep, zero)

    @pl.when(last_ref[0] == 1)
    def _():
        tiles = top_ref[...].reshape((layers + 1) * rows, cols)
        tile_row = lax.broadcasted_iota(jnp.int32, tiles.shape, 0) % rows
        sign = jnp.where(tile_row < 4, 1.0, -1.0)
        swapped = jnp.where(
            (tile_row & 1) == 0, rolled(tiles, -1, 0), rolled(tiles, 1, 0)
        ) * sign
        src_lane = lax.broadcasted_iota(jnp.int32, (cols, cols), 0)
        dst_lane = lax.broadcasted_iota(jnp.int32, (cols, cols), 1)
        reverse = (src_lane + dst_lane == cols - 1).astype(jnp.float32)
        flipped = jnp.dot(
            swapped, reverse, precision=lax.Precision.HIGHEST,
            preferred_element_type=jnp.float32,
        )
        top_ref[...] = flipped.reshape(layers + 1, rows, cols)


def xpart_kernel(
    lat_ref, h_ref, zmid_ref, shore_ref, bottom_ref, t_ref, s_ref, u_ref, v_ref,
    west_ref, east_ref, divx_ref,
):
    layers, rows, cols = t_ref.shape
    groups = layers // GROUP
    lane = lax.broadcasted_iota(jnp.int32, (rows, cols), 1)
    row = lax.broadcasted_iota(jnp.int32, (rows, cols), 0)
    total_rows = rows * lat_ref[1]
    row_ids = (lat_ref[0] * rows + row).astype(jnp.float32)
    turning = coriolis * (2.0 * (row_ids + 0.5) / total_rows.astype(jnp.float32) - 1.0)

    def xs(v, e, s):
        if s == 1:
            return pltpu.roll(jnp.where(lane == 0, e, v), cols - 1, 1)
        if s == 2:
            return pltpu.roll(jnp.where(lane < 2, e, v), cols - 2, 1)
        if s == -1:
            return pltpu.roll(jnp.where(lane == cols - 1, e, v), 1, 1)
        return pltpu.roll(jnp.where(lane >= cols - 2, e, v), 2, 1)

    def lon_edge(tile_e, tile_w, m):
        return jnp.where(lane < 64, rolled(tile_e, -2 * m, 1), rolled(tile_w, cols - 2 - 2 * m, 1))

    dep = (shore_ref[...] * bottom_ref[...]).astype(jnp.float32)
    dep_lon = lon_edge(east_ref[groups], west_ref[groups], 0)
    dep_xm = xs(dep, dep_lon, -1)
    dep_xp = xs(dep, dep_lon, 1)
    zero = jnp.zeros((rows, cols), jnp.float32)

    def group_body(g, carry):
        tile_e = east_ref[g]
        tile_w = west_ref[g]
        for j in range(GROUP):
            cum_xm, cum_xp = carry
            k = g * GROUP + j
            kf = k.astype(jnp.float32)
            h = h_ref[k]
            zmid = zmid_ref[k]
            w0 = (kf < dep).astype(jnp.float32)
            wxm = (kf < dep_xm).astype(jnp.float32)
            wxp = (kf < dep_xp).astype(jnp.float32)
            q = [r[k] * w0 for r in (t_ref, s_ref, u_ref, v_ref)]
            ex = [lon_edge(tile_e, tile_w, j * 4 + c) for c in range(4)]
            xsh = {s: [xs(q[c], ex[c], s) for c in range(4)] for s in (-2, -1, 1, 2)}
            a_r = 0.5 * (q[2] + xsh[1][2]) * w0 * wxp
            a_l = 0.5 * (xsh[-1][2] + q[2]) * wxm * w0
            w_r = face_weights(a_r)
            w_l = face_weights(a_l)
            part = [
                q[c] - courant * flux_divergence(
                    w_r, w_l, xsh[-2][c], xsh[-1][c], q[c], xsh[1][c], xsh[2][c]
                )
                for c in range(4)
            ]
            load_xm = density(xsh[-1][0], xsh[-1][1], zmid) * wxm * h
            load_xp = density(xsh[1][0], xsh[1][1], zmid) * wxp * h
            cum_xm = cum_xm + load_xm
            cum_xp = cum_xp + load_xp
            grad_x = 0.5 * ((cum_xp - 0.5 * load_xp) - (cum_xm - 0.5 * load_xm))
            part[2] = part[2] + time_step * (turning * q[3] - gravity * grad_x)
            part[3] = part[3] + time_step * (-turning * q[2])
            for c in range(4):
                divx_ref[c * layers + k] = part[c]
            carry = (cum_xm, cum_xp)
        return carry

    lax.fori_loop(0, groups, group_body, (zero, zero))


def step_kernel(
    lat_ref, h_ref, inv_h_ref, zmid_ref, inv_sp_ref,
    shore_ref, bottom_ref, flux_ref, t_ref, s_ref, u_ref, v_ref,
    south_ref, north_ref, fold_ref, divx_ref,
    o0_ref, o1_ref, o2_ref, o3_ref,
    star_scr, r_scr, rs_scr,
):
    layers = t_ref.shape[0]
    rows, cols = t_ref.shape[1], t_ref.shape[2]
    groups = layers // GROUP
    lane = lax.broadcasted_iota(jnp.int32, (rows, cols), 1)
    row = lax.broadcasted_iota(jnp.int32, (rows, cols), 0)

    def ys(v, e, s):
        if s == 1:
            return pltpu.roll(jnp.where(row == 0, e, v), rows - 1, 0)
        if s == 2:
            return pltpu.roll(jnp.where(row < 2, e, v), rows - 2, 0)
        if s == -1:
            return pltpu.roll(jnp.where(row == rows - 1, e, v), 1, 0)
        return pltpu.roll(jnp.where(row >= rows - 2, e, v), 2, 0)

    def lat_edge(tile_n, tile_s, c):
        return jnp.where(row < 4, rolled(tile_n, -2 * c, 0), rolled(tile_s, rows - 2 - 2 * c, 0))

    dep = (shore_ref[...] * bottom_ref[...]).astype(jnp.float32)
    dep_lat = lat_edge(north_ref[layers] + fold_ref[layers], south_ref[layers], 0)
    dep_ym = ys(dep, dep_lat, -1)
    dep_yp = ys(dep, dep_lat, 1)
    zero = jnp.zeros((rows, cols), jnp.float32)

    def explicit(k, carry):
        cum_ym, cum_yp = carry
        kf = k.astype(jnp.float32)
        h = h_ref[k]
        zmid = zmid_ref[k]
        w0 = (kf < dep).astype(jnp.float32)
        wym = (kf < dep_ym).astype(jnp.float32)
        wyp = (kf < dep_yp).astype(jnp.float32)
        q = [r[k] * w0 for r in (t_ref, s_ref, u_ref, v_ref)]
        tile_n = north_ref[k] + fold_ref[k]
        tile_s = south_ref[k]
        ey = [lat_edge(tile_n, tile_s, c) for c in range(4)]
        ysh = {s: [ys(q[c], ey[c], s) for c in range(4)] for s in (-2, -1, 1, 2)}
        b_r = 0.5 * (q[3] + ysh[1][3]) * w0 * wyp
        b_l = 0.5 * (ysh[-1][3] + q[3]) * wym * w0
        w_r = face_weights(b_r)
        w_l = face_weights(b_l)
        adv = []
        for c in range(4):
            div_y = flux_divergence(w_r, w_l, ysh[-2][c], ysh[-1][c], q[c], ysh[1][c], ysh[2][c])
            adv.append(divx_ref[c * layers + k] - courant * div_y)
        load_ym = density(ysh[-1][0], ysh[-1][1], zmid) * wym * h
        load_yp = density(ysh[1][0], ysh[1][1], zmid) * wyp * h
        cum_ym = cum_ym + load_ym
        cum_yp = cum_yp + load_yp
        grad_y = 0.5 * ((cum_yp - 0.5 * load_yp) - (cum_ym - 0.5 * load_ym))
        star0 = adv[0] * w0
        star1 = adv[1] * w0
        star2 = adv[2] * w0
        star3 = (adv[3] - time_step * gravity * grad_y) * w0
        for c, val in enumerate((star0, star1, star2, star3)):
            star_scr[c * layers + k] = val
        rs_scr[k] = density(star0, star1, zmid)
        return (cum_ym, cum_yp)

    lag = 2
    carry_e = lax.fori_loop(0, lag, explicit, (zero, zero))

    surface_scale = surface_gain * inv_h_ref[0]
    w_top = (0.0 < dep).astype(jnp.float32)
    for c in range(4):
        star_scr[c * layers] = star_scr[c * layers] + flux_ref[c] * w_top * surface_scale

    def forward(k, carry):
        mix_prev, r_a, r_b, s0, s1, s2, s3 = carry
        kf = k.astype(jnp.float32)
        inv_h = inv_h_ref[k]
        nxt = jnp.minimum(k + 1, layers - 1)
        stratified = (rs_scr[nxt] - rs_scr[k]) * inv_sp_ref[k]
        sig = 1.0 / (1.0 + jnp.exp(stratified * (1.0 / strat_scale)))
        w_next = (kf + 1.0 < dep).astype(jnp.float32)
        mix = (mix_back + mix_conv * sig) * w_next
        mix = jnp.where(k < layers - 1, mix, 0.0)
        low_a = -mix_prev * inv_h
        up_a = -mix * inv_h
        cen_a = 1.0 - low_a - up_a
        low_b = -mix_prev * momentum_mix * inv_h
        up_b = -mix * momentum_mix * inv_h
        floor = (kf == dep - 1.0).astype(jnp.float32)
        cen_b = 1.0 - low_b - up_b + bottom_drag * floor * inv_h
        inv_a = 1.0 / (cen_a - low_a * r_a)
        inv_b = 1.0 / (cen_b - low_b * r_b)
        r_a = up_a * inv_a
        r_b = up_b * inv_b
        r_scr[k] = r_a
        r_scr[layers + k] = r_b
        s0 = (star_scr[k] - low_a * s0) * inv_a
        s1 = (star_scr[layers + k] - low_a * s1) * inv_a
        s2 = (star_scr[2 * layers + k] - low_b * s2) * inv_b
        s3 = (star_scr[3 * layers + k] - low_b * s3) * inv_b
        star_scr[k] = s0
        star_scr[layers + k] = s1
        star_scr[2 * layers + k] = s2
        star_scr[3 * layers + k] = s3
        return (mix, r_a, r_b, s0, s1, s2, s3)

    def fused(k, carry):
        carry_e, carry_f = carry
        return (explicit(k, carry_e), forward(k - lag, carry_f))

    _, carry_f = lax.fori_loop(lag, layers, fused, (carry_e, (zero,) * 7), unroll=3)
    lax.fori_loop(layers - lag, layers, forward, carry_f)

    def backward(i, carry):
        x0, x1, x2, x3 = carry
        k = layers - 1 - i
        r_a = r_scr[k]
        r_b = r_scr[layers + k]
        x0 = star_scr[k] - r_a * x0
        x1 = star_scr[layers + k] - r_a * x1
        x2 = star_scr[2 * layers + k] - r_b * x2
        x3 = star_scr[3 * layers + k] - r_b * x3
        o0_ref[k] = x0
        o1_ref[k] = x1
        o2_ref[k] = x2
        o3_ref[k] = x3
        return (x0, x1, x2, x3)

    lax.fori_loop(0, layers, backward, (zero,) * 4, unroll=3)


def level_tables(layers):
    offsets = np.arange(layers, dtype=np.float32) + np.float32(0.5)
    zmid = offsets / np.float32(layers)
    thickness = np.float32(0.5) + zmid
    inverse = np.float32(1.0) / thickness
    spacing = np.float32(0.5) * (thickness[1:] + thickness[:-1])
    inv_spacing = np.concatenate([np.float32(1.0) / spacing, np.ones((1,), np.float32)])
    return [jnp.asarray(t.astype(np.float32)) for t in (thickness, inverse, zmid, inv_spacing)]


def on_device(
    heat_anomaly,
    brine_anomaly,
    eastward_current,
    northward_current,
    shoreline_indicator,
    bottom_layer_index,
    boundary_fluxes,
):
    layers, rows, cols = heat_anomaly.shape
    fields = (heat_anomaly, brine_anomaly, eastward_current, northward_current)
    groups = layers // GROUP
    n_lat = lax.axis_size("lat")
    n_lon = lax.axis_size("lon")
    lat_idx = lax.axis_index("lat").astype(jnp.int32)
    is_last = (lat_idx == n_lat - 1).astype(jnp.int32).reshape(1)
    lat_info = jnp.stack([lat_idx, jnp.int32(n_lat)])

    smem = pl.BlockSpec(memory_space=pltpu.SMEM)
    vmem = pl.BlockSpec(memory_space=pltpu.VMEM)
    row_tiles = jax.ShapeDtypeStruct((layers + 1, rows, cols), jnp.float32)
    col_tiles = jax.ShapeDtypeStruct((groups + 1, rows, cols), jnp.float32)
    top, bot, right, left = pl.pallas_call(
        pack_kernel,
        out_shape=(row_tiles, row_tiles, col_tiles, col_tiles),
        in_specs=[smem] + [vmem] * 6,
        out_specs=(vmem,) * 4,
    )(is_last, shoreline_indicator, bottom_layer_index, *fields)

    from_south = lax.ppermute(top, "lat", [(i, i + 1) for i in range(n_lat - 1)])
    from_north = lax.ppermute(bot, "lat", [(i + 1, i) for i in range(n_lat - 1)])
    from_west = lax.ppermute(right, "lon", [(i, (i + 1) % n_lon) for i in range(n_lon)])
    from_east = lax.ppermute(left, "lon", [((i + 1) % n_lon, i) for i in range(n_lon)])
    last = (n_lat - 1) * n_lon
    fold, from_west, from_east = lax.optimization_barrier((top, from_west, from_east))
    from_fold = lax.ppermute(
        fold, ("lat", "lon"), [(last + x, last + n_lon - 1 - x) for x in range(n_lon)]
    )

    plane = jax.ShapeDtypeStruct((layers, rows, cols), jnp.float32)
    tables = level_tables(layers)
    divx = pl.pallas_call(
        xpart_kernel,
        out_shape=jax.ShapeDtypeStruct((4 * layers, rows, cols), jnp.float32),
        in_specs=[smem] * 3 + [vmem] * 8,
        out_specs=vmem,
    )(lat_info, tables[0], tables[2], shoreline_indicator, bottom_layer_index, *fields,
      from_west, from_east)
    outs = pl.pallas_call(
        step_kernel,
        out_shape=(plane,) * 4,
        in_specs=[smem] * 5 + [vmem] * 11,
        out_specs=(vmem,) * 4,
        scratch_shapes=[
            pltpu.VMEM((4 * layers, rows, cols), jnp.float32),
            pltpu.VMEM((2 * layers, rows, cols), jnp.float32),
            pltpu.VMEM((layers, rows, cols), jnp.float32),
        ],
    )(
        lat_info, *tables,
        shoreline_indicator, bottom_layer_index, boundary_fluxes, *fields,
        from_south, from_north, from_fold, divx,
    )
    return tuple(outs)


def solution(mesh):
    in_specs = (
        P(None, "lat", "lon"),
        P(None, "lat", "lon"),
        P(None, "lat", "lon"),
        P(None, "lat", "lon"),
        P("lat", "lon"),
        P("lat", "lon"),
        P(None, "lat", "lon"),
    )
    out_specs = (
        P(None, "lat", "lon"),
        P(None, "lat", "lon"),
        P(None, "lat", "lon"),
        P(None, "lat", "lon"),
    )
    return jax.shard_map(
        on_device, mesh=mesh, in_specs=in_specs, out_specs=out_specs, check_vma=False
    )
```

```python
import numpy as np
import jax
import jax.numpy as jnp
from jax import lax
from jax.experimental import pallas as pl
from jax.experimental.pallas import tpu as pltpu
from jax.sharding import PartitionSpec as P

courant = 0.25
time_step = 0.2
gravity = 0.2
coriolis = 0.5
thermal = 0.6
thermal_sq = 0.1
haline = 0.8
mix_back = 5.0
mix_conv = 60.0
strat_scale = 2.0
momentum_mix = 2.0
bottom_drag = 1.0
surface_gain = 0.5

GROUP = 15


def density(warmth, saltiness, depth_column):
    return -thermal * warmth * (1.0 + thermal_sq * warmth + depth_column) + haline * saltiness


def face_weights(face_vel):
    return (
        0.5 * face_vel,
        jnp.maximum(face_vel, 0.0) * (1.0 / 6.0),
        jnp.minimum(face_vel, 0.0) * (1.0 / 6.0),
    )


def flux_divergence(right_w, left_w, m2, m1, q0, p1, p2):
    half_r, pos_r, neg_r = right_w
    half_l, pos_l, neg_l = left_w
    step_r = p1 - q0
    step_l = q0 - m1
    curv_0 = step_r - step_l
    curv_p = (p2 - p1) - step_r
    curv_m = step_l - (m1 - m2)
    flux_r = half_r * (q0 + p1) - (pos_r * curv_0 + neg_r * curv_p)
    flux_l = half_l * (m1 + q0) - (pos_l * curv_m + neg_l * curv_0)
    return flux_r - flux_l


def rolled(x, shift, axis):
    shift %= x.shape[axis]
    return x if shift == 0 else pltpu.roll(x, shift, axis)


def pack_kernel(
    last_ref, shore_ref, bottom_ref, t_ref, s_ref, u_ref, v_ref,
    top_ref, bot_ref, right_ref, left_ref,
):
    layers, rows, cols = t_ref.shape
    groups = layers // GROUP
    lane = lax.broadcasted_iota(jnp.int32, (rows, cols), 1)
    row = lax.broadcasted_iota(jnp.int32, (rows, cols), 0)
    dep = (shore_ref[...] * bottom_ref[...]).astype(jnp.float32)
    zero = jnp.zeros((rows, cols), jnp.float32)

    def pack_rows(vals, first):
        out = zero
        for c, val in enumerate(vals):
            out = jnp.where((row >> 1) == c, rolled(val, 2 * c - first, 0), out)
        return out

    def group_body(g, carry):
        right = zero
        left = zero
        for j in range(GROUP):
            k = g * GROUP + j
            w = (k.astype(jnp.float32) < dep).astype(jnp.float32)
            q = [r[k] * w for r in (t_ref, s_ref, u_ref, v_ref)]
            top_ref[k] = pack_rows(q, rows - 2)
            bot_ref[k] = pack_rows(q, 0)
            for c in range(4):
                m = j * 4 + c
                slot = (lane >> 1) == m
                right = jnp.where(slot, rolled(q[c], 2 * m - (cols - 2), 1), right)
                left = jnp.where(slot, rolled(q[c], 2 * m, 1), left)
        right_ref[g] = right
        left_ref[g] = left
        return carry

    lax.fori_loop(0, groups, group_body, 0)
    top_ref[layers] = pack_rows([dep], rows - 2)
    bot_ref[layers] = pack_rows([dep], 0)
    right_ref[groups] = jnp.where(lane < 2, rolled(dep, 2, 1), zero)
    left_ref[groups] = jnp.where(lane < 2, dep, zero)

    @pl.when(last_ref[0] == 1)
    def _():
        tiles = top_ref[...].reshape((layers + 1) * rows, cols)
        tile_row = lax.broadcasted_iota(jnp.int32, tiles.shape, 0) % rows
        sign = jnp.where(tile_row < 4, 1.0, -1.0)
        swapped = jnp.where(
            (tile_row & 1) == 0, rolled(tiles, -1, 0), rolled(tiles, 1, 0)
        ) * sign
        src_lane = lax.broadcasted_iota(jnp.int32, (cols, cols), 0)
        dst_lane = lax.broadcasted_iota(jnp.int32, (cols, cols), 1)
        reverse = (src_lane + dst_lane == cols - 1).astype(jnp.float32)
        flipped = jnp.dot(
            swapped, reverse, precision=lax.Precision.HIGHEST,
            preferred_element_type=jnp.float32,
        )
        top_ref[...] = flipped.reshape(layers + 1, rows, cols)


def xpart_kernel(
    h_ref, zmid_ref, shore_ref, bottom_ref, t_ref, s_ref, u_ref, v_ref, west_ref, east_ref,
    divx_ref, gradx_ref,
):
    layers, rows, cols = t_ref.shape
    groups = layers // GROUP
    lane = lax.broadcasted_iota(jnp.int32, (rows, cols), 1)

    def xs(v, e, s):
        if s == 1:
            return pltpu.roll(jnp.where(lane == 0, e, v), cols - 1, 1)
        if s == 2:
            return pltpu.roll(jnp.where(lane < 2, e, v), cols - 2, 1)
        if s == -1:
            return pltpu.roll(jnp.where(lane == cols - 1, e, v), 1, 1)
        return pltpu.roll(jnp.where(lane >= cols - 2, e, v), 2, 1)

    def lon_edge(tile_e, tile_w, m):
        return jnp.where(lane < 64, rolled(tile_e, -2 * m, 1), rolled(tile_w, cols - 2 - 2 * m, 1))

    dep = (shore_ref[...] * bottom_ref[...]).astype(jnp.float32)
    dep_lon = lon_edge(east_ref[groups], west_ref[groups], 0)
    dep_xm = xs(dep, dep_lon, -1)
    dep_xp = xs(dep, dep_lon, 1)
    zero = jnp.zeros((rows, cols), jnp.float32)

    def group_body(g, carry):
        tile_e = east_ref[g]
        tile_w = west_ref[g]
        for j in range(GROUP):
            cum_xm, cum_xp = carry
            k = g * GROUP + j
            kf = k.astype(jnp.float32)
            h = h_ref[k]
            zmid = zmid_ref[k]
            w0 = (kf < dep).astype(jnp.float32)
            wxm = (kf < dep_xm).astype(jnp.float32)
            wxp = (kf < dep_xp).astype(jnp.float32)
            q = [r[k] * w0 for r in (t_ref, s_ref, u_ref, v_ref)]
            ex = [lon_edge(tile_e, tile_w, j * 4 + c) for c in range(4)]
            xsh = {s: [xs(q[c], ex[c], s) for c in range(4)] for s in (-2, -1, 1, 2)}
            a_r = 0.5 * (q[2] + xsh[1][2]) * w0 * wxp
            a_l = 0.5 * (xsh[-1][2] + q[2]) * wxm * w0
            w_r = face_weights(a_r)
            w_l = face_weights(a_l)
            for c in range(4):
                divx_ref[c * layers + k] = q[c] - courant * flux_divergence(
                    w_r, w_l, xsh[-2][c], xsh[-1][c], q[c], xsh[1][c], xsh[2][c]
                )
            load_xm = density(xsh[-1][0], xsh[-1][1], zmid) * wxm * h
            load_xp = density(xsh[1][0], xsh[1][1], zmid) * wxp * h
            cum_xm = cum_xm + load_xm
            cum_xp = cum_xp + load_xp
            gradx_ref[k] = 0.5 * ((cum_xp - 0.5 * load_xp) - (cum_xm - 0.5 * load_xm))
            carry = (cum_xm, cum_xp)
        return carry

    lax.fori_loop(0, groups, group_body, (zero, zero))


def step_kernel(
    lat_ref, h_ref, inv_h_ref, zmid_ref, inv_sp_ref,
    shore_ref, bottom_ref, flux_ref, t_ref, s_ref, u_ref, v_ref,
    south_ref, north_ref, fold_ref, divx_ref, gradx_ref,
    o0_ref, o1_ref, o2_ref, o3_ref,
    star_scr, r_scr, rs_scr,
):
    layers = t_ref.shape[0]
    rows, cols = t_ref.shape[1], t_ref.shape[2]
    groups = layers // GROUP
    lane = lax.broadcasted_iota(jnp.int32, (rows, cols), 1)
    row = lax.broadcasted_iota(jnp.int32, (rows, cols), 0)

    def ys(v, e, s):
        if s == 1:
            return pltpu.roll(jnp.where(row == 0, e, v), rows - 1, 0)
        if s == 2:
            return pltpu.roll(jnp.where(row < 2, e, v), rows - 2, 0)
        if s == -1:
            return pltpu.roll(jnp.where(row == rows - 1, e, v), 1, 0)
        return pltpu.roll(jnp.where(row >= rows - 2, e, v), 2, 0)

    def lat_edge(tile_n, tile_s, c):
        return jnp.where(row < 4, rolled(tile_n, -2 * c, 0), rolled(tile_s, rows - 2 - 2 * c, 0))

    dep = (shore_ref[...] * bottom_ref[...]).astype(jnp.float32)
    dep_lat = lat_edge(north_ref[layers] + fold_ref[layers], south_ref[layers], 0)
    dep_ym = ys(dep, dep_lat, -1)
    dep_yp = ys(dep, dep_lat, 1)
    total_rows = rows * lat_ref[1]
    row_ids = (lat_ref[0] * rows + row).astype(jnp.float32)
    turning = coriolis * (2.0 * (row_ids + 0.5) / total_rows.astype(jnp.float32) - 1.0)
    zero = jnp.zeros((rows, cols), jnp.float32)

    def explicit(k, carry):
        cum_ym, cum_yp = carry
        kf = k.astype(jnp.float32)
        h = h_ref[k]
        zmid = zmid_ref[k]
        w0 = (kf < dep).astype(jnp.float32)
        wym = (kf < dep_ym).astype(jnp.float32)
        wyp = (kf < dep_yp).astype(jnp.float32)
        q = [r[k] * w0 for r in (t_ref, s_ref, u_ref, v_ref)]
        tile_n = north_ref[k] + fold_ref[k]
        tile_s = south_ref[k]
        ey = [lat_edge(tile_n, tile_s, c) for c in range(4)]
        ysh = {s: [ys(q[c], ey[c], s) for c in range(4)] for s in (-2, -1, 1, 2)}
        b_r = 0.5 * (q[3] + ysh[1][3]) * w0 * wyp
        b_l = 0.5 * (ysh[-1][3] + q[3]) * wym * w0
        w_r = face_weights(b_r)
        w_l = face_weights(b_l)
        adv = []
        for c in range(4):
            div_y = flux_divergence(w_r, w_l, ysh[-2][c], ysh[-1][c], q[c], ysh[1][c], ysh[2][c])
            adv.append(divx_ref[c * layers + k] - courant * div_y)
        load_ym = density(ysh[-1][0], ysh[-1][1], zmid) * wym * h
        load_yp = density(ysh[1][0], ysh[1][1], zmid) * wyp * h
        cum_ym = cum_ym + load_ym
        cum_yp = cum_yp + load_yp
        grad_x = gradx_ref[k]
        grad_y = 0.5 * ((cum_yp - 0.5 * load_yp) - (cum_ym - 0.5 * load_ym))
        star0 = adv[0] * w0
        star1 = adv[1] * w0
        star2 = (adv[2] + time_step * (turning * q[3] - gravity * grad_x)) * w0
        star3 = (adv[3] + time_step * (-turning * q[2] - gravity * grad_y)) * w0
        for c, val in enumerate((star0, star1, star2, star3)):
            star_scr[c * layers + k] = val
        rs_scr[k] = density(star0, star1, zmid)
        return (cum_ym, cum_yp)

    lag = 3
    carry_e = lax.fori_loop(0, lag, explicit, (zero, zero))

    surface_scale = surface_gain * inv_h_ref[0]
    w_top = (0.0 < dep).astype(jnp.float32)
    for c in range(4):
        star_scr[c * layers] = star_scr[c * layers] + flux_ref[c] * w_top * surface_scale

    def forward(k, carry):
        mix_prev, r_a, r_b, s0, s1, s2, s3 = carry
        kf = k.astype(jnp.float32)
        inv_h = inv_h_ref[k]
        nxt = jnp.minimum(k + 1, layers - 1)
        stratified = (rs_scr[nxt] - rs_scr[k]) * inv_sp_ref[k]
        sig = 1.0 / (1.0 + jnp.exp(stratified * (1.0 / strat_scale)))
        w_next = (kf + 1.0 < dep).astype(jnp.float32)
        mix = (mix_back + mix_conv * sig) * w_next
        mix = jnp.where(k < layers - 1, mix, 0.0)
        low_a = -mix_prev * inv_h
        up_a = -mix * inv_h
        cen_a = 1.0 - low_a - up_a
        low_b = -mix_prev * momentum_mix * inv_h
        up_b = -mix * momentum_mix * inv_h
        floor = (kf == dep - 1.0).astype(jnp.float32)
        cen_b = 1.0 - low_b - up_b + bottom_drag * floor * inv_h
        inv_a = 1.0 / (cen_a - low_a * r_a)
        inv_b = 1.0 / (cen_b - low_b * r_b)
        r_a = up_a * inv_a
        r_b = up_b * inv_b
        r_scr[k] = r_a
        r_scr[layers + k] = r_b
        s0 = (star_scr[k] - low_a * s0) * inv_a
        s1 = (star_scr[layers + k] - low_a * s1) * inv_a
        s2 = (star_scr[2 * layers + k] - low_b * s2) * inv_b
        s3 = (star_scr[3 * layers + k] - low_b * s3) * inv_b
        star_scr[k] = s0
        star_scr[layers + k] = s1
        star_scr[2 * layers + k] = s2
        star_scr[3 * layers + k] = s3
        return (mix, r_a, r_b, s0, s1, s2, s3)

    def fused(k, carry):
        carry_e, carry_f = carry
        return (explicit(k, carry_e), forward(k - lag, carry_f))

    _, carry_f = lax.fori_loop(lag, layers, fused, (carry_e, (zero,) * 7), unroll=6)
    lax.fori_loop(layers - lag, layers, forward, carry_f)

    def backward(i, carry):
        x0, x1, x2, x3 = carry
        k = layers - 1 - i
        r_a = r_scr[k]
        r_b = r_scr[layers + k]
        x0 = star_scr[k] - r_a * x0
        x1 = star_scr[layers + k] - r_a * x1
        x2 = star_scr[2 * layers + k] - r_b * x2
        x3 = star_scr[3 * layers + k] - r_b * x3
        o0_ref[k] = x0
        o1_ref[k] = x1
        o2_ref[k] = x2
        o3_ref[k] = x3
        return (x0, x1, x2, x3)

    lax.fori_loop(0, layers, backward, (zero,) * 4, unroll=3)


def level_tables(layers):
    offsets = np.arange(layers, dtype=np.float32) + np.float32(0.5)
    zmid = offsets / np.float32(layers)
    thickness = np.float32(0.5) + zmid
    inverse = np.float32(1.0) / thickness
    spacing = np.float32(0.5) * (thickness[1:] + thickness[:-1])
    inv_spacing = np.concatenate([np.float32(1.0) / spacing, np.ones((1,), np.float32)])
    return [jnp.asarray(t.astype(np.float32)) for t in (thickness, inverse, zmid, inv_spacing)]


def on_device(
    heat_anomaly,
    brine_anomaly,
    eastward_current,
    northward_current,
    shoreline_indicator,
    bottom_layer_index,
    boundary_fluxes,
):
    layers, rows, cols = heat_anomaly.shape
    fields = (heat_anomaly, brine_anomaly, eastward_current, northward_current)
    groups = layers // GROUP
    n_lat = lax.axis_size("lat")
    n_lon = lax.axis_size("lon")
    lat_idx = lax.axis_index("lat").astype(jnp.int32)
    is_last = (lat_idx == n_lat - 1).astype(jnp.int32).reshape(1)
    lat_info = jnp.stack([lat_idx, jnp.int32(n_lat)])

    smem = pl.BlockSpec(memory_space=pltpu.SMEM)
    vmem = pl.BlockSpec(memory_space=pltpu.VMEM)
    row_tiles = jax.ShapeDtypeStruct((layers + 1, rows, cols), jnp.float32)
    col_tiles = jax.ShapeDtypeStruct((groups + 1, rows, cols), jnp.float32)
    top, bot, right, left = pl.pallas_call(
        pack_kernel,
        out_shape=(row_tiles, row_tiles, col_tiles, col_tiles),
        in_specs=[smem] + [vmem] * 6,
        out_specs=(vmem,) * 4,
    )(is_last, shoreline_indicator, bottom_layer_index, *fields)

    from_south = lax.ppermute(top, "lat", [(i, i + 1) for i in range(n_lat - 1)])
    from_north = lax.ppermute(bot, "lat", [(i + 1, i) for i in range(n_lat - 1)])
    from_west = lax.ppermute(right, "lon", [(i, (i + 1) % n_lon) for i in range(n_lon)])
    from_east = lax.ppermute(left, "lon", [((i + 1) % n_lon, i) for i in range(n_lon)])
    last = (n_lat - 1) * n_lon
    fold, from_west, from_east = lax.optimization_barrier((top, from_west, from_east))
    from_fold = lax.ppermute(
        fold, ("lat", "lon"), [(last + x, last + n_lon - 1 - x) for x in range(n_lon)]
    )

    plane = jax.ShapeDtypeStruct((layers, rows, cols), jnp.float32)
    tables = level_tables(layers)
    divx, gradx = pl.pallas_call(
        xpart_kernel,
        out_shape=(jax.ShapeDtypeStruct((4 * layers, rows, cols), jnp.float32), plane),
        in_specs=[smem] * 2 + [vmem] * 8,
        out_specs=(vmem,) * 2,
    )(tables[0], tables[2], shoreline_indicator, bottom_layer_index, *fields, from_west, from_east)
    outs = pl.pallas_call(
        step_kernel,
        out_shape=(plane,) * 4,
        in_specs=[smem] * 5 + [vmem] * 12,
        out_specs=(vmem,) * 4,
        scratch_shapes=[
            pltpu.VMEM((4 * layers, rows, cols), jnp.float32),
            pltpu.VMEM((2 * layers, rows, cols), jnp.float32),
            pltpu.VMEM((layers, rows, cols), jnp.float32),
        ],
    )(
        lat_info, *tables,
        shoreline_indicator, bottom_layer_index, boundary_fluxes, *fields,
        from_south, from_north, from_fold, divx, gradx,
    )
    return tuple(outs)


def solution(mesh):
    in_specs = (
        P(None, "lat", "lon"),
        P(None, "lat", "lon"),
        P(None, "lat", "lon"),
        P(None, "lat", "lon"),
        P("lat", "lon"),
        P("lat", "lon"),
        P(None, "lat", "lon"),
    )
    out_specs = (
        P(None, "lat", "lon"),
        P(None, "lat", "lon"),
        P(None, "lat", "lon"),
        P(None, "lat", "lon"),
    )
    return jax.shard_map(
        on_device, mesh=mesh, in_specs=in_specs, out_specs=out_specs, check_vma=False
    )
```

```python
import numpy as np
import jax
import jax.numpy as jnp
from jax import lax
from jax.experimental import pallas as pl
from jax.experimental.pallas import tpu as pltpu
from jax.sharding import PartitionSpec as P

courant = 0.25
time_step = 0.2
gravity = 0.2
coriolis = 0.5
thermal = 0.6
thermal_sq = 0.1
haline = 0.8
mix_back = 5.0
mix_conv = 60.0
strat_scale = 2.0
momentum_mix = 2.0
bottom_drag = 1.0
surface_gain = 0.5

GROUP = 15


def density(warmth, saltiness, depth_column):
    return -thermal * warmth * (1.0 + thermal_sq * warmth + depth_column) + haline * saltiness


def face_weights(face_vel):
    return (
        0.5 * face_vel,
        jnp.maximum(face_vel, 0.0) * (1.0 / 6.0),
        jnp.minimum(face_vel, 0.0) * (1.0 / 6.0),
    )


def flux_divergence(right_w, left_w, m2, m1, q0, p1, p2):
    half_r, pos_r, neg_r = right_w
    half_l, pos_l, neg_l = left_w
    step_r = p1 - q0
    step_l = q0 - m1
    curv_0 = step_r - step_l
    curv_p = (p2 - p1) - step_r
    curv_m = step_l - (m1 - m2)
    flux_r = half_r * (q0 + p1) - (pos_r * curv_0 + neg_r * curv_p)
    flux_l = half_l * (m1 + q0) - (pos_l * curv_m + neg_l * curv_0)
    return flux_r - flux_l


def rolled(x, shift, axis):
    shift %= x.shape[axis]
    return x if shift == 0 else pltpu.roll(x, shift, axis)


def pack_kernel(
    last_ref, shore_ref, bottom_ref, t_hbm, s_hbm, u_hbm, v_hbm,
    top_ref, bot_ref, right_ref, left_ref,
    t_ref, s_ref, u_ref, v_ref, sems,
):
    layers, rows, cols = t_ref.shape
    groups = layers // GROUP

    def chunk_copies(g):
        span = pl.ds(g * GROUP, GROUP)
        return [
            pltpu.make_async_copy(src.at[span], dst.at[span], sems.at[g, i])
            for i, (src, dst) in enumerate(
                ((t_hbm, t_ref), (s_hbm, s_ref), (u_hbm, u_ref), (v_hbm, v_ref))
            )
        ]

    for g in range(groups):
        for copy in chunk_copies(g):
            copy.start()
    lane = lax.broadcasted_iota(jnp.int32, (rows, cols), 1)
    row = lax.broadcasted_iota(jnp.int32, (rows, cols), 0)
    dep = (shore_ref[...] * bottom_ref[...]).astype(jnp.float32)
    zero = jnp.zeros((rows, cols), jnp.float32)

    def pack_rows(vals, first):
        out = zero
        for c, val in enumerate(vals):
            out = jnp.where((row >> 1) == c, rolled(val, 2 * c - first, 0), out)
        return out

    def group_body(g, carry):
        for copy in chunk_copies(g):
            copy.wait()
        right = zero
        left = zero
        for j in range(GROUP):
            k = g * GROUP + j
            w = (k.astype(jnp.float32) < dep).astype(jnp.float32)
            q = [r[k] * w for r in (t_ref, s_ref, u_ref, v_ref)]
            top_ref[k] = pack_rows(q, rows - 2)
            bot_ref[k] = pack_rows(q, 0)
            for c in range(4):
                m = j * 4 + c
                slot = (lane >> 1) == m
                right = jnp.where(slot, rolled(q[c], 2 * m - (cols - 2), 1), right)
                left = jnp.where(slot, rolled(q[c], 2 * m, 1), left)
        right_ref[g] = right
        left_ref[g] = left
        return carry

    lax.fori_loop(0, groups, group_body, 0)
    top_ref[layers] = pack_rows([dep], rows - 2)
    bot_ref[layers] = pack_rows([dep], 0)
    right_ref[groups] = jnp.where(lane < 2, rolled(dep, 2, 1), zero)
    left_ref[groups] = jnp.where(lane < 2, dep, zero)

    @pl.when(last_ref[0] == 1)
    def _():
        tiles = top_ref[...].reshape((layers + 1) * rows, cols)
        tile_row = lax.broadcasted_iota(jnp.int32, tiles.shape, 0) % rows
        sign = jnp.where(tile_row < 4, 1.0, -1.0)
        swapped = jnp.where(
            (tile_row & 1) == 0, rolled(tiles, -1, 0), rolled(tiles, 1, 0)
        ) * sign
        src_lane = lax.broadcasted_iota(jnp.int32, (cols, cols), 0)
        dst_lane = lax.broadcasted_iota(jnp.int32, (cols, cols), 1)
        reverse = (src_lane + dst_lane == cols - 1).astype(jnp.float32)
        flipped = jnp.dot(
            swapped, reverse, precision=lax.Precision.HIGHEST,
            preferred_element_type=jnp.float32,
        )
        top_ref[...] = flipped.reshape(layers + 1, rows, cols)


def xpart_kernel(
    h_ref, zmid_ref, shore_ref, bottom_ref, t_ref, s_ref, u_ref, v_ref, west_ref, east_ref,
    divx_ref, gradx_ref,
):
    layers, rows, cols = t_ref.shape
    groups = layers // GROUP
    lane = lax.broadcasted_iota(jnp.int32, (rows, cols), 1)

    def xs(v, e, s):
        if s == 1:
            return pltpu.roll(jnp.where(lane == 0, e, v), cols - 1, 1)
        if s == 2:
            return pltpu.roll(jnp.where(lane < 2, e, v), cols - 2, 1)
        if s == -1:
            return pltpu.roll(jnp.where(lane == cols - 1, e, v), 1, 1)
        return pltpu.roll(jnp.where(lane >= cols - 2, e, v), 2, 1)

    def lon_edge(tile_e, tile_w, m):
        return jnp.where(lane < 64, rolled(tile_e, -2 * m, 1), rolled(tile_w, cols - 2 - 2 * m, 1))

    dep = (shore_ref[...] * bottom_ref[...]).astype(jnp.float32)
    dep_lon = lon_edge(east_ref[groups], west_ref[groups], 0)
    dep_xm = xs(dep, dep_lon, -1)
    dep_xp = xs(dep, dep_lon, 1)
    zero = jnp.zeros((rows, cols), jnp.float32)

    def group_body(g, carry):
        tile_e = east_ref[g]
        tile_w = west_ref[g]
        for j in range(GROUP):
            cum_xm, cum_xp = carry
            k = g * GROUP + j
            kf = k.astype(jnp.float32)
            h = h_ref[k]
            zmid = zmid_ref[k]
            w0 = (kf < dep).astype(jnp.float32)
            wxm = (kf < dep_xm).astype(jnp.float32)
            wxp = (kf < dep_xp).astype(jnp.float32)
            q = [r[k] * w0 for r in (t_ref, s_ref, u_ref, v_ref)]
            ex = [lon_edge(tile_e, tile_w, j * 4 + c) for c in range(4)]
            xsh = {s: [xs(q[c], ex[c], s) for c in range(4)] for s in (-2, -1, 1, 2)}
            a_r = 0.5 * (q[2] + xsh[1][2]) * w0 * wxp
            a_l = 0.5 * (xsh[-1][2] + q[2]) * wxm * w0
            w_r = face_weights(a_r)
            w_l = face_weights(a_l)
            for c in range(4):
                divx_ref[c * layers + k] = q[c] - courant * flux_divergence(
                    w_r, w_l, xsh[-2][c], xsh[-1][c], q[c], xsh[1][c], xsh[2][c]
                )
            load_xm = density(xsh[-1][0], xsh[-1][1], zmid) * wxm * h
            load_xp = density(xsh[1][0], xsh[1][1], zmid) * wxp * h
            cum_xm = cum_xm + load_xm
            cum_xp = cum_xp + load_xp
            gradx_ref[k] = 0.5 * ((cum_xp - 0.5 * load_xp) - (cum_xm - 0.5 * load_xm))
            carry = (cum_xm, cum_xp)
        return carry

    lax.fori_loop(0, groups, group_body, (zero, zero))


def step_kernel(
    lat_ref, h_ref, inv_h_ref, zmid_ref, inv_sp_ref,
    shore_ref, bottom_ref, flux_ref, t_ref, s_ref, u_ref, v_ref,
    south_ref, north_ref, fold_ref, divx_ref, gradx_ref,
    o0_ref, o1_ref, o2_ref, o3_ref,
    star_scr, r_scr, rs_scr,
):
    layers = t_ref.shape[0]
    rows, cols = t_ref.shape[1], t_ref.shape[2]
    groups = layers // GROUP
    lane = lax.broadcasted_iota(jnp.int32, (rows, cols), 1)
    row = lax.broadcasted_iota(jnp.int32, (rows, cols), 0)

    def ys(v, e, s):
        if s == 1:
            return pltpu.roll(jnp.where(row == 0, e, v), rows - 1, 0)
        if s == 2:
            return pltpu.roll(jnp.where(row < 2, e, v), rows - 2, 0)
        if s == -1:
            return pltpu.roll(jnp.where(row == rows - 1, e, v), 1, 0)
        return pltpu.roll(jnp.where(row >= rows - 2, e, v), 2, 0)

    def lat_edge(tile_n, tile_s, c):
        return jnp.where(row < 4, rolled(tile_n, -2 * c, 0), rolled(tile_s, rows - 2 - 2 * c, 0))

    dep = (shore_ref[...] * bottom_ref[...]).astype(jnp.float32)
    dep_lat = lat_edge(north_ref[layers] + fold_ref[layers], south_ref[layers], 0)
    dep_ym = ys(dep, dep_lat, -1)
    dep_yp = ys(dep, dep_lat, 1)
    total_rows = rows * lat_ref[1]
    row_ids = (lat_ref[0] * rows + row).astype(jnp.float32)
    turning = coriolis * (2.0 * (row_ids + 0.5) / total_rows.astype(jnp.float32) - 1.0)
    zero = jnp.zeros((rows, cols), jnp.float32)

    def explicit(k, carry):
        cum_ym, cum_yp = carry
        kf = k.astype(jnp.float32)
        h = h_ref[k]
        zmid = zmid_ref[k]
        w0 = (kf < dep).astype(jnp.float32)
        wym = (kf < dep_ym).astype(jnp.float32)
        wyp = (kf < dep_yp).astype(jnp.float32)
        q = [r[k] * w0 for r in (t_ref, s_ref, u_ref, v_ref)]
        tile_n = north_ref[k] + fold_ref[k]
        tile_s = south_ref[k]
        ey = [lat_edge(tile_n, tile_s, c) for c in range(4)]
        ysh = {s: [ys(q[c], ey[c], s) for c in range(4)] for s in (-2, -1, 1, 2)}
        b_r = 0.5 * (q[3] + ysh[1][3]) * w0 * wyp
        b_l = 0.5 * (ysh[-1][3] + q[3]) * wym * w0
        w_r = face_weights(b_r)
        w_l = face_weights(b_l)
        adv = []
        for c in range(4):
            div_y = flux_divergence(w_r, w_l, ysh[-2][c], ysh[-1][c], q[c], ysh[1][c], ysh[2][c])
            adv.append(divx_ref[c * layers + k] - courant * div_y)
        load_ym = density(ysh[-1][0], ysh[-1][1], zmid) * wym * h
        load_yp = density(ysh[1][0], ysh[1][1], zmid) * wyp * h
        cum_ym = cum_ym + load_ym
        cum_yp = cum_yp + load_yp
        grad_x = gradx_ref[k]
        grad_y = 0.5 * ((cum_yp - 0.5 * load_yp) - (cum_ym - 0.5 * load_ym))
        star0 = adv[0] * w0
        star1 = adv[1] * w0
        star2 = (adv[2] + time_step * (turning * q[3] - gravity * grad_x)) * w0
        star3 = (adv[3] + time_step * (-turning * q[2] - gravity * grad_y)) * w0
        for c, val in enumerate((star0, star1, star2, star3)):
            star_scr[c * layers + k] = val
        rs_scr[k] = density(star0, star1, zmid)
        return (cum_ym, cum_yp)

    lag = 3
    carry_e = lax.fori_loop(0, lag, explicit, (zero, zero))

    surface_scale = surface_gain * inv_h_ref[0]
    w_top = (0.0 < dep).astype(jnp.float32)
    for c in range(4):
        star_scr[c * layers] = star_scr[c * layers] + flux_ref[c] * w_top * surface_scale

    def forward(k, carry):
        mix_prev, r_a, r_b, s0, s1, s2, s3 = carry
        kf = k.astype(jnp.float32)
        inv_h = inv_h_ref[k]
        nxt = jnp.minimum(k + 1, layers - 1)
        stratified = (rs_scr[nxt] - rs_scr[k]) * inv_sp_ref[k]
        sig = 1.0 / (1.0 + jnp.exp(stratified * (1.0 / strat_scale)))
        w_next = (kf + 1.0 < dep).astype(jnp.float32)
        mix = (mix_back + mix_conv * sig) * w_next
        mix = jnp.where(k < layers - 1, mix, 0.0)
        low_a = -mix_prev * inv_h
        up_a = -mix * inv_h
        cen_a = 1.0 - low_a - up_a
        low_b = -mix_prev * momentum_mix * inv_h
        up_b = -mix * momentum_mix * inv_h
        floor = (kf == dep - 1.0).astype(jnp.float32)
        cen_b = 1.0 - low_b - up_b + bottom_drag * floor * inv_h
        inv_a = 1.0 / (cen_a - low_a * r_a)
        inv_b = 1.0 / (cen_b - low_b * r_b)
        r_a = up_a * inv_a
        r_b = up_b * inv_b
        r_scr[k] = r_a
        r_scr[layers + k] = r_b
        s0 = (star_scr[k] - low_a * s0) * inv_a
        s1 = (star_scr[layers + k] - low_a * s1) * inv_a
        s2 = (star_scr[2 * layers + k] - low_b * s2) * inv_b
        s3 = (star_scr[3 * layers + k] - low_b * s3) * inv_b
        star_scr[k] = s0
        star_scr[layers + k] = s1
        star_scr[2 * layers + k] = s2
        star_scr[3 * layers + k] = s3
        return (mix, r_a, r_b, s0, s1, s2, s3)

    def fused(k, carry):
        carry_e, carry_f = carry
        return (explicit(k, carry_e), forward(k - lag, carry_f))

    _, carry_f = lax.fori_loop(lag, layers, fused, (carry_e, (zero,) * 7), unroll=6)
    lax.fori_loop(layers - lag, layers, forward, carry_f)

    def backward(i, carry):
        x0, x1, x2, x3 = carry
        k = layers - 1 - i
        r_a = r_scr[k]
        r_b = r_scr[layers + k]
        x0 = star_scr[k] - r_a * x0
        x1 = star_scr[layers + k] - r_a * x1
        x2 = star_scr[2 * layers + k] - r_b * x2
        x3 = star_scr[3 * layers + k] - r_b * x3
        o0_ref[k] = x0
        o1_ref[k] = x1
        o2_ref[k] = x2
        o3_ref[k] = x3
        return (x0, x1, x2, x3)

    lax.fori_loop(0, layers, backward, (zero,) * 4, unroll=3)


def level_tables(layers):
    offsets = np.arange(layers, dtype=np.float32) + np.float32(0.5)
    zmid = offsets / np.float32(layers)
    thickness = np.float32(0.5) + zmid
    inverse = np.float32(1.0) / thickness
    spacing = np.float32(0.5) * (thickness[1:] + thickness[:-1])
    inv_spacing = np.concatenate([np.float32(1.0) / spacing, np.ones((1,), np.float32)])
    return [jnp.asarray(t.astype(np.float32)) for t in (thickness, inverse, zmid, inv_spacing)]


def on_device(
    heat_anomaly,
    brine_anomaly,
    eastward_current,
    northward_current,
    shoreline_indicator,
    bottom_layer_index,
    boundary_fluxes,
):
    layers, rows, cols = heat_anomaly.shape
    fields = (heat_anomaly, brine_anomaly, eastward_current, northward_current)
    groups = layers // GROUP
    n_lat = lax.axis_size("lat")
    n_lon = lax.axis_size("lon")
    lat_idx = lax.axis_index("lat").astype(jnp.int32)
    is_last = (lat_idx == n_lat - 1).astype(jnp.int32).reshape(1)
    lat_info = jnp.stack([lat_idx, jnp.int32(n_lat)])

    smem = pl.BlockSpec(memory_space=pltpu.SMEM)
    vmem = pl.BlockSpec(memory_space=pltpu.VMEM)
    row_tiles = jax.ShapeDtypeStruct((layers + 1, rows, cols), jnp.float32)
    col_tiles = jax.ShapeDtypeStruct((groups + 1, rows, cols), jnp.float32)
    top, bot, right, left = pl.pallas_call(
        pack_kernel,
        out_shape=(row_tiles, row_tiles, col_tiles, col_tiles),
        in_specs=[smem] + [vmem] * 2 + [pl.BlockSpec(memory_space=pl.ANY)] * 4,
        out_specs=(vmem,) * 4,
        scratch_shapes=[pltpu.VMEM((layers, rows, cols), jnp.float32)] * 4
        + [pltpu.SemaphoreType.DMA((groups, 4))],
    )(is_last, shoreline_indicator, bottom_layer_index, *fields)

    from_south = lax.ppermute(top, "lat", [(i, i + 1) for i in range(n_lat - 1)])
    from_north = lax.ppermute(bot, "lat", [(i + 1, i) for i in range(n_lat - 1)])
    from_west = lax.ppermute(right, "lon", [(i, (i + 1) % n_lon) for i in range(n_lon)])
    from_east = lax.ppermute(left, "lon", [((i + 1) % n_lon, i) for i in range(n_lon)])
    last = (n_lat - 1) * n_lon
    fold, from_west, from_east = lax.optimization_barrier((top, from_west, from_east))
    from_fold = lax.ppermute(
        fold, ("lat", "lon"), [(last + x, last + n_lon - 1 - x) for x in range(n_lon)]
    )

    plane = jax.ShapeDtypeStruct((layers, rows, cols), jnp.float32)
    tables = level_tables(layers)
    divx, gradx = pl.pallas_call(
        xpart_kernel,
        out_shape=(jax.ShapeDtypeStruct((4 * layers, rows, cols), jnp.float32), plane),
        in_specs=[smem] * 2 + [vmem] * 8,
        out_specs=(vmem,) * 2,
    )(tables[0], tables[2], shoreline_indicator, bottom_layer_index, *fields, from_west, from_east)
    outs = pl.pallas_call(
        step_kernel,
        out_shape=(plane,) * 4,
        in_specs=[smem] * 5 + [vmem] * 12,
        out_specs=(vmem,) * 4,
        scratch_shapes=[
            pltpu.VMEM((4 * layers, rows, cols), jnp.float32),
            pltpu.VMEM((2 * layers, rows, cols), jnp.float32),
            pltpu.VMEM((layers, rows, cols), jnp.float32),
        ],
    )(
        lat_info, *tables,
        shoreline_indicator, bottom_layer_index, boundary_fluxes, *fields,
        from_south, from_north, from_fold, divx, gradx,
    )
    return tuple(outs)


def solution(mesh):
    in_specs = (
        P(None, "lat", "lon"),
        P(None, "lat", "lon"),
        P(None, "lat", "lon"),
        P(None, "lat", "lon"),
        P("lat", "lon"),
        P("lat", "lon"),
        P(None, "lat", "lon"),
    )
    out_specs = (
        P(None, "lat", "lon"),
        P(None, "lat", "lon"),
        P(None, "lat", "lon"),
        P(None, "lat", "lon"),
    )
    return jax.shard_map(
        on_device, mesh=mesh, in_specs=in_specs, out_specs=out_specs, check_vma=False
    )
```

```python
import numpy as np
import jax
import jax.numpy as jnp
from jax import lax
from jax.experimental import pallas as pl
from jax.experimental.pallas import tpu as pltpu
from jax.sharding import PartitionSpec as P

courant = 0.25
time_step = 0.2
gravity = 0.2
coriolis = 0.5
thermal = 0.6
thermal_sq = 0.1
haline = 0.8
mix_back = 5.0
mix_conv = 60.0
strat_scale = 2.0
momentum_mix = 2.0
bottom_drag = 1.0
surface_gain = 0.5

GROUP = 15


def density(warmth, saltiness, depth_column):
    return -thermal * warmth * (1.0 + thermal_sq * warmth + depth_column) + haline * saltiness


def face_weights(face_vel):
    return (
        0.5 * face_vel,
        jnp.maximum(face_vel, 0.0) * (1.0 / 6.0),
        jnp.minimum(face_vel, 0.0) * (1.0 / 6.0),
    )


def flux_divergence(right_w, left_w, m2, m1, q0, p1, p2):
    half_r, pos_r, neg_r = right_w
    half_l, pos_l, neg_l = left_w
    step_r = p1 - q0
    step_l = q0 - m1
    curv_0 = step_r - step_l
    curv_p = (p2 - p1) - step_r
    curv_m = step_l - (m1 - m2)
    flux_r = half_r * (q0 + p1) - (pos_r * curv_0 + neg_r * curv_p)
    flux_l = half_l * (m1 + q0) - (pos_l * curv_m + neg_l * curv_0)
    return flux_r - flux_l


def rolled(x, shift, axis):
    shift %= x.shape[axis]
    return x if shift == 0 else pltpu.roll(x, shift, axis)


def pack_kernel(
    last_ref, shore_ref, bottom_ref, t_ref, s_ref, u_ref, v_ref,
    top_ref, bot_ref, right_ref, left_ref,
):
    layers, rows, cols = t_ref.shape
    groups = layers // GROUP
    lane = lax.broadcasted_iota(jnp.int32, (rows, cols), 1)
    row = lax.broadcasted_iota(jnp.int32, (rows, cols), 0)
    dep = (shore_ref[...] * bottom_ref[...]).astype(jnp.float32)
    zero = jnp.zeros((rows, cols), jnp.float32)

    def pack_rows(vals, first):
        out = zero
        for c, val in enumerate(vals):
            out = jnp.where((row >> 1) == c, rolled(val, 2 * c - first, 0), out)
        return out

    def group_body(g, carry):
        right = zero
        left = zero
        for j in range(GROUP):
            k = g * GROUP + j
            w = (k.astype(jnp.float32) < dep).astype(jnp.float32)
            q = [r[k] * w for r in (t_ref, s_ref, u_ref, v_ref)]
            top_ref[k] = pack_rows(q, rows - 2)
            bot_ref[k] = pack_rows(q, 0)
            for c in range(4):
                m = j * 4 + c
                slot = (lane >> 1) == m
                right = jnp.where(slot, rolled(q[c], 2 * m - (cols - 2), 1), right)
                left = jnp.where(slot, rolled(q[c], 2 * m, 1), left)
        right_ref[g] = right
        left_ref[g] = left
        return carry

    lax.fori_loop(0, groups, group_body, 0)
    top_ref[layers] = pack_rows([dep], rows - 2)
    bot_ref[layers] = pack_rows([dep], 0)
    right_ref[groups] = jnp.where(lane < 2, rolled(dep, 2, 1), zero)
    left_ref[groups] = jnp.where(lane < 2, dep, zero)

    @pl.when(last_ref[0] == 1)
    def _():
        tiles = top_ref[...].reshape((layers + 1) * rows, cols)
        tile_row = lax.broadcasted_iota(jnp.int32, tiles.shape, 0) % rows
        sign = jnp.where(tile_row < 4, 1.0, -1.0)
        swapped = jnp.where(
            (tile_row & 1) == 0, rolled(tiles, -1, 0), rolled(tiles, 1, 0)
        ) * sign
        src_lane = lax.broadcasted_iota(jnp.int32, (cols, cols), 0)
        dst_lane = lax.broadcasted_iota(jnp.int32, (cols, cols), 1)
        reverse = (src_lane + dst_lane == cols - 1).astype(jnp.float32)
        flipped = jnp.dot(
            swapped, reverse, precision=lax.Precision.HIGHEST,
            preferred_element_type=jnp.float32,
        )
        top_ref[...] = flipped.reshape(layers + 1, rows, cols)


def xpart_kernel(
    h_ref, zmid_ref, shore_ref, bottom_ref, t_ref, s_ref, u_ref, v_ref, west_ref, east_ref,
    divx_ref, gradx_ref,
):
    layers, rows, cols = t_ref.shape
    groups = layers // GROUP
    lane = lax.broadcasted_iota(jnp.int32, (rows, cols), 1)

    def xs(v, e, s):
        if s == 1:
            return pltpu.roll(jnp.where(lane == 0, e, v), cols - 1, 1)
        if s == 2:
            return pltpu.roll(jnp.where(lane < 2, e, v), cols - 2, 1)
        if s == -1:
            return pltpu.roll(jnp.where(lane == cols - 1, e, v), 1, 1)
        return pltpu.roll(jnp.where(lane >= cols - 2, e, v), 2, 1)

    def lon_edge(tile_e, tile_w, m):
        return jnp.where(lane < 64, rolled(tile_e, -2 * m, 1), rolled(tile_w, cols - 2 - 2 * m, 1))

    dep = (shore_ref[...] * bottom_ref[...]).astype(jnp.float32)
    dep_lon = lon_edge(east_ref[groups], west_ref[groups], 0)
    dep_xm = xs(dep, dep_lon, -1)
    dep_xp = xs(dep, dep_lon, 1)
    zero = jnp.zeros((rows, cols), jnp.float32)

    def group_body(g, carry):
        tile_e = east_ref[g]
        tile_w = west_ref[g]
        for j in range(GROUP):
            cum_xm, cum_xp = carry
            k = g * GROUP + j
            kf = k.astype(jnp.float32)
            h = h_ref[k]
            zmid = zmid_ref[k]
            w0 = (kf < dep).astype(jnp.float32)
            wxm = (kf < dep_xm).astype(jnp.float32)
            wxp = (kf < dep_xp).astype(jnp.float32)
            q = [r[k] * w0 for r in (t_ref, s_ref, u_ref, v_ref)]
            ex = [lon_edge(tile_e, tile_w, j * 4 + c) for c in range(4)]
            xsh = {s: [xs(q[c], ex[c], s) for c in range(4)] for s in (-2, -1, 1, 2)}
            a_r = 0.5 * (q[2] + xsh[1][2]) * w0 * wxp
            a_l = 0.5 * (xsh[-1][2] + q[2]) * wxm * w0
            w_r = face_weights(a_r)
            w_l = face_weights(a_l)
            for c in range(4):
                divx_ref[c * layers + k] = q[c] - courant * flux_divergence(
                    w_r, w_l, xsh[-2][c], xsh[-1][c], q[c], xsh[1][c], xsh[2][c]
                )
            load_xm = density(xsh[-1][0], xsh[-1][1], zmid) * wxm * h
            load_xp = density(xsh[1][0], xsh[1][1], zmid) * wxp * h
            cum_xm = cum_xm + load_xm
            cum_xp = cum_xp + load_xp
            gradx_ref[k] = 0.5 * ((cum_xp - 0.5 * load_xp) - (cum_xm - 0.5 * load_xm))
            carry = (cum_xm, cum_xp)
        return carry

    lax.fori_loop(0, groups, group_body, (zero, zero))


def step_kernel(
    lat_ref, h_ref, inv_h_ref, zmid_ref, inv_sp_ref,
    shore_ref, bottom_ref, flux_ref, t_ref, s_ref, u_ref, v_ref,
    south_ref, north_ref, fold_ref, divx_ref, gradx_ref,
    o0_ref, o1_ref, o2_ref, o3_ref,
    star_scr, r_scr, rs_scr,
):
    layers = t_ref.shape[0]
    rows, cols = t_ref.shape[1], t_ref.shape[2]
    groups = layers // GROUP
    lane = lax.broadcasted_iota(jnp.int32, (rows, cols), 1)
    row = lax.broadcasted_iota(jnp.int32, (rows, cols), 0)

    def ys(v, e, s):
        if s == 1:
            return pltpu.roll(jnp.where(row == 0, e, v), rows - 1, 0)
        if s == 2:
            return pltpu.roll(jnp.where(row < 2, e, v), rows - 2, 0)
        if s == -1:
            return pltpu.roll(jnp.where(row == rows - 1, e, v), 1, 0)
        return pltpu.roll(jnp.where(row >= rows - 2, e, v), 2, 0)

    def lat_edge(tile_n, tile_s, c):
        return jnp.where(row < 4, rolled(tile_n, -2 * c, 0), rolled(tile_s, rows - 2 - 2 * c, 0))

    dep = (shore_ref[...] * bottom_ref[...]).astype(jnp.float32)
    dep_lat = lat_edge(north_ref[layers] + fold_ref[layers], south_ref[layers], 0)
    dep_ym = ys(dep, dep_lat, -1)
    dep_yp = ys(dep, dep_lat, 1)
    total_rows = rows * lat_ref[1]
    row_ids = (lat_ref[0] * rows + row).astype(jnp.float32)
    turning = coriolis * (2.0 * (row_ids + 0.5) / total_rows.astype(jnp.float32) - 1.0)
    zero = jnp.zeros((rows, cols), jnp.float32)

    def explicit(k, carry):
        cum_ym, cum_yp = carry
        kf = k.astype(jnp.float32)
        h = h_ref[k]
        zmid = zmid_ref[k]
        w0 = (kf < dep).astype(jnp.float32)
        wym = (kf < dep_ym).astype(jnp.float32)
        wyp = (kf < dep_yp).astype(jnp.float32)
        q = [r[k] * w0 for r in (t_ref, s_ref, u_ref, v_ref)]
        tile_n = north_ref[k] + fold_ref[k]
        tile_s = south_ref[k]
        ey = [lat_edge(tile_n, tile_s, c) for c in range(4)]
        ysh = {s: [ys(q[c], ey[c], s) for c in range(4)] for s in (-2, -1, 1, 2)}
        b_r = 0.5 * (q[3] + ysh[1][3]) * w0 * wyp
        b_l = 0.5 * (ysh[-1][3] + q[3]) * wym * w0
        w_r = face_weights(b_r)
        w_l = face_weights(b_l)
        adv = []
        for c in range(4):
            div_y = flux_divergence(w_r, w_l, ysh[-2][c], ysh[-1][c], q[c], ysh[1][c], ysh[2][c])
            adv.append(divx_ref[c * layers + k] - courant * div_y)
        load_ym = density(ysh[-1][0], ysh[-1][1], zmid) * wym * h
        load_yp = density(ysh[1][0], ysh[1][1], zmid) * wyp * h
        cum_ym = cum_ym + load_ym
        cum_yp = cum_yp + load_yp
        grad_x = gradx_ref[k]
        grad_y = 0.5 * ((cum_yp - 0.5 * load_yp) - (cum_ym - 0.5 * load_ym))
        star0 = adv[0] * w0
        star1 = adv[1] * w0
        star2 = (adv[2] + time_step * (turning * q[3] - gravity * grad_x)) * w0
        star3 = (adv[3] + time_step * (-turning * q[2] - gravity * grad_y)) * w0
        for c, val in enumerate((star0, star1, star2, star3)):
            star_scr[c * layers + k] = val
        rs_scr[k] = density(star0, star1, zmid)
        return (cum_ym, cum_yp)

    lag = 3
    carry_e = lax.fori_loop(0, lag, explicit, (zero, zero))

    surface_scale = surface_gain * inv_h_ref[0]
    w_top = (0.0 < dep).astype(jnp.float32)
    for c in range(4):
        star_scr[c * layers] = star_scr[c * layers] + flux_ref[c] * w_top * surface_scale

    def forward(k, carry):
        mix_prev, r_a, r_b, s0, s1, s2, s3 = carry
        kf = k.astype(jnp.float32)
        inv_h = inv_h_ref[k]
        nxt = jnp.minimum(k + 1, layers - 1)
        stratified = (rs_scr[nxt] - rs_scr[k]) * inv_sp_ref[k]
        sig = 1.0 / (1.0 + jnp.exp(stratified * (1.0 / strat_scale)))
        w_next = (kf + 1.0 < dep).astype(jnp.float32)
        mix = (mix_back + mix_conv * sig) * w_next
        mix = jnp.where(k < layers - 1, mix, 0.0)
        low_a = -mix_prev * inv_h
        up_a = -mix * inv_h
        cen_a = 1.0 - low_a - up_a
        low_b = -mix_prev * momentum_mix * inv_h
        up_b = -mix * momentum_mix * inv_h
        floor = (kf == dep - 1.0).astype(jnp.float32)
        cen_b = 1.0 - low_b - up_b + bottom_drag * floor * inv_h
        inv_a = 1.0 / (cen_a - low_a * r_a)
        inv_b = 1.0 / (cen_b - low_b * r_b)
        r_a = up_a * inv_a
        r_b = up_b * inv_b
        r_scr[k] = r_a
        r_scr[layers + k] = r_b
        s0 = (star_scr[k] - low_a * s0) * inv_a
        s1 = (star_scr[layers + k] - low_a * s1) * inv_a
        s2 = (star_scr[2 * layers + k] - low_b * s2) * inv_b
        s3 = (star_scr[3 * layers + k] - low_b * s3) * inv_b
        star_scr[k] = s0
        star_scr[layers + k] = s1
        star_scr[2 * layers + k] = s2
        star_scr[3 * layers + k] = s3
        return (mix, r_a, r_b, s0, s1, s2, s3)

    def fused(k, carry):
        carry_e, carry_f = carry
        return (explicit(k, carry_e), forward(k - lag, carry_f))

    _, carry_f = lax.fori_loop(lag, layers, fused, (carry_e, (zero,) * 7), unroll=6)
    lax.fori_loop(layers - lag, layers, forward, carry_f)

    def backward(i, carry):
        x0, x1, x2, x3 = carry
        k = layers - 1 - i
        r_a = r_scr[k]
        r_b = r_scr[layers + k]
        x0 = star_scr[k] - r_a * x0
        x1 = star_scr[layers + k] - r_a * x1
        x2 = star_scr[2 * layers + k] - r_b * x2
        x3 = star_scr[3 * layers + k] - r_b * x3
        o0_ref[k] = x0
        o1_ref[k] = x1
        o2_ref[k] = x2
        o3_ref[k] = x3
        return (x0, x1, x2, x3)

    lax.fori_loop(0, layers, backward, (zero,) * 4, unroll=3)


def level_tables(layers):
    offsets = np.arange(layers, dtype=np.float32) + np.float32(0.5)
    zmid = offsets / np.float32(layers)
    thickness = np.float32(0.5) + zmid
    inverse = np.float32(1.0) / thickness
    spacing = np.float32(0.5) * (thickness[1:] + thickness[:-1])
    inv_spacing = np.concatenate([np.float32(1.0) / spacing, np.ones((1,), np.float32)])
    return [jnp.asarray(t.astype(np.float32)) for t in (thickness, inverse, zmid, inv_spacing)]


def on_device(
    heat_anomaly,
    brine_anomaly,
    eastward_current,
    northward_current,
    shoreline_indicator,
    bottom_layer_index,
    boundary_fluxes,
):
    layers, rows, cols = heat_anomaly.shape
    fields = (heat_anomaly, brine_anomaly, eastward_current, northward_current)
    groups = layers // GROUP
    n_lat = lax.axis_size("lat")
    n_lon = lax.axis_size("lon")
    lat_idx = lax.axis_index("lat").astype(jnp.int32)
    is_last = (lat_idx == n_lat - 1).astype(jnp.int32).reshape(1)
    lat_info = jnp.stack([lat_idx, jnp.int32(n_lat)])

    smem = pl.BlockSpec(memory_space=pltpu.SMEM)
    vmem = pl.BlockSpec(memory_space=pltpu.VMEM)
    row_tiles = jax.ShapeDtypeStruct((layers + 1, rows, cols), jnp.float32)
    col_tiles = jax.ShapeDtypeStruct((groups + 1, rows, cols), jnp.float32)
    top, bot, right, left = pl.pallas_call(
        pack_kernel,
        out_shape=(row_tiles, row_tiles, col_tiles, col_tiles),
        in_specs=[smem] + [vmem] * 6,
        out_specs=(vmem,) * 4,
    )(is_last, shoreline_indicator, bottom_layer_index, *fields)

    from_south = lax.ppermute(top, "lat", [(i, i + 1) for i in range(n_lat - 1)])
    from_north = lax.ppermute(bot, "lat", [(i + 1, i) for i in range(n_lat - 1)])
    from_west = lax.ppermute(right, "lon", [(i, (i + 1) % n_lon) for i in range(n_lon)])
    from_east = lax.ppermute(left, "lon", [((i + 1) % n_lon, i) for i in range(n_lon)])
    last = (n_lat - 1) * n_lon
    fold, from_west, from_east = lax.optimization_barrier((top, from_west, from_east))
    from_fold = lax.ppermute(
        fold, ("lat", "lon"), [(last + x, last + n_lon - 1 - x) for x in range(n_lon)]
    )

    plane = jax.ShapeDtypeStruct((layers, rows, cols), jnp.float32)
    tables = level_tables(layers)
    divx, gradx = pl.pallas_call(
        xpart_kernel,
        out_shape=(jax.ShapeDtypeStruct((4 * layers, rows, cols), jnp.float32), plane),
        in_specs=[smem] * 2 + [vmem] * 8,
        out_specs=(vmem,) * 2,
        compiler_params=pltpu.CompilerParams(vmem_limit_bytes=16 * 1024 * 1024),
    )(tables[0], tables[2], shoreline_indicator, bottom_layer_index, *fields, from_west, from_east)
    outs = pl.pallas_call(
        step_kernel,
        out_shape=(plane,) * 4,
        in_specs=[smem] * 5 + [vmem] * 12,
        out_specs=(vmem,) * 4,
        scratch_shapes=[
            pltpu.VMEM((4 * layers, rows, cols), jnp.float32),
            pltpu.VMEM((2 * layers, rows, cols), jnp.float32),
            pltpu.VMEM((layers, rows, cols), jnp.float32),
        ],
        compiler_params=pltpu.CompilerParams(vmem_limit_bytes=16 * 1024 * 1024),
    )(
        lat_info, *tables,
        shoreline_indicator, bottom_layer_index, boundary_fluxes, *fields,
        from_south, from_north, from_fold, divx, gradx,
    )
    return tuple(outs)


def solution(mesh):
    in_specs = (
        P(None, "lat", "lon"),
        P(None, "lat", "lon"),
        P(None, "lat", "lon"),
        P(None, "lat", "lon"),
        P("lat", "lon"),
        P("lat", "lon"),
        P(None, "lat", "lon"),
    )
    out_specs = (
        P(None, "lat", "lon"),
        P(None, "lat", "lon"),
        P(None, "lat", "lon"),
        P(None, "lat", "lon"),
    )
    return jax.shard_map(
        on_device, mesh=mesh, in_specs=in_specs, out_specs=out_specs, check_vma=False
    )
```

```python
import numpy as np
import jax
import jax.numpy as jnp
from jax import lax
from jax.experimental import pallas as pl
from jax.experimental.pallas import tpu as pltpu
from jax.sharding import PartitionSpec as P

courant = 0.25
time_step = 0.2
gravity = 0.2
coriolis = 0.5
thermal = 0.6
thermal_sq = 0.1
haline = 0.8
mix_back = 5.0
mix_conv = 60.0
strat_scale = 2.0
momentum_mix = 2.0
bottom_drag = 1.0
surface_gain = 0.5

GROUP = 15


def density(warmth, saltiness, depth_column):
    return -thermal * warmth * (1.0 + thermal_sq * warmth + depth_column) + haline * saltiness


def face_weights(face_vel):
    return (
        0.5 * face_vel,
        jnp.maximum(face_vel, 0.0) * (1.0 / 6.0),
        jnp.minimum(face_vel, 0.0) * (1.0 / 6.0),
    )


def flux_divergence(right_w, left_w, m2, m1, q0, p1, p2):
    half_r, pos_r, neg_r = right_w
    half_l, pos_l, neg_l = left_w
    step_r = p1 - q0
    step_l = q0 - m1
    curv_0 = step_r - step_l
    curv_p = (p2 - p1) - step_r
    curv_m = step_l - (m1 - m2)
    flux_r = half_r * (q0 + p1) - (pos_r * curv_0 + neg_r * curv_p)
    flux_l = half_l * (m1 + q0) - (pos_l * curv_m + neg_l * curv_0)
    return flux_r - flux_l


def rolled(x, shift, axis):
    shift %= x.shape[axis]
    return x if shift == 0 else pltpu.roll(x, shift, axis)


def pack_kernel(
    last_ref, shore_ref, bottom_ref, t_ref, s_ref, u_ref, v_ref,
    top_ref, bot_ref, right_ref, left_ref,
):
    layers, rows, cols = t_ref.shape
    groups = layers // GROUP
    lane = lax.broadcasted_iota(jnp.int32, (rows, cols), 1)
    row = lax.broadcasted_iota(jnp.int32, (rows, cols), 0)
    dep = (shore_ref[...] * bottom_ref[...]).astype(jnp.float32)
    zero = jnp.zeros((rows, cols), jnp.float32)

    def pack_rows(vals, first):
        out = zero
        for c, val in enumerate(vals):
            out = jnp.where((row >> 1) == c, rolled(val, 2 * c - first, 0), out)
        return out

    def group_body(g, carry):
        right = zero
        left = zero
        for j in range(GROUP):
            k = g * GROUP + j
            w = (k.astype(jnp.float32) < dep).astype(jnp.float32)
            q = [r[k] * w for r in (t_ref, s_ref, u_ref, v_ref)]
            top_ref[k] = pack_rows(q, rows - 2)
            bot_ref[k] = pack_rows(q, 0)
            for c in range(4):
                m = j * 4 + c
                slot = (lane >> 1) == m
                right = jnp.where(slot, rolled(q[c], 2 * m - (cols - 2), 1), right)
                left = jnp.where(slot, rolled(q[c], 2 * m, 1), left)
        right_ref[g] = right
        left_ref[g] = left
        return carry

    lax.fori_loop(0, groups, group_body, 0)
    top_ref[layers] = pack_rows([dep], rows - 2)
    bot_ref[layers] = pack_rows([dep], 0)
    right_ref[groups] = jnp.where(lane < 2, rolled(dep, 2, 1), zero)
    left_ref[groups] = jnp.where(lane < 2, dep, zero)

    @pl.when(last_ref[0] == 1)
    def _():
        tiles = top_ref[...].reshape((layers + 1) * rows, cols)
        tile_row = lax.broadcasted_iota(jnp.int32, tiles.shape, 0) % rows
        sign = jnp.where(tile_row < 4, 1.0, -1.0)
        swapped = jnp.where(
            (tile_row & 1) == 0, rolled(tiles, -1, 0), rolled(tiles, 1, 0)
        ) * sign
        src_lane = lax.broadcasted_iota(jnp.int32, (cols, cols), 0)
        dst_lane = lax.broadcasted_iota(jnp.int32, (cols, cols), 1)
        reverse = (src_lane + dst_lane == cols - 1).astype(jnp.float32)
        flipped = jnp.dot(
            swapped, reverse, precision=lax.Precision.HIGHEST,
            preferred_element_type=jnp.float32,
        )
        top_ref[...] = flipped.reshape(layers + 1, rows, cols)


def xpart_kernel(
    h_ref, zmid_ref, shore_ref, bottom_ref, t_ref, s_ref, u_ref, v_ref, west_ref, east_ref,
    divx_ref, gradx_ref,
):
    layers, rows, cols = t_ref.shape
    groups = layers // GROUP
    lane = lax.broadcasted_iota(jnp.int32, (rows, cols), 1)

    def xs(v, e, s):
        if s == 1:
            return pltpu.roll(jnp.where(lane == 0, e, v), cols - 1, 1)
        if s == 2:
            return pltpu.roll(jnp.where(lane < 2, e, v), cols - 2, 1)
        if s == -1:
            return pltpu.roll(jnp.where(lane == cols - 1, e, v), 1, 1)
        return pltpu.roll(jnp.where(lane >= cols - 2, e, v), 2, 1)

    def lon_edge(tile_e, tile_w, m):
        return jnp.where(lane < 64, rolled(tile_e, -2 * m, 1), rolled(tile_w, cols - 2 - 2 * m, 1))

    dep = (shore_ref[...] * bottom_ref[...]).astype(jnp.float32)
    dep_lon = lon_edge(east_ref[groups], west_ref[groups], 0)
    dep_xm = xs(dep, dep_lon, -1)
    dep_xp = xs(dep, dep_lon, 1)
    zero = jnp.zeros((rows, cols), jnp.float32)

    def group_body(g, carry):
        tile_e = east_ref[g]
        tile_w = west_ref[g]
        for j in range(GROUP):
            cum_xm, cum_xp = carry
            k = g * GROUP + j
            kf = k.astype(jnp.float32)
            h = h_ref[k]
            zmid = zmid_ref[k]
            w0 = (kf < dep).astype(jnp.float32)
            wxm = (kf < dep_xm).astype(jnp.float32)
            wxp = (kf < dep_xp).astype(jnp.float32)
            q = [r[k] * w0 for r in (t_ref, s_ref, u_ref, v_ref)]
            ex = [lon_edge(tile_e, tile_w, j * 4 + c) for c in range(4)]
            xsh = {s: [xs(q[c], ex[c], s) for c in range(4)] for s in (-2, -1, 1, 2)}
            a_r = 0.5 * (q[2] + xsh[1][2]) * w0 * wxp
            a_l = 0.5 * (xsh[-1][2] + q[2]) * wxm * w0
            w_r = face_weights(a_r)
            w_l = face_weights(a_l)
            for c in range(4):
                divx_ref[c * layers + k] = q[c] - courant * flux_divergence(
                    w_r, w_l, xsh[-2][c], xsh[-1][c], q[c], xsh[1][c], xsh[2][c]
                )
            load_xm = density(xsh[-1][0], xsh[-1][1], zmid) * wxm * h
            load_xp = density(xsh[1][0], xsh[1][1], zmid) * wxp * h
            cum_xm = cum_xm + load_xm
            cum_xp = cum_xp + load_xp
            gradx_ref[k] = 0.5 * ((cum_xp - 0.5 * load_xp) - (cum_xm - 0.5 * load_xm))
            carry = (cum_xm, cum_xp)
        return carry

    lax.fori_loop(0, groups, group_body, (zero, zero))


def step_kernel(
    lat_ref, h_ref, inv_h_ref, zmid_ref, inv_sp_ref,
    shore_ref, bottom_ref, flux_ref, t_ref, s_ref, u_ref, v_ref,
    south_ref, north_ref, fold_ref, divx_ref, gradx_ref,
    o0_ref, o1_ref, o2_ref, o3_ref,
    star_scr, r_scr, rs_scr,
):
    layers = t_ref.shape[0]
    rows, cols = t_ref.shape[1], t_ref.shape[2]
    groups = layers // GROUP
    lane = lax.broadcasted_iota(jnp.int32, (rows, cols), 1)
    row = lax.broadcasted_iota(jnp.int32, (rows, cols), 0)

    def ys(v, e, s):
        if s == 1:
            return pltpu.roll(jnp.where(row == 0, e, v), rows - 1, 0)
        if s == 2:
            return pltpu.roll(jnp.where(row < 2, e, v), rows - 2, 0)
        if s == -1:
            return pltpu.roll(jnp.where(row == rows - 1, e, v), 1, 0)
        return pltpu.roll(jnp.where(row >= rows - 2, e, v), 2, 0)

    def lat_edge(tile_n, tile_s, c):
        return jnp.where(row < 4, rolled(tile_n, -2 * c, 0), rolled(tile_s, rows - 2 - 2 * c, 0))

    dep = (shore_ref[...] * bottom_ref[...]).astype(jnp.float32)
    dep_lat = lat_edge(north_ref[layers] + fold_ref[layers], south_ref[layers], 0)
    dep_ym = ys(dep, dep_lat, -1)
    dep_yp = ys(dep, dep_lat, 1)
    total_rows = rows * lat_ref[1]
    row_ids = (lat_ref[0] * rows + row).astype(jnp.float32)
    turning = coriolis * (2.0 * (row_ids + 0.5) / total_rows.astype(jnp.float32) - 1.0)
    zero = jnp.zeros((rows, cols), jnp.float32)

    def explicit(k, carry):
        cum_ym, cum_yp = carry
        kf = k.astype(jnp.float32)
        h = h_ref[k]
        zmid = zmid_ref[k]
        w0 = (kf < dep).astype(jnp.float32)
        wym = (kf < dep_ym).astype(jnp.float32)
        wyp = (kf < dep_yp).astype(jnp.float32)
        q = [r[k] * w0 for r in (t_ref, s_ref, u_ref, v_ref)]
        tile_n = north_ref[k] + fold_ref[k]
        tile_s = south_ref[k]
        ey = [lat_edge(tile_n, tile_s, c) for c in range(4)]
        ysh = {s: [ys(q[c], ey[c], s) for c in range(4)] for s in (-2, -1, 1, 2)}
        b_r = 0.5 * (q[3] + ysh[1][3]) * w0 * wyp
        b_l = 0.5 * (ysh[-1][3] + q[3]) * wym * w0
        w_r = face_weights(b_r)
        w_l = face_weights(b_l)
        adv = []
        for c in range(4):
            div_y = flux_divergence(w_r, w_l, ysh[-2][c], ysh[-1][c], q[c], ysh[1][c], ysh[2][c])
            adv.append(divx_ref[c * layers + k] - courant * div_y)
        load_ym = density(ysh[-1][0], ysh[-1][1], zmid) * wym * h
        load_yp = density(ysh[1][0], ysh[1][1], zmid) * wyp * h
        cum_ym = cum_ym + load_ym
        cum_yp = cum_yp + load_yp
        grad_x = gradx_ref[k]
        grad_y = 0.5 * ((cum_yp - 0.5 * load_yp) - (cum_ym - 0.5 * load_ym))
        star0 = adv[0] * w0
        star1 = adv[1] * w0
        star2 = (adv[2] + time_step * (turning * q[3] - gravity * grad_x)) * w0
        star3 = (adv[3] + time_step * (-turning * q[2] - gravity * grad_y)) * w0
        for c, val in enumerate((star0, star1, star2, star3)):
            star_scr[c * layers + k] = val
        rs_scr[k] = density(star0, star1, zmid)
        return (cum_ym, cum_yp)

    lag = 3
    carry_e = lax.fori_loop(0, lag, explicit, (zero, zero))

    surface_scale = surface_gain * inv_h_ref[0]
    w_top = (0.0 < dep).astype(jnp.float32)
    for c in range(4):
        star_scr[c * layers] = star_scr[c * layers] + flux_ref[c] * w_top * surface_scale

    def forward(k, carry):
        mix_prev, r_a, r_b, s0, s1, s2, s3 = carry
        kf = k.astype(jnp.float32)
        inv_h = inv_h_ref[k]
        nxt = jnp.minimum(k + 1, layers - 1)
        stratified = (rs_scr[nxt] - rs_scr[k]) * inv_sp_ref[k]
        sig = 1.0 / (1.0 + jnp.exp(stratified * (1.0 / strat_scale)))
        w_next = (kf + 1.0 < dep).astype(jnp.float32)
        mix = (mix_back + mix_conv * sig) * w_next
        mix = jnp.where(k < layers - 1, mix, 0.0)
        low_a = -mix_prev * inv_h
        up_a = -mix * inv_h
        cen_a = 1.0 - low_a - up_a
        low_b = -mix_prev * momentum_mix * inv_h
        up_b = -mix * momentum_mix * inv_h
        floor = (kf == dep - 1.0).astype(jnp.float32)
        cen_b = 1.0 - low_b - up_b + bottom_drag * floor * inv_h
        inv_a = 1.0 / (cen_a - low_a * r_a)
        inv_b = 1.0 / (cen_b - low_b * r_b)
        r_a = up_a * inv_a
        r_b = up_b * inv_b
        r_scr[k] = r_a
        r_scr[layers + k] = r_b
        s0 = (star_scr[k] - low_a * s0) * inv_a
        s1 = (star_scr[layers + k] - low_a * s1) * inv_a
        s2 = (star_scr[2 * layers + k] - low_b * s2) * inv_b
        s3 = (star_scr[3 * layers + k] - low_b * s3) * inv_b
        star_scr[k] = s0
        star_scr[layers + k] = s1
        star_scr[2 * layers + k] = s2
        star_scr[3 * layers + k] = s3
        return (mix, r_a, r_b, s0, s1, s2, s3)

    def fused(k, carry):
        carry_e, carry_f = carry
        return (explicit(k, carry_e), forward(k - lag, carry_f))

    _, carry_f = lax.fori_loop(lag, layers, fused, (carry_e, (zero,) * 7), unroll=6)
    lax.fori_loop(layers - lag, layers, forward, carry_f)

    def backward(i, carry):
        x0, x1, x2, x3 = carry
        k = layers - 1 - i
        r_a = r_scr[k]
        r_b = r_scr[layers + k]
        x0 = star_scr[k] - r_a * x0
        x1 = star_scr[layers + k] - r_a * x1
        x2 = star_scr[2 * layers + k] - r_b * x2
        x3 = star_scr[3 * layers + k] - r_b * x3
        o0_ref[k] = x0
        o1_ref[k] = x1
        o2_ref[k] = x2
        o3_ref[k] = x3
        return (x0, x1, x2, x3)

    lax.fori_loop(0, layers, backward, (zero,) * 4, unroll=3)


def level_tables(layers):
    offsets = np.arange(layers, dtype=np.float32) + np.float32(0.5)
    zmid = offsets / np.float32(layers)
    thickness = np.float32(0.5) + zmid
    inverse = np.float32(1.0) / thickness
    spacing = np.float32(0.5) * (thickness[1:] + thickness[:-1])
    inv_spacing = np.concatenate([np.float32(1.0) / spacing, np.ones((1,), np.float32)])
    return [jnp.asarray(t.astype(np.float32)) for t in (thickness, inverse, zmid, inv_spacing)]


def on_device(
    heat_anomaly,
    brine_anomaly,
    eastward_current,
    northward_current,
    shoreline_indicator,
    bottom_layer_index,
    boundary_fluxes,
):
    layers, rows, cols = heat_anomaly.shape
    fields = (heat_anomaly, brine_anomaly, eastward_current, northward_current)
    groups = layers // GROUP
    n_lat = lax.axis_size("lat")
    n_lon = lax.axis_size("lon")
    lat_idx = lax.axis_index("lat").astype(jnp.int32)
    is_last = (lat_idx == n_lat - 1).astype(jnp.int32).reshape(1)
    lat_info = jnp.stack([lat_idx, jnp.int32(n_lat)])

    smem = pl.BlockSpec(memory_space=pltpu.SMEM)
    vmem = pl.BlockSpec(memory_space=pltpu.VMEM)
    row_tiles = jax.ShapeDtypeStruct((layers + 1, rows, cols), jnp.float32)
    col_tiles = jax.ShapeDtypeStruct((groups + 1, rows, cols), jnp.float32)
    top, bot, right, left = pl.pallas_call(
        pack_kernel,
        out_shape=(row_tiles, row_tiles, col_tiles, col_tiles),
        in_specs=[smem] + [vmem] * 6,
        out_specs=(vmem,) * 4,
        compiler_params=pltpu.CompilerParams(vmem_limit_bytes=16 * 1024 * 1024),
    )(is_last, shoreline_indicator, bottom_layer_index, *fields)

    from_south = lax.ppermute(top, "lat", [(i, i + 1) for i in range(n_lat - 1)])
    from_north = lax.ppermute(bot, "lat", [(i + 1, i) for i in range(n_lat - 1)])
    from_west = lax.ppermute(right, "lon", [(i, (i + 1) % n_lon) for i in range(n_lon)])
    from_east = lax.ppermute(left, "lon", [((i + 1) % n_lon, i) for i in range(n_lon)])
    last = (n_lat - 1) * n_lon
    fold, from_west, from_east = lax.optimization_barrier((top, from_west, from_east))
    from_fold = lax.ppermute(
        fold, ("lat", "lon"), [(last + x, last + n_lon - 1 - x) for x in range(n_lon)]
    )

    plane = jax.ShapeDtypeStruct((layers, rows, cols), jnp.float32)
    tables = level_tables(layers)
    divx, gradx = pl.pallas_call(
        xpart_kernel,
        out_shape=(jax.ShapeDtypeStruct((4 * layers, rows, cols), jnp.float32), plane),
        in_specs=[smem] * 2 + [vmem] * 8,
        out_specs=(vmem,) * 2,
        compiler_params=pltpu.CompilerParams(vmem_limit_bytes=16 * 1024 * 1024),
    )(tables[0], tables[2], shoreline_indicator, bottom_layer_index, *fields, from_west, from_east)
    outs = pl.pallas_call(
        step_kernel,
        out_shape=(plane,) * 4,
        in_specs=[smem] * 5 + [vmem] * 12,
        out_specs=(vmem,) * 4,
        scratch_shapes=[
            pltpu.VMEM((4 * layers, rows, cols), jnp.float32),
            pltpu.VMEM((2 * layers, rows, cols), jnp.float32),
            pltpu.VMEM((layers, rows, cols), jnp.float32),
        ],
        compiler_params=pltpu.CompilerParams(vmem_limit_bytes=16 * 1024 * 1024),
    )(
        lat_info, *tables,
        shoreline_indicator, bottom_layer_index, boundary_fluxes, *fields,
        from_south, from_north, from_fold, divx, gradx,
    )
    return tuple(outs)


def solution(mesh):
    in_specs = (
        P(None, "lat", "lon"),
        P(None, "lat", "lon"),
        P(None, "lat", "lon"),
        P(None, "lat", "lon"),
        P("lat", "lon"),
        P("lat", "lon"),
        P(None, "lat", "lon"),
    )
    out_specs = (
        P(None, "lat", "lon"),
        P(None, "lat", "lon"),
        P(None, "lat", "lon"),
        P(None, "lat", "lon"),
    )
    return jax.shard_map(
        on_device, mesh=mesh, in_specs=in_specs, out_specs=out_specs, check_vma=False
    )
```

```python
import numpy as np
import jax
import jax.numpy as jnp
from jax import lax
from jax.experimental import pallas as pl
from jax.experimental.pallas import tpu as pltpu
from jax.sharding import PartitionSpec as P

courant = 0.25
time_step = 0.2
gravity = 0.2
coriolis = 0.5
thermal = 0.6
thermal_sq = 0.1
haline = 0.8
mix_back = 5.0
mix_conv = 60.0
strat_scale = 2.0
momentum_mix = 2.0
bottom_drag = 1.0
surface_gain = 0.5

GROUP = 15


def density(warmth, saltiness, depth_column):
    return -thermal * warmth * (1.0 + thermal_sq * warmth + depth_column) + haline * saltiness


def face_weights(face_vel):
    return (
        0.5 * face_vel,
        jnp.maximum(face_vel, 0.0) * (1.0 / 6.0),
        jnp.minimum(face_vel, 0.0) * (1.0 / 6.0),
    )


def flux_divergence(right_w, left_w, m2, m1, q0, p1, p2):
    half_r, pos_r, neg_r = right_w
    half_l, pos_l, neg_l = left_w
    step_r = p1 - q0
    step_l = q0 - m1
    curv_0 = step_r - step_l
    curv_p = (p2 - p1) - step_r
    curv_m = step_l - (m1 - m2)
    flux_r = half_r * (q0 + p1) - (pos_r * curv_0 + neg_r * curv_p)
    flux_l = half_l * (m1 + q0) - (pos_l * curv_m + neg_l * curv_0)
    return flux_r - flux_l


def rolled(x, shift, axis):
    shift %= x.shape[axis]
    return x if shift == 0 else pltpu.roll(x, shift, axis)


def pack_kernel(
    last_ref, shore_ref, bottom_ref, t_ref, s_ref, u_ref, v_ref,
    top_ref, bot_ref, right_ref, left_ref,
):
    layers = top_ref.shape[0] - 1
    rows, cols = t_ref.shape[1], t_ref.shape[2]
    groups = layers // GROUP
    g = pl.program_id(0)
    lane = lax.broadcasted_iota(jnp.int32, (rows, cols), 1)
    row = lax.broadcasted_iota(jnp.int32, (rows, cols), 0)
    dep = (shore_ref[...] * bottom_ref[...]).astype(jnp.float32)
    zero = jnp.zeros((rows, cols), jnp.float32)

    def pack_rows(vals, first):
        out = zero
        for c, val in enumerate(vals):
            out = jnp.where((row >> 1) == c, rolled(val, 2 * c - first, 0), out)
        return out

    def group_body(g, carry):
        right = zero
        left = zero
        for j in range(GROUP):
            k = g * GROUP + j
            w = (k.astype(jnp.float32) < dep).astype(jnp.float32)
            q = [r[j] * w for r in (t_ref, s_ref, u_ref, v_ref)]
            top_ref[k] = pack_rows(q, rows - 2)
            bot_ref[k] = pack_rows(q, 0)
            for c in range(4):
                m = j * 4 + c
                slot = (lane >> 1) == m
                right = jnp.where(slot, rolled(q[c], 2 * m - (cols - 2), 1), right)
                left = jnp.where(slot, rolled(q[c], 2 * m, 1), left)
        right_ref[g] = right
        left_ref[g] = left
        return carry

    group_body(g, 0)

    @pl.when(g == groups - 1)
    def _():
        top_ref[layers] = pack_rows([dep], rows - 2)
        bot_ref[layers] = pack_rows([dep], 0)
        right_ref[groups] = jnp.where(lane < 2, rolled(dep, 2, 1), zero)
        left_ref[groups] = jnp.where(lane < 2, dep, zero)

    @pl.when(jnp.logical_and(g == groups - 1, last_ref[0] == 1))
    def _():
        tiles = top_ref[...].reshape((layers + 1) * rows, cols)
        tile_row = lax.broadcasted_iota(jnp.int32, tiles.shape, 0) % rows
        sign = jnp.where(tile_row < 4, 1.0, -1.0)
        swapped = jnp.where(
            (tile_row & 1) == 0, rolled(tiles, -1, 0), rolled(tiles, 1, 0)
        ) * sign
        src_lane = lax.broadcasted_iota(jnp.int32, (cols, cols), 0)
        dst_lane = lax.broadcasted_iota(jnp.int32, (cols, cols), 1)
        reverse = (src_lane + dst_lane == cols - 1).astype(jnp.float32)
        flipped = jnp.dot(
            swapped, reverse, precision=lax.Precision.HIGHEST,
            preferred_element_type=jnp.float32,
        )
        top_ref[...] = flipped.reshape(layers + 1, rows, cols)


def xpart_kernel(
    h_ref, zmid_ref, shore_ref, bottom_ref, t_ref, s_ref, u_ref, v_ref, west_ref, east_ref,
    divx_ref, gradx_ref,
):
    layers, rows, cols = t_ref.shape
    groups = layers // GROUP
    lane = lax.broadcasted_iota(jnp.int32, (rows, cols), 1)

    def xs(v, e, s):
        if s == 1:
            return pltpu.roll(jnp.where(lane == 0, e, v), cols - 1, 1)
        if s == 2:
            return pltpu.roll(jnp.where(lane < 2, e, v), cols - 2, 1)
        if s == -1:
            return pltpu.roll(jnp.where(lane == cols - 1, e, v), 1, 1)
        return pltpu.roll(jnp.where(lane >= cols - 2, e, v), 2, 1)

    def lon_edge(tile_e, tile_w, m):
        return jnp.where(lane < 64, rolled(tile_e, -2 * m, 1), rolled(tile_w, cols - 2 - 2 * m, 1))

    dep = (shore_ref[...] * bottom_ref[...]).astype(jnp.float32)
    dep_lon = lon_edge(east_ref[groups], west_ref[groups], 0)
    dep_xm = xs(dep, dep_lon, -1)
    dep_xp = xs(dep, dep_lon, 1)
    zero = jnp.zeros((rows, cols), jnp.float32)

    def group_body(g, carry):
        tile_e = east_ref[g]
        tile_w = west_ref[g]
        for j in range(GROUP):
            cum_xm, cum_xp = carry
            k = g * GROUP + j
            kf = k.astype(jnp.float32)
            h = h_ref[k]
            zmid = zmid_ref[k]
            w0 = (kf < dep).astype(jnp.float32)
            wxm = (kf < dep_xm).astype(jnp.float32)
            wxp = (kf < dep_xp).astype(jnp.float32)
            q = [r[k] * w0 for r in (t_ref, s_ref, u_ref, v_ref)]
            ex = [lon_edge(tile_e, tile_w, j * 4 + c) for c in range(4)]
            xsh = {s: [xs(q[c], ex[c], s) for c in range(4)] for s in (-2, -1, 1, 2)}
            a_r = 0.5 * (q[2] + xsh[1][2]) * w0 * wxp
            a_l = 0.5 * (xsh[-1][2] + q[2]) * wxm * w0
            w_r = face_weights(a_r)
            w_l = face_weights(a_l)
            for c in range(4):
                divx_ref[c * layers + k] = q[c] - courant * flux_divergence(
                    w_r, w_l, xsh[-2][c], xsh[-1][c], q[c], xsh[1][c], xsh[2][c]
                )
            load_xm = density(xsh[-1][0], xsh[-1][1], zmid) * wxm * h
            load_xp = density(xsh[1][0], xsh[1][1], zmid) * wxp * h
            cum_xm = cum_xm + load_xm
            cum_xp = cum_xp + load_xp
            gradx_ref[k] = 0.5 * ((cum_xp - 0.5 * load_xp) - (cum_xm - 0.5 * load_xm))
            carry = (cum_xm, cum_xp)
        return carry

    lax.fori_loop(0, groups, group_body, (zero, zero))


def step_kernel(
    lat_ref, h_ref, inv_h_ref, zmid_ref, inv_sp_ref,
    shore_ref, bottom_ref, flux_ref, t_ref, s_ref, u_ref, v_ref,
    south_ref, north_ref, fold_ref, divx_ref, gradx_ref,
    o0_ref, o1_ref, o2_ref, o3_ref,
    star_scr, r_scr, rs_scr,
):
    layers = t_ref.shape[0]
    rows, cols = t_ref.shape[1], t_ref.shape[2]
    groups = layers // GROUP
    lane = lax.broadcasted_iota(jnp.int32, (rows, cols), 1)
    row = lax.broadcasted_iota(jnp.int32, (rows, cols), 0)

    def ys(v, e, s):
        if s == 1:
            return pltpu.roll(jnp.where(row == 0, e, v), rows - 1, 0)
        if s == 2:
            return pltpu.roll(jnp.where(row < 2, e, v), rows - 2, 0)
        if s == -1:
            return pltpu.roll(jnp.where(row == rows - 1, e, v), 1, 0)
        return pltpu.roll(jnp.where(row >= rows - 2, e, v), 2, 0)

    def lat_edge(tile_n, tile_s, c):
        return jnp.where(row < 4, rolled(tile_n, -2 * c, 0), rolled(tile_s, rows - 2 - 2 * c, 0))

    dep = (shore_ref[...] * bottom_ref[...]).astype(jnp.float32)
    dep_lat = lat_edge(north_ref[layers] + fold_ref[layers], south_ref[layers], 0)
    dep_ym = ys(dep, dep_lat, -1)
    dep_yp = ys(dep, dep_lat, 1)
    total_rows = rows * lat_ref[1]
    row_ids = (lat_ref[0] * rows + row).astype(jnp.float32)
    turning = coriolis * (2.0 * (row_ids + 0.5) / total_rows.astype(jnp.float32) - 1.0)
    zero = jnp.zeros((rows, cols), jnp.float32)

    def explicit(k, carry):
        cum_ym, cum_yp = carry
        kf = k.astype(jnp.float32)
        h = h_ref[k]
        zmid = zmid_ref[k]
        w0 = (kf < dep).astype(jnp.float32)
        wym = (kf < dep_ym).astype(jnp.float32)
        wyp = (kf < dep_yp).astype(jnp.float32)
        q = [r[k] * w0 for r in (t_ref, s_ref, u_ref, v_ref)]
        tile_n = north_ref[k] + fold_ref[k]
        tile_s = south_ref[k]
        ey = [lat_edge(tile_n, tile_s, c) for c in range(4)]
        ysh = {s: [ys(q[c], ey[c], s) for c in range(4)] for s in (-2, -1, 1, 2)}
        b_r = 0.5 * (q[3] + ysh[1][3]) * w0 * wyp
        b_l = 0.5 * (ysh[-1][3] + q[3]) * wym * w0
        w_r = face_weights(b_r)
        w_l = face_weights(b_l)
        adv = []
        for c in range(4):
            div_y = flux_divergence(w_r, w_l, ysh[-2][c], ysh[-1][c], q[c], ysh[1][c], ysh[2][c])
            adv.append(divx_ref[c * layers + k] - courant * div_y)
        load_ym = density(ysh[-1][0], ysh[-1][1], zmid) * wym * h
        load_yp = density(ysh[1][0], ysh[1][1], zmid) * wyp * h
        cum_ym = cum_ym + load_ym
        cum_yp = cum_yp + load_yp
        grad_x = gradx_ref[k]
        grad_y = 0.5 * ((cum_yp - 0.5 * load_yp) - (cum_ym - 0.5 * load_ym))
        star0 = adv[0] * w0
        star1 = adv[1] * w0
        star2 = (adv[2] + time_step * (turning * q[3] - gravity * grad_x)) * w0
        star3 = (adv[3] + time_step * (-turning * q[2] - gravity * grad_y)) * w0
        for c, val in enumerate((star0, star1, star2, star3)):
            star_scr[c * layers + k] = val
        rs_scr[k] = density(star0, star1, zmid)
        return (cum_ym, cum_yp)

    lag = 3
    carry_e = lax.fori_loop(0, lag, explicit, (zero, zero))

    surface_scale = surface_gain * inv_h_ref[0]
    w_top = (0.0 < dep).astype(jnp.float32)
    for c in range(4):
        star_scr[c * layers] = star_scr[c * layers] + flux_ref[c] * w_top * surface_scale

    def forward(k, carry):
        mix_prev, r_a, r_b, s0, s1, s2, s3 = carry
        kf = k.astype(jnp.float32)
        inv_h = inv_h_ref[k]
        nxt = jnp.minimum(k + 1, layers - 1)
        stratified = (rs_scr[nxt] - rs_scr[k]) * inv_sp_ref[k]
        sig = 1.0 / (1.0 + jnp.exp(stratified * (1.0 / strat_scale)))
        w_next = (kf + 1.0 < dep).astype(jnp.float32)
        mix = (mix_back + mix_conv * sig) * w_next
        mix = jnp.where(k < layers - 1, mix, 0.0)
        low_a = -mix_prev * inv_h
        up_a = -mix * inv_h
        cen_a = 1.0 - low_a - up_a
        low_b = -mix_prev * momentum_mix * inv_h
        up_b = -mix * momentum_mix * inv_h
        floor = (kf == dep - 1.0).astype(jnp.float32)
        cen_b = 1.0 - low_b - up_b + bottom_drag * floor * inv_h
        inv_a = 1.0 / (cen_a - low_a * r_a)
        inv_b = 1.0 / (cen_b - low_b * r_b)
        r_a = up_a * inv_a
        r_b = up_b * inv_b
        r_scr[k] = r_a
        r_scr[layers + k] = r_b
        s0 = (star_scr[k] - low_a * s0) * inv_a
        s1 = (star_scr[layers + k] - low_a * s1) * inv_a
        s2 = (star_scr[2 * layers + k] - low_b * s2) * inv_b
        s3 = (star_scr[3 * layers + k] - low_b * s3) * inv_b
        star_scr[k] = s0
        star_scr[layers + k] = s1
        star_scr[2 * layers + k] = s2
        star_scr[3 * layers + k] = s3
        return (mix, r_a, r_b, s0, s1, s2, s3)

    def fused(k, carry):
        carry_e, carry_f = carry
        return (explicit(k, carry_e), forward(k - lag, carry_f))

    _, carry_f = lax.fori_loop(lag, layers, fused, (carry_e, (zero,) * 7), unroll=6)
    lax.fori_loop(layers - lag, layers, forward, carry_f)

    def backward(i, carry):
        x0, x1, x2, x3 = carry
        k = layers - 1 - i
        r_a = r_scr[k]
        r_b = r_scr[layers + k]
        x0 = star_scr[k] - r_a * x0
        x1 = star_scr[layers + k] - r_a * x1
        x2 = star_scr[2 * layers + k] - r_b * x2
        x3 = star_scr[3 * layers + k] - r_b * x3
        o0_ref[k] = x0
        o1_ref[k] = x1
        o2_ref[k] = x2
        o3_ref[k] = x3
        return (x0, x1, x2, x3)

    lax.fori_loop(0, layers, backward, (zero,) * 4, unroll=3)


def level_tables(layers):
    offsets = np.arange(layers, dtype=np.float32) + np.float32(0.5)
    zmid = offsets / np.float32(layers)
    thickness = np.float32(0.5) + zmid
    inverse = np.float32(1.0) / thickness
    spacing = np.float32(0.5) * (thickness[1:] + thickness[:-1])
    inv_spacing = np.concatenate([np.float32(1.0) / spacing, np.ones((1,), np.float32)])
    return [jnp.asarray(t.astype(np.float32)) for t in (thickness, inverse, zmid, inv_spacing)]


def on_device(
    heat_anomaly,
    brine_anomaly,
    eastward_current,
    northward_current,
    shoreline_indicator,
    bottom_layer_index,
    boundary_fluxes,
):
    layers, rows, cols = heat_anomaly.shape
    fields = (heat_anomaly, brine_anomaly, eastward_current, northward_current)
    groups = layers // GROUP
    n_lat = lax.axis_size("lat")
    n_lon = lax.axis_size("lon")
    lat_idx = lax.axis_index("lat").astype(jnp.int32)
    is_last = (lat_idx == n_lat - 1).astype(jnp.int32).reshape(1)
    lat_info = jnp.stack([lat_idx, jnp.int32(n_lat)])

    smem = pl.BlockSpec(memory_space=pltpu.SMEM)
    vmem = pl.BlockSpec(memory_space=pltpu.VMEM)
    row_tiles = jax.ShapeDtypeStruct((layers + 1, rows, cols), jnp.float32)
    col_tiles = jax.ShapeDtypeStruct((groups + 1, rows, cols), jnp.float32)
    level_block = pl.BlockSpec((GROUP, rows, cols), lambda g: (g, 0, 0))
    plane_block = pl.BlockSpec((rows, cols), lambda g: (0, 0))
    row_block = pl.BlockSpec((layers + 1, rows, cols), lambda g: (0, 0, 0))
    col_block = pl.BlockSpec((groups + 1, rows, cols), lambda g: (0, 0, 0))
    top, bot, right, left = pl.pallas_call(
        pack_kernel,
        out_shape=(row_tiles, row_tiles, col_tiles, col_tiles),
        grid=(groups,),
        in_specs=[smem, plane_block, plane_block] + [level_block] * 4,
        out_specs=(row_block, row_block, col_block, col_block),
    )(is_last, shoreline_indicator, bottom_layer_index, *fields)

    from_south = lax.ppermute(top, "lat", [(i, i + 1) for i in range(n_lat - 1)])
    from_north = lax.ppermute(bot, "lat", [(i + 1, i) for i in range(n_lat - 1)])
    from_west = lax.ppermute(right, "lon", [(i, (i + 1) % n_lon) for i in range(n_lon)])
    from_east = lax.ppermute(left, "lon", [((i + 1) % n_lon, i) for i in range(n_lon)])
    last = (n_lat - 1) * n_lon
    fold, from_west, from_east = lax.optimization_barrier((top, from_west, from_east))
    from_fold = lax.ppermute(
        fold, ("lat", "lon"), [(last + x, last + n_lon - 1 - x) for x in range(n_lon)]
    )

    plane = jax.ShapeDtypeStruct((layers, rows, cols), jnp.float32)
    tables = level_tables(layers)
    divx, gradx = pl.pallas_call(
        xpart_kernel,
        out_shape=(jax.ShapeDtypeStruct((4 * layers, rows, cols), jnp.float32), plane),
        in_specs=[smem] * 2 + [vmem] * 8,
        out_specs=(vmem,) * 2,
        compiler_params=pltpu.CompilerParams(vmem_limit_bytes=16 * 1024 * 1024),
    )(tables[0], tables[2], shoreline_indicator, bottom_layer_index, *fields, from_west, from_east)
    outs = pl.pallas_call(
        step_kernel,
        out_shape=(plane,) * 4,
        in_specs=[smem] * 5 + [vmem] * 12,
        out_specs=(vmem,) * 4,
        scratch_shapes=[
            pltpu.VMEM((4 * layers, rows, cols), jnp.float32),
            pltpu.VMEM((2 * layers, rows, cols), jnp.float32),
            pltpu.VMEM((layers, rows, cols), jnp.float32),
        ],
        compiler_params=pltpu.CompilerParams(vmem_limit_bytes=16 * 1024 * 1024),
    )(
        lat_info, *tables,
        shoreline_indicator, bottom_layer_index, boundary_fluxes, *fields,
        from_south, from_north, from_fold, divx, gradx,
    )
    return tuple(outs)


def solution(mesh):
    in_specs = (
        P(None, "lat", "lon"),
        P(None, "lat", "lon"),
        P(None, "lat", "lon"),
        P(None, "lat", "lon"),
        P("lat", "lon"),
        P("lat", "lon"),
        P(None, "lat", "lon"),
    )
    out_specs = (
        P(None, "lat", "lon"),
        P(None, "lat", "lon"),
        P(None, "lat", "lon"),
        P(None, "lat", "lon"),
    )
    return jax.shard_map(
        on_device, mesh=mesh, in_specs=in_specs, out_specs=out_specs, check_vma=False
    )
```

```python
import numpy as np
import jax
import jax.numpy as jnp
from jax import lax
from jax.experimental import pallas as pl
from jax.experimental.pallas import tpu as pltpu
from jax.sharding import PartitionSpec as P

courant = 0.25
time_step = 0.2
gravity = 0.2
coriolis = 0.5
thermal = 0.6
thermal_sq = 0.1
haline = 0.8
mix_back = 5.0
mix_conv = 60.0
strat_scale = 2.0
momentum_mix = 2.0
bottom_drag = 1.0
surface_gain = 0.5

GROUP = 15


def density(warmth, saltiness, depth_column):
    return -thermal * warmth * (1.0 + thermal_sq * warmth + depth_column) + haline * saltiness


def face_weights(face_vel):
    return (
        0.5 * face_vel,
        jnp.maximum(face_vel, 0.0) * (1.0 / 6.0),
        jnp.minimum(face_vel, 0.0) * (1.0 / 6.0),
    )


def flux_divergence(right_w, left_w, m2, m1, q0, p1, p2):
    half_r, pos_r, neg_r = right_w
    half_l, pos_l, neg_l = left_w
    step_r = p1 - q0
    step_l = q0 - m1
    curv_0 = step_r - step_l
    curv_p = (p2 - p1) - step_r
    curv_m = step_l - (m1 - m2)
    flux_r = half_r * (q0 + p1) - (pos_r * curv_0 + neg_r * curv_p)
    flux_l = half_l * (m1 + q0) - (pos_l * curv_m + neg_l * curv_0)
    return flux_r - flux_l


def rolled(x, shift, axis):
    shift %= x.shape[axis]
    return x if shift == 0 else pltpu.roll(x, shift, axis)


def pack_kernel(
    last_ref, shore_ref, bottom_ref, t_ref, s_ref, u_ref, v_ref,
    top_ref, bot_ref, right_ref, left_ref,
):
    layers, rows, cols = t_ref.shape
    groups = layers // GROUP
    lane = lax.broadcasted_iota(jnp.int32, (rows, cols), 1)
    row = lax.broadcasted_iota(jnp.int32, (rows, cols), 0)
    dep = (shore_ref[...] * bottom_ref[...]).astype(jnp.float32)
    zero = jnp.zeros((rows, cols), jnp.float32)

    def pack_rows(vals, first):
        out = zero
        for c, val in enumerate(vals):
            out = jnp.where((row >> 1) == c, rolled(val, 2 * c - first, 0), out)
        return out

    def group_body(g, carry):
        right = zero
        left = zero
        for j in range(GROUP):
            k = g * GROUP + j
            w = (k.astype(jnp.float32) < dep).astype(jnp.float32)
            q = [r[k] * w for r in (t_ref, s_ref, u_ref, v_ref)]
            top_ref[k] = pack_rows(q, rows - 2)
            bot_ref[k] = pack_rows(q, 0)
            for c in range(4):
                m = j * 4 + c
                slot = (lane >> 1) == m
                right = jnp.where(slot, rolled(q[c], 2 * m - (cols - 2), 1), right)
                left = jnp.where(slot, rolled(q[c], 2 * m, 1), left)
        right_ref[g] = right
        left_ref[g] = left
        return carry

    lax.fori_loop(0, groups, group_body, 0)
    top_ref[layers] = pack_rows([dep], rows - 2)
    bot_ref[layers] = pack_rows([dep], 0)
    right_ref[groups] = jnp.where(lane < 2, rolled(dep, 2, 1), zero)
    left_ref[groups] = jnp.where(lane < 2, dep, zero)

    @pl.when(last_ref[0] == 1)
    def _():
        tiles = top_ref[...].reshape((layers + 1) * rows, cols)
        tile_row = lax.broadcasted_iota(jnp.int32, tiles.shape, 0) % rows
        sign = jnp.where(tile_row < 4, 1.0, -1.0)
        swapped = jnp.where(
            (tile_row & 1) == 0, rolled(tiles, -1, 0), rolled(tiles, 1, 0)
        ) * sign
        src_lane = lax.broadcasted_iota(jnp.int32, (cols, cols), 0)
        dst_lane = lax.broadcasted_iota(jnp.int32, (cols, cols), 1)
        reverse = (src_lane + dst_lane == cols - 1).astype(jnp.float32)
        flipped = jnp.dot(
            swapped, reverse, precision=lax.Precision.HIGHEST,
            preferred_element_type=jnp.float32,
        )
        top_ref[...] = flipped.reshape(layers + 1, rows, cols)


def xpart_kernel(
    lat_ref, h_ref, zmid_ref, shore_ref, bottom_ref, t_ref, s_ref, u_ref, v_ref,
    west_ref, east_ref, divx_ref,
):
    layers, rows, cols = t_ref.shape
    groups = layers // GROUP
    lane = lax.broadcasted_iota(jnp.int32, (rows, cols), 1)
    row = lax.broadcasted_iota(jnp.int32, (rows, cols), 0)
    total_rows = rows * lat_ref[1]
    row_ids = (lat_ref[0] * rows + row).astype(jnp.float32)
    turning = coriolis * (2.0 * (row_ids + 0.5) / total_rows.astype(jnp.float32) - 1.0)

    def xs(v, e, s):
        if s == 1:
            return pltpu.roll(jnp.where(lane == 0, e, v), cols - 1, 1)
        if s == 2:
            return pltpu.roll(jnp.where(lane < 2, e, v), cols - 2, 1)
        if s == -1:
            return pltpu.roll(jnp.where(lane == cols - 1, e, v), 1, 1)
        return pltpu.roll(jnp.where(lane >= cols - 2, e, v), 2, 1)

    def lon_edge(tile_e, tile_w, m):
        return jnp.where(lane < 64, rolled(tile_e, -2 * m, 1), rolled(tile_w, cols - 2 - 2 * m, 1))

    dep = (shore_ref[...] * bottom_ref[...]).astype(jnp.float32)
    dep_lon = lon_edge(east_ref[groups], west_ref[groups], 0)
    dep_xm = xs(dep, dep_lon, -1)
    dep_xp = xs(dep, dep_lon, 1)
    zero = jnp.zeros((rows, cols), jnp.float32)

    def group_body(g, carry):
        tile_e = east_ref[g]
        tile_w = west_ref[g]
        for j in range(GROUP):
            cum_xm, cum_xp = carry
            k = g * GROUP + j
            kf = k.astype(jnp.float32)
            h = h_ref[k]
            zmid = zmid_ref[k]
            w0 = (kf < dep).astype(jnp.float32)
            wxm = (kf < dep_xm).astype(jnp.float32)
            wxp = (kf < dep_xp).astype(jnp.float32)
            q = [r[k] * w0 for r in (t_ref, s_ref, u_ref, v_ref)]
            ex = [lon_edge(tile_e, tile_w, j * 4 + c) for c in range(4)]
            xsh = {s: [xs(q[c], ex[c], s) for c in range(4)] for s in (-2, -1, 1, 2)}
            a_r = 0.5 * (q[2] + xsh[1][2]) * w0 * wxp
            a_l = 0.5 * (xsh[-1][2] + q[2]) * wxm * w0
            w_r = face_weights(a_r)
            w_l = face_weights(a_l)
            part = [
                q[c] - courant * flux_divergence(
                    w_r, w_l, xsh[-2][c], xsh[-1][c], q[c], xsh[1][c], xsh[2][c]
                )
                for c in range(4)
            ]
            load_xm = density(xsh[-1][0], xsh[-1][1], zmid) * wxm * h
            load_xp = density(xsh[1][0], xsh[1][1], zmid) * wxp * h
            cum_xm = cum_xm + load_xm
            cum_xp = cum_xp + load_xp
            grad_x = 0.5 * ((cum_xp - 0.5 * load_xp) - (cum_xm - 0.5 * load_xm))
            part[2] = part[2] + time_step * (turning * q[3] - gravity * grad_x)
            part[3] = part[3] + time_step * (-turning * q[2])
            for c in range(4):
                divx_ref[c * layers + k] = part[c]
            carry = (cum_xm, cum_xp)
        return carry

    lax.fori_loop(0, groups, group_body, (zero, zero))


def step_kernel(
    lat_ref, h_ref, inv_h_ref, zmid_ref, inv_sp_ref,
    shore_ref, bottom_ref, flux_ref, t_ref, s_ref, u_ref, v_ref,
    south_ref, north_ref, fold_ref, divx_ref,
    o0_ref, o1_ref, o2_ref, o3_ref,
    star_scr, r_scr, rs_scr,
):
    layers = t_ref.shape[0]
    rows, cols = t_ref.shape[1], t_ref.shape[2]
    groups = layers // GROUP
    lane = lax.broadcasted_iota(jnp.int32, (rows, cols), 1)
    row = lax.broadcasted_iota(jnp.int32, (rows, cols), 0)

    def ys(v, e, s):
        if s == 1:
            return pltpu.roll(jnp.where(row == 0, e, v), rows - 1, 0)
        if s == 2:
            return pltpu.roll(jnp.where(row < 2, e, v), rows - 2, 0)
        if s == -1:
            return pltpu.roll(jnp.where(row == rows - 1, e, v), 1, 0)
        return pltpu.roll(jnp.where(row >= rows - 2, e, v), 2, 0)

    def lat_edge(tile_n, tile_s, c):
        return jnp.where(row < 4, rolled(tile_n, -2 * c, 0), rolled(tile_s, rows - 2 - 2 * c, 0))

    dep = (shore_ref[...] * bottom_ref[...]).astype(jnp.float32)
    dep_lat = lat_edge(north_ref[layers] + fold_ref[layers], south_ref[layers], 0)
    dep_ym = ys(dep, dep_lat, -1)
    dep_yp = ys(dep, dep_lat, 1)
    zero = jnp.zeros((rows, cols), jnp.float32)

    def explicit(k, carry):
        cum_ym, cum_yp = carry
        kf = k.astype(jnp.float32)
        h = h_ref[k]
        zmid = zmid_ref[k]
        w0 = (kf < dep).astype(jnp.float32)
        wym = (kf < dep_ym).astype(jnp.float32)
        wyp = (kf < dep_yp).astype(jnp.float32)
        q = [r[k] * w0 for r in (t_ref, s_ref, u_ref, v_ref)]
        tile_n = north_ref[k] + fold_ref[k]
        tile_s = south_ref[k]
        ey = [lat_edge(tile_n, tile_s, c) for c in range(4)]
        ysh = {s: [ys(q[c], ey[c], s) for c in range(4)] for s in (-2, -1, 1, 2)}
        b_r = 0.5 * (q[3] + ysh[1][3]) * w0 * wyp
        b_l = 0.5 * (ysh[-1][3] + q[3]) * wym * w0
        w_r = face_weights(b_r)
        w_l = face_weights(b_l)
        adv = []
        for c in range(4):
            div_y = flux_divergence(w_r, w_l, ysh[-2][c], ysh[-1][c], q[c], ysh[1][c], ysh[2][c])
            adv.append(divx_ref[c * layers + k] - courant * div_y)
        load_ym = density(ysh[-1][0], ysh[-1][1], zmid) * wym * h
        load_yp = density(ysh[1][0], ysh[1][1], zmid) * wyp * h
        cum_ym = cum_ym + load_ym
        cum_yp = cum_yp + load_yp
        grad_y = 0.5 * ((cum_yp - 0.5 * load_yp) - (cum_ym - 0.5 * load_ym))
        star0 = adv[0] * w0
        star1 = adv[1] * w0
        star2 = adv[2] * w0
        star3 = (adv[3] - time_step * gravity * grad_y) * w0
        for c, val in enumerate((star0, star1, star2, star3)):
            star_scr[c * layers + k] = val
        rs_scr[k] = density(star0, star1, zmid)
        return (cum_ym, cum_yp)

    lag = 3
    carry_e = lax.fori_loop(0, lag, explicit, (zero, zero))

    surface_scale = surface_gain * inv_h_ref[0]
    w_top = (0.0 < dep).astype(jnp.float32)
    for c in range(4):
        star_scr[c * layers] = star_scr[c * layers] + flux_ref[c] * w_top * surface_scale

    def forward(k, carry):
        mix_prev, r_a, r_b, s0, s1, s2, s3 = carry
        kf = k.astype(jnp.float32)
        inv_h = inv_h_ref[k]
        nxt = jnp.minimum(k + 1, layers - 1)
        stratified = (rs_scr[nxt] - rs_scr[k]) * inv_sp_ref[k]
        sig = 1.0 / (1.0 + jnp.exp(stratified * (1.0 / strat_scale)))
        w_next = (kf + 1.0 < dep).astype(jnp.float32)
        mix = (mix_back + mix_conv * sig) * w_next
        mix = jnp.where(k < layers - 1, mix, 0.0)
        low_a = -mix_prev * inv_h
        up_a = -mix * inv_h
        cen_a = 1.0 - low_a - up_a
        low_b = -mix_prev * momentum_mix * inv_h
        up_b = -mix * momentum_mix * inv_h
        floor = (kf == dep - 1.0).astype(jnp.float32)
        cen_b = 1.0 - low_b - up_b + bottom_drag * floor * inv_h
        inv_a = 1.0 / (cen_a - low_a * r_a)
        inv_b = 1.0 / (cen_b - low_b * r_b)
        r_a = up_a * inv_a
        r_b = up_b * inv_b
        r_scr[k] = r_a
        r_scr[layers + k] = r_b
        s0 = (star_scr[k] - low_a * s0) * inv_a
        s1 = (star_scr[layers + k] - low_a * s1) * inv_a
        s2 = (star_scr[2 * layers + k] - low_b * s2) * inv_b
        s3 = (star_scr[3 * layers + k] - low_b * s3) * inv_b
        star_scr[k] = s0
        star_scr[layers + k] = s1
        star_scr[2 * layers + k] = s2
        star_scr[3 * layers + k] = s3
        return (mix, r_a, r_b, s0, s1, s2, s3)

    def fused(k, carry):
        carry_e, carry_f = carry
        return (explicit(k, carry_e), forward(k - lag, carry_f))

    _, carry_f = lax.fori_loop(lag, layers, fused, (carry_e, (zero,) * 7), unroll=9)
    lax.fori_loop(layers - lag, layers, forward, carry_f)

    def backward(i, carry):
        x0, x1, x2, x3 = carry
        k = layers - 1 - i
        r_a = r_scr[k]
        r_b = r_scr[layers + k]
        x0 = star_scr[k] - r_a * x0
        x1 = star_scr[layers + k] - r_a * x1
        x2 = star_scr[2 * layers + k] - r_b * x2
        x3 = star_scr[3 * layers + k] - r_b * x3
        o0_ref[k] = x0
        o1_ref[k] = x1
        o2_ref[k] = x2
        o3_ref[k] = x3
        return (x0, x1, x2, x3)

    lax.fori_loop(0, layers, backward, (zero,) * 4, unroll=3)


def level_tables(layers):
    offsets = np.arange(layers, dtype=np.float32) + np.float32(0.5)
    zmid = offsets / np.float32(layers)
    thickness = np.float32(0.5) + zmid
    inverse = np.float32(1.0) / thickness
    spacing = np.float32(0.5) * (thickness[1:] + thickness[:-1])
    inv_spacing = np.concatenate([np.float32(1.0) / spacing, np.ones((1,), np.float32)])
    return [jnp.asarray(t.astype(np.float32)) for t in (thickness, inverse, zmid, inv_spacing)]


def on_device(
    heat_anomaly,
    brine_anomaly,
    eastward_current,
    northward_current,
    shoreline_indicator,
    bottom_layer_index,
    boundary_fluxes,
):
    layers, rows, cols = heat_anomaly.shape
    fields = (heat_anomaly, brine_anomaly, eastward_current, northward_current)
    groups = layers // GROUP
    n_lat = lax.axis_size("lat")
    n_lon = lax.axis_size("lon")
    lat_idx = lax.axis_index("lat").astype(jnp.int32)
    is_last = (lat_idx == n_lat - 1).astype(jnp.int32).reshape(1)
    lat_info = jnp.stack([lat_idx, jnp.int32(n_lat)])

    smem = pl.BlockSpec(memory_space=pltpu.SMEM)
    vmem = pl.BlockSpec(memory_space=pltpu.VMEM)
    row_tiles = jax.ShapeDtypeStruct((layers + 1, rows, cols), jnp.float32)
    col_tiles = jax.ShapeDtypeStruct((groups + 1, rows, cols), jnp.float32)
    top, bot, right, left = pl.pallas_call(
        pack_kernel,
        out_shape=(row_tiles, row_tiles, col_tiles, col_tiles),
        in_specs=[smem] + [vmem] * 6,
        out_specs=(vmem,) * 4,
    )(is_last, shoreline_indicator, bottom_layer_index, *fields)

    from_south = lax.ppermute(top, "lat", [(i, i + 1) for i in range(n_lat - 1)])
    from_north = lax.ppermute(bot, "lat", [(i + 1, i) for i in range(n_lat - 1)])
    from_west = lax.ppermute(right, "lon", [(i, (i + 1) % n_lon) for i in range(n_lon)])
    from_east = lax.ppermute(left, "lon", [((i + 1) % n_lon, i) for i in range(n_lon)])
    last = (n_lat - 1) * n_lon
    fold, from_west, from_east = lax.optimization_barrier((top, from_west, from_east))
    from_fold = lax.ppermute(
        fold, ("lat", "lon"), [(last + x, last + n_lon - 1 - x) for x in range(n_lon)]
    )

    plane = jax.ShapeDtypeStruct((layers, rows, cols), jnp.float32)
    tables = level_tables(layers)
    divx = pl.pallas_call(
        xpart_kernel,
        out_shape=jax.ShapeDtypeStruct((4 * layers, rows, cols), jnp.float32),
        in_specs=[smem] * 3 + [vmem] * 8,
        out_specs=vmem,
        compiler_params=pltpu.CompilerParams(vmem_limit_bytes=16 * 1024 * 1024),
    )(lat_info, tables[0], tables[2], shoreline_indicator, bottom_layer_index, *fields,
      from_west, from_east)
    outs = pl.pallas_call(
        step_kernel,
        out_shape=(plane,) * 4,
        in_specs=[smem] * 5 + [vmem] * 11,
        out_specs=(vmem,) * 4,
        scratch_shapes=[
            pltpu.VMEM((4 * layers, rows, cols), jnp.float32),
            pltpu.VMEM((2 * layers, rows, cols), jnp.float32),
            pltpu.VMEM((layers, rows, cols), jnp.float32),
        ],
        compiler_params=pltpu.CompilerParams(vmem_limit_bytes=16 * 1024 * 1024),
    )(
        lat_info, *tables,
        shoreline_indicator, bottom_layer_index, boundary_fluxes, *fields,
        from_south, from_north, from_fold, divx,
    )
    return tuple(outs)


def solution(mesh):
    in_specs = (
        P(None, "lat", "lon"),
        P(None, "lat", "lon"),
        P(None, "lat", "lon"),
        P(None, "lat", "lon"),
        P("lat", "lon"),
        P("lat", "lon"),
        P(None, "lat", "lon"),
    )
    out_specs = (
        P(None, "lat", "lon"),
        P(None, "lat", "lon"),
        P(None, "lat", "lon"),
        P(None, "lat", "lon"),
    )
    return jax.shard_map(
        on_device, mesh=mesh, in_specs=in_specs, out_specs=out_specs, check_vma=False
    )
```

```python
import numpy as np
import jax
import jax.numpy as jnp
from jax import lax
from jax.experimental import pallas as pl
from jax.experimental.pallas import tpu as pltpu
from jax.sharding import PartitionSpec as P

courant = 0.25
time_step = 0.2
gravity = 0.2
coriolis = 0.5
thermal = 0.6
thermal_sq = 0.1
haline = 0.8
mix_back = 5.0
mix_conv = 60.0
strat_scale = 2.0
momentum_mix = 2.0
bottom_drag = 1.0
surface_gain = 0.5

GROUP = 15


def density(warmth, saltiness, depth_column):
    return -thermal * warmth * (1.0 + thermal_sq * warmth + depth_column) + haline * saltiness


def face_weights(face_vel):
    return (
        0.5 * face_vel,
        jnp.maximum(face_vel, 0.0) * (1.0 / 6.0),
        jnp.minimum(face_vel, 0.0) * (1.0 / 6.0),
    )


def flux_divergence(right_w, left_w, m2, m1, q0, p1, p2):
    half_r, pos_r, neg_r = right_w
    half_l, pos_l, neg_l = left_w
    step_r = p1 - q0
    step_l = q0 - m1
    curv_0 = step_r - step_l
    curv_p = (p2 - p1) - step_r
    curv_m = step_l - (m1 - m2)
    flux_r = half_r * (q0 + p1) - (pos_r * curv_0 + neg_r * curv_p)
    flux_l = half_l * (m1 + q0) - (pos_l * curv_m + neg_l * curv_0)
    return flux_r - flux_l


def rolled(x, shift, axis):
    shift %= x.shape[axis]
    return x if shift == 0 else pltpu.roll(x, shift, axis)


def pack_kernel(
    last_ref, shore_ref, bottom_ref, t_ref, s_ref, u_ref, v_ref,
    top_ref, bot_ref, right_ref, left_ref,
):
    layers, rows, cols = t_ref.shape
    groups = layers // GROUP
    lane = lax.broadcasted_iota(jnp.int32, (rows, cols), 1)
    row = lax.broadcasted_iota(jnp.int32, (rows, cols), 0)
    dep = (shore_ref[...] * bottom_ref[...]).astype(jnp.float32)
    zero = jnp.zeros((rows, cols), jnp.float32)

    def pack_rows(vals, first):
        out = zero
        for c, val in enumerate(vals):
            out = jnp.where((row >> 1) == c, rolled(val, 2 * c - first, 0), out)
        return out

    def group_body(g, carry):
        right = zero
        left = zero
        for j in range(GROUP):
            k = g * GROUP + j
            w = (k.astype(jnp.float32) < dep).astype(jnp.float32)
            q = [r[k] * w for r in (t_ref, s_ref, u_ref, v_ref)]
            top_ref[k] = pack_rows(q, rows - 2)
            bot_ref[k] = pack_rows(q, 0)
            for c in range(4):
                m = j * 4 + c
                slot = (lane >> 1) == m
                right = jnp.where(slot, rolled(q[c], 2 * m - (cols - 2), 1), right)
                left = jnp.where(slot, rolled(q[c], 2 * m, 1), left)
        right_ref[g] = right
        left_ref[g] = left
        return carry

    lax.fori_loop(0, groups, group_body, 0)
    top_ref[layers] = pack_rows([dep], rows - 2)
    bot_ref[layers] = pack_rows([dep], 0)
    right_ref[groups] = jnp.where(lane < 2, rolled(dep, 2, 1), zero)
    left_ref[groups] = jnp.where(lane < 2, dep, zero)

    @pl.when(last_ref[0] == 1)
    def _():
        tiles = top_ref[...].reshape((layers + 1) * rows, cols)
        tile_row = lax.broadcasted_iota(jnp.int32, tiles.shape, 0) % rows
        sign = jnp.where(tile_row < 4, 1.0, -1.0)
        swapped = jnp.where(
            (tile_row & 1) == 0, rolled(tiles, -1, 0), rolled(tiles, 1, 0)
        ) * sign
        src_lane = lax.broadcasted_iota(jnp.int32, (cols, cols), 0)
        dst_lane = lax.broadcasted_iota(jnp.int32, (cols, cols), 1)
        reverse = (src_lane + dst_lane == cols - 1).astype(jnp.float32)
        flipped = jnp.dot(
            swapped, reverse, precision=lax.Precision.HIGHEST,
            preferred_element_type=jnp.float32,
        )
        top_ref[...] = flipped.reshape(layers + 1, rows, cols)


def xpart_kernel(
    lat_ref, h_ref, zmid_ref, shore_ref, bottom_ref, t_ref, s_ref, u_ref, v_ref,
    west_ref, east_ref, divx_ref,
):
    layers, rows, cols = t_ref.shape
    groups = layers // GROUP
    lane = lax.broadcasted_iota(jnp.int32, (rows, cols), 1)
    row = lax.broadcasted_iota(jnp.int32, (rows, cols), 0)
    total_rows = rows * lat_ref[1]
    row_ids = (lat_ref[0] * rows + row).astype(jnp.float32)
    turning = coriolis * (2.0 * (row_ids + 0.5) / total_rows.astype(jnp.float32) - 1.0)

    def xs(v, e, s):
        if s == 1:
            return pltpu.roll(jnp.where(lane == 0, e, v), cols - 1, 1)
        if s == 2:
            return pltpu.roll(jnp.where(lane < 2, e, v), cols - 2, 1)
        if s == -1:
            return pltpu.roll(jnp.where(lane == cols - 1, e, v), 1, 1)
        return pltpu.roll(jnp.where(lane >= cols - 2, e, v), 2, 1)

    def lon_edge(tile_e, tile_w, m):
        return jnp.where(lane < 64, rolled(tile_e, -2 * m, 1), rolled(tile_w, cols - 2 - 2 * m, 1))

    dep = (shore_ref[...] * bottom_ref[...]).astype(jnp.float32)
    dep_lon = lon_edge(east_ref[groups], west_ref[groups], 0)
    dep_xm = xs(dep, dep_lon, -1)
    dep_xp = xs(dep, dep_lon, 1)
    zero = jnp.zeros((rows, cols), jnp.float32)

    def group_body(g, carry):
        tile_e = east_ref[g]
        tile_w = west_ref[g]
        for j in range(GROUP):
            cum_xm, cum_xp = carry
            k = g * GROUP + j
            kf = k.astype(jnp.float32)
            h = h_ref[k]
            zmid = zmid_ref[k]
            w0 = (kf < dep).astype(jnp.float32)
            wxm = (kf < dep_xm).astype(jnp.float32)
            wxp = (kf < dep_xp).astype(jnp.float32)
            q = [r[k] * w0 for r in (t_ref, s_ref, u_ref, v_ref)]
            ex = [lon_edge(tile_e, tile_w, j * 4 + c) for c in range(4)]
            xsh = {s: [xs(q[c], ex[c], s) for c in range(4)] for s in (-2, -1, 1, 2)}
            a_r = 0.5 * (q[2] + xsh[1][2]) * w0 * wxp
            a_l = 0.5 * (xsh[-1][2] + q[2]) * wxm * w0
            w_r = face_weights(a_r)
            w_l = face_weights(a_l)
            part = [
                q[c] - courant * flux_divergence(
                    w_r, w_l, xsh[-2][c], xsh[-1][c], q[c], xsh[1][c], xsh[2][c]
                )
                for c in range(4)
            ]
            load_xm = density(xsh[-1][0], xsh[-1][1], zmid) * wxm * h
            load_xp = density(xsh[1][0], xsh[1][1], zmid) * wxp * h
            cum_xm = cum_xm + load_xm
            cum_xp = cum_xp + load_xp
            grad_x = 0.5 * ((cum_xp - 0.5 * load_xp) - (cum_xm - 0.5 * load_xm))
            part[2] = part[2] + time_step * (turning * q[3] - gravity * grad_x)
            part[3] = part[3] + time_step * (-turning * q[2])
            for c in range(4):
                divx_ref[c * layers + k] = part[c]
            carry = (cum_xm, cum_xp)
        return carry

    lax.fori_loop(0, groups, group_body, (zero, zero))


def step_kernel(
    lat_ref, h_ref, inv_h_ref, zmid_ref, inv_sp_ref,
    shore_ref, bottom_ref, flux_ref, t_ref, s_ref, u_ref, v_ref,
    south_ref, north_ref, fold_ref, divx_ref,
    o0_hbm, o1_hbm, o2_hbm, o3_hbm,
    star_scr, r_scr, rs_scr, o0_ref, o1_ref, o2_ref, o3_ref, out_sems,
):
    layers = t_ref.shape[0]
    rows, cols = t_ref.shape[1], t_ref.shape[2]
    groups = layers // GROUP
    lane = lax.broadcasted_iota(jnp.int32, (rows, cols), 1)
    row = lax.broadcasted_iota(jnp.int32, (rows, cols), 0)

    def ys(v, e, s):
        if s == 1:
            return pltpu.roll(jnp.where(row == 0, e, v), rows - 1, 0)
        if s == 2:
            return pltpu.roll(jnp.where(row < 2, e, v), rows - 2, 0)
        if s == -1:
            return pltpu.roll(jnp.where(row == rows - 1, e, v), 1, 0)
        return pltpu.roll(jnp.where(row >= rows - 2, e, v), 2, 0)

    def lat_edge(tile_n, tile_s, c):
        return jnp.where(row < 4, rolled(tile_n, -2 * c, 0), rolled(tile_s, rows - 2 - 2 * c, 0))

    dep = (shore_ref[...] * bottom_ref[...]).astype(jnp.float32)
    dep_lat = lat_edge(north_ref[layers] + fold_ref[layers], south_ref[layers], 0)
    dep_ym = ys(dep, dep_lat, -1)
    dep_yp = ys(dep, dep_lat, 1)
    zero = jnp.zeros((rows, cols), jnp.float32)

    def explicit(k, carry):
        cum_ym, cum_yp = carry
        kf = k.astype(jnp.float32)
        h = h_ref[k]
        zmid = zmid_ref[k]
        w0 = (kf < dep).astype(jnp.float32)
        wym = (kf < dep_ym).astype(jnp.float32)
        wyp = (kf < dep_yp).astype(jnp.float32)
        q = [r[k] * w0 for r in (t_ref, s_ref, u_ref, v_ref)]
        tile_n = north_ref[k] + fold_ref[k]
        tile_s = south_ref[k]
        ey = [lat_edge(tile_n, tile_s, c) for c in range(4)]
        ysh = {s: [ys(q[c], ey[c], s) for c in range(4)] for s in (-2, -1, 1, 2)}
        b_r = 0.5 * (q[3] + ysh[1][3]) * w0 * wyp
        b_l = 0.5 * (ysh[-1][3] + q[3]) * wym * w0
        w_r = face_weights(b_r)
        w_l = face_weights(b_l)
        adv = []
        for c in range(4):
            div_y = flux_divergence(w_r, w_l, ysh[-2][c], ysh[-1][c], q[c], ysh[1][c], ysh[2][c])
            adv.append(divx_ref[c * layers + k] - courant * div_y)
        load_ym = density(ysh[-1][0], ysh[-1][1], zmid) * wym * h
        load_yp = density(ysh[1][0], ysh[1][1], zmid) * wyp * h
        cum_ym = cum_ym + load_ym
        cum_yp = cum_yp + load_yp
        grad_y = 0.5 * ((cum_yp - 0.5 * load_yp) - (cum_ym - 0.5 * load_ym))
        star0 = adv[0] * w0
        star1 = adv[1] * w0
        star2 = adv[2] * w0
        star3 = (adv[3] - time_step * gravity * grad_y) * w0
        for c, val in enumerate((star0, star1, star2, star3)):
            star_scr[c * layers + k] = val
        rs_scr[k] = density(star0, star1, zmid)
        return (cum_ym, cum_yp)

    lag = 3
    carry_e = lax.fori_loop(0, lag, explicit, (zero, zero))

    surface_scale = surface_gain * inv_h_ref[0]
    w_top = (0.0 < dep).astype(jnp.float32)
    for c in range(4):
        star_scr[c * layers] = star_scr[c * layers] + flux_ref[c] * w_top * surface_scale

    def forward(k, carry):
        mix_prev, r_a, r_b, s0, s1, s2, s3 = carry
        kf = k.astype(jnp.float32)
        inv_h = inv_h_ref[k]
        nxt = jnp.minimum(k + 1, layers - 1)
        stratified = (rs_scr[nxt] - rs_scr[k]) * inv_sp_ref[k]
        sig = 1.0 / (1.0 + jnp.exp(stratified * (1.0 / strat_scale)))
        w_next = (kf + 1.0 < dep).astype(jnp.float32)
        mix = (mix_back + mix_conv * sig) * w_next
        mix = jnp.where(k < layers - 1, mix, 0.0)
        low_a = -mix_prev * inv_h
        up_a = -mix * inv_h
        cen_a = 1.0 - low_a - up_a
        low_b = -mix_prev * momentum_mix * inv_h
        up_b = -mix * momentum_mix * inv_h
        floor = (kf == dep - 1.0).astype(jnp.float32)
        cen_b = 1.0 - low_b - up_b + bottom_drag * floor * inv_h
        inv_a = 1.0 / (cen_a - low_a * r_a)
        inv_b = 1.0 / (cen_b - low_b * r_b)
        r_a = up_a * inv_a
        r_b = up_b * inv_b
        r_scr[k] = r_a
        r_scr[layers + k] = r_b
        s0 = (star_scr[k] - low_a * s0) * inv_a
        s1 = (star_scr[layers + k] - low_a * s1) * inv_a
        s2 = (star_scr[2 * layers + k] - low_b * s2) * inv_b
        s3 = (star_scr[3 * layers + k] - low_b * s3) * inv_b
        star_scr[k] = s0
        star_scr[layers + k] = s1
        star_scr[2 * layers + k] = s2
        star_scr[3 * layers + k] = s3
        return (mix, r_a, r_b, s0, s1, s2, s3)

    def fused(k, carry):
        carry_e, carry_f = carry
        return (explicit(k, carry_e), forward(k - lag, carry_f))

    _, carry_f = lax.fori_loop(lag, layers, fused, (carry_e, (zero,) * 7), unroll=9)
    lax.fori_loop(layers - lag, layers, forward, carry_f)

    def backward(i, carry):
        x0, x1, x2, x3 = carry
        k = layers - 1 - i
        r_a = r_scr[k]
        r_b = r_scr[layers + k]
        x0 = star_scr[k] - r_a * x0
        x1 = star_scr[layers + k] - r_a * x1
        x2 = star_scr[2 * layers + k] - r_b * x2
        x3 = star_scr[3 * layers + k] - r_b * x3
        o0_ref[k] = x0
        o1_ref[k] = x1
        o2_ref[k] = x2
        o3_ref[k] = x3
        return (x0, x1, x2, x3)

    pairs = ((o0_ref, o0_hbm), (o1_ref, o1_hbm), (o2_ref, o2_hbm), (o3_ref, o3_hbm))
    writes = []
    carry = (zero,) * 4
    for chunk in range(groups):
        carry = lax.fori_loop(chunk * GROUP, (chunk + 1) * GROUP, backward, carry, unroll=3)
        span = pl.ds(layers - (chunk + 1) * GROUP, GROUP)
        for c, (src, dst) in enumerate(pairs):
            write = pltpu.make_async_copy(src.at[span], dst.at[span], out_sems.at[chunk, c])
            write.start()
            writes.append(write)
    for write in writes:
        write.wait()


def level_tables(layers):
    offsets = np.arange(layers, dtype=np.float32) + np.float32(0.5)
    zmid = offsets / np.float32(layers)
    thickness = np.float32(0.5) + zmid
    inverse = np.float32(1.0) / thickness
    spacing = np.float32(0.5) * (thickness[1:] + thickness[:-1])
    inv_spacing = np.concatenate([np.float32(1.0) / spacing, np.ones((1,), np.float32)])
    return [jnp.asarray(t.astype(np.float32)) for t in (thickness, inverse, zmid, inv_spacing)]


def on_device(
    heat_anomaly,
    brine_anomaly,
    eastward_current,
    northward_current,
    shoreline_indicator,
    bottom_layer_index,
    boundary_fluxes,
):
    layers, rows, cols = heat_anomaly.shape
    fields = (heat_anomaly, brine_anomaly, eastward_current, northward_current)
    groups = layers // GROUP
    n_lat = lax.axis_size("lat")
    n_lon = lax.axis_size("lon")
    lat_idx = lax.axis_index("lat").astype(jnp.int32)
    is_last = (lat_idx == n_lat - 1).astype(jnp.int32).reshape(1)
    lat_info = jnp.stack([lat_idx, jnp.int32(n_lat)])

    smem = pl.BlockSpec(memory_space=pltpu.SMEM)
    vmem = pl.BlockSpec(memory_space=pltpu.VMEM)
    row_tiles = jax.ShapeDtypeStruct((layers + 1, rows, cols), jnp.float32)
    col_tiles = jax.ShapeDtypeStruct((groups + 1, rows, cols), jnp.float32)
    top, bot, right, left = pl.pallas_call(
        pack_kernel,
        out_shape=(row_tiles, row_tiles, col_tiles, col_tiles),
        in_specs=[smem] + [vmem] * 6,
        out_specs=(vmem,) * 4,
    )(is_last, shoreline_indicator, bottom_layer_index, *fields)

    from_south = lax.ppermute(top, "lat", [(i, i + 1) for i in range(n_lat - 1)])
    from_north = lax.ppermute(bot, "lat", [(i + 1, i) for i in range(n_lat - 1)])
    from_west = lax.ppermute(right, "lon", [(i, (i + 1) % n_lon) for i in range(n_lon)])
    from_east = lax.ppermute(left, "lon", [((i + 1) % n_lon, i) for i in range(n_lon)])
    last = (n_lat - 1) * n_lon
    fold, from_west, from_east = lax.optimization_barrier((top, from_west, from_east))
    from_fold = lax.ppermute(
        fold, ("lat", "lon"), [(last + x, last + n_lon - 1 - x) for x in range(n_lon)]
    )

    plane = jax.ShapeDtypeStruct((layers, rows, cols), jnp.float32)
    tables = level_tables(layers)
    divx = pl.pallas_call(
        xpart_kernel,
        out_shape=jax.ShapeDtypeStruct((4 * layers, rows, cols), jnp.float32),
        in_specs=[smem] * 3 + [vmem] * 8,
        out_specs=vmem,
        compiler_params=pltpu.CompilerParams(vmem_limit_bytes=16 * 1024 * 1024),
    )(lat_info, tables[0], tables[2], shoreline_indicator, bottom_layer_index, *fields,
      from_west, from_east)
    outs = pl.pallas_call(
        step_kernel,
        out_shape=(plane,) * 4,
        in_specs=[smem] * 5 + [vmem] * 11,
        out_specs=(pl.BlockSpec(memory_space=pl.ANY),) * 4,
        scratch_shapes=[
            pltpu.VMEM((4 * layers, rows, cols), jnp.float32),
            pltpu.VMEM((2 * layers, rows, cols), jnp.float32),
            pltpu.VMEM((layers, rows, cols), jnp.float32),
        ] + [pltpu.VMEM((layers, rows, cols), jnp.float32)] * 4 + [
            pltpu.SemaphoreType.DMA((groups, 4)),
        ],
        compiler_params=pltpu.CompilerParams(vmem_limit_bytes=16 * 1024 * 1024),
    )(
        lat_info, *tables,
        shoreline_indicator, bottom_layer_index, boundary_fluxes, *fields,
        from_south, from_north, from_fold, divx,
    )
    return tuple(outs)


def solution(mesh):
    in_specs = (
        P(None, "lat", "lon"),
        P(None, "lat", "lon"),
        P(None, "lat", "lon"),
        P(None, "lat", "lon"),
        P("lat", "lon"),
        P("lat", "lon"),
        P(None, "lat", "lon"),
    )
    out_specs = (
        P(None, "lat", "lon"),
        P(None, "lat", "lon"),
        P(None, "lat", "lon"),
        P(None, "lat", "lon"),
    )
    return jax.shard_map(
        on_device, mesh=mesh, in_specs=in_specs, out_specs=out_specs, check_vma=False
    )
```

```python
import numpy as np
import jax
import jax.numpy as jnp
from jax import lax
from jax.experimental import pallas as pl
from jax.experimental.pallas import tpu as pltpu
from jax.sharding import PartitionSpec as P

courant = 0.25
time_step = 0.2
gravity = 0.2
coriolis = 0.5
thermal = 0.6
thermal_sq = 0.1
haline = 0.8
mix_back = 5.0
mix_conv = 60.0
strat_scale = 2.0
momentum_mix = 2.0
bottom_drag = 1.0
surface_gain = 0.5

GROUP = 15


def density(warmth, saltiness, depth_column):
    return -thermal * warmth * (1.0 + thermal_sq * warmth + depth_column) + haline * saltiness


def face_weights(face_vel):
    return (
        0.5 * face_vel,
        jnp.maximum(face_vel, 0.0) * (1.0 / 6.0),
        jnp.minimum(face_vel, 0.0) * (1.0 / 6.0),
    )


def flux_divergence(right_w, left_w, m2, m1, q0, p1, p2):
    half_r, pos_r, neg_r = right_w
    half_l, pos_l, neg_l = left_w
    step_r = p1 - q0
    step_l = q0 - m1
    curv_0 = step_r - step_l
    curv_p = (p2 - p1) - step_r
    curv_m = step_l - (m1 - m2)
    flux_r = half_r * (q0 + p1) - (pos_r * curv_0 + neg_r * curv_p)
    flux_l = half_l * (m1 + q0) - (pos_l * curv_m + neg_l * curv_0)
    return flux_r - flux_l


def rolled(x, shift, axis):
    shift %= x.shape[axis]
    return x if shift == 0 else pltpu.roll(x, shift, axis)


def pack_kernel(
    last_ref, shore_ref, bottom_ref, t_ref, s_ref, u_ref, v_ref,
    top_ref, bot_ref, right_ref, left_ref,
):
    layers, rows, cols = t_ref.shape
    groups = layers // GROUP
    lane = lax.broadcasted_iota(jnp.int32, (rows, cols), 1)
    row = lax.broadcasted_iota(jnp.int32, (rows, cols), 0)
    dep = (shore_ref[...] * bottom_ref[...]).astype(jnp.float32)
    zero = jnp.zeros((rows, cols), jnp.float32)

    def pack_rows(vals, first):
        out = zero
        for c, val in enumerate(vals):
            out = jnp.where((row >> 1) == c, rolled(val, 2 * c - first, 0), out)
        return out

    def group_body(g, carry):
        right = zero
        left = zero
        for j in range(GROUP):
            k = g * GROUP + j
            w = (k.astype(jnp.float32) < dep).astype(jnp.float32)
            q = [r[k] * w for r in (t_ref, s_ref, u_ref, v_ref)]
            top_ref[k] = pack_rows(q, rows - 2)
            bot_ref[k] = pack_rows(q, 0)
            for c in range(4):
                m = j * 4 + c
                slot = (lane >> 1) == m
                right = jnp.where(slot, rolled(q[c], 2 * m - (cols - 2), 1), right)
                left = jnp.where(slot, rolled(q[c], 2 * m, 1), left)
        right_ref[g] = right
        left_ref[g] = left
        return carry

    lax.fori_loop(0, groups, group_body, 0)
    top_ref[layers] = pack_rows([dep], rows - 2)
    bot_ref[layers] = pack_rows([dep], 0)
    right_ref[groups] = jnp.where(lane < 2, rolled(dep, 2, 1), zero)
    left_ref[groups] = jnp.where(lane < 2, dep, zero)

    @pl.when(last_ref[0] == 1)
    def _():
        tiles = top_ref[...].reshape((layers + 1) * rows, cols)
        tile_row = lax.broadcasted_iota(jnp.int32, tiles.shape, 0) % rows
        sign = jnp.where(tile_row < 4, 1.0, -1.0)
        swapped = jnp.where(
            (tile_row & 1) == 0, rolled(tiles, -1, 0), rolled(tiles, 1, 0)
        ) * sign
        src_lane = lax.broadcasted_iota(jnp.int32, (cols, cols), 0)
        dst_lane = lax.broadcasted_iota(jnp.int32, (cols, cols), 1)
        reverse = (src_lane + dst_lane == cols - 1).astype(jnp.float32)
        flipped = jnp.dot(
            swapped, reverse, precision=lax.Precision.HIGHEST,
            preferred_element_type=jnp.float32,
        )
        top_ref[...] = flipped.reshape(layers + 1, rows, cols)


def xpart_kernel(
    lat_ref, h_ref, zmid_ref, shore_ref, bottom_ref, t_ref, s_ref, u_ref, v_ref,
    west_ref, east_ref, divx_ref,
):
    layers, rows, cols = t_ref.shape
    groups = layers // GROUP
    lane = lax.broadcasted_iota(jnp.int32, (rows, cols), 1)
    row = lax.broadcasted_iota(jnp.int32, (rows, cols), 0)
    total_rows = rows * lat_ref[1]
    row_ids = (lat_ref[0] * rows + row).astype(jnp.float32)
    turning = coriolis * (2.0 * (row_ids + 0.5) / total_rows.astype(jnp.float32) - 1.0)

    def xs(v, e, s):
        if s == 1:
            return pltpu.roll(jnp.where(lane == 0, e, v), cols - 1, 1)
        if s == 2:
            return pltpu.roll(jnp.where(lane < 2, e, v), cols - 2, 1)
        if s == -1:
            return pltpu.roll(jnp.where(lane == cols - 1, e, v), 1, 1)
        return pltpu.roll(jnp.where(lane >= cols - 2, e, v), 2, 1)

    def lon_edge(tile_e, tile_w, m):
        return jnp.where(lane < 64, rolled(tile_e, -2 * m, 1), rolled(tile_w, cols - 2 - 2 * m, 1))

    dep = (shore_ref[...] * bottom_ref[...]).astype(jnp.float32)
    dep_lon = lon_edge(east_ref[groups], west_ref[groups], 0)
    dep_xm = xs(dep, dep_lon, -1)
    dep_xp = xs(dep, dep_lon, 1)
    zero = jnp.zeros((rows, cols), jnp.float32)

    def group_body(g, carry):
        tile_e = east_ref[g]
        tile_w = west_ref[g]
        for j in range(GROUP):
            cum_xm, cum_xp = carry
            k = g * GROUP + j
            kf = k.astype(jnp.float32)
            h = h_ref[k]
            zmid = zmid_ref[k]
            w0 = (kf < dep).astype(jnp.float32)
            wxm = (kf < dep_xm).astype(jnp.float32)
            wxp = (kf < dep_xp).astype(jnp.float32)
            q = [r[k] * w0 for r in (t_ref, s_ref, u_ref, v_ref)]
            ex = [lon_edge(tile_e, tile_w, j * 4 + c) for c in range(4)]
            xsh = {s: [xs(q[c], ex[c], s) for c in range(4)] for s in (-2, -1, 1, 2)}
            a_r = 0.5 * (q[2] + xsh[1][2]) * w0 * wxp
            a_l = 0.5 * (xsh[-1][2] + q[2]) * wxm * w0
            w_r = face_weights(a_r)
            w_l = face_weights(a_l)
            part = [
                q[c] - courant * flux_divergence(
                    w_r, w_l, xsh[-2][c], xsh[-1][c], q[c], xsh[1][c], xsh[2][c]
                )
                for c in range(4)
            ]
            load_xm = density(xsh[-1][0], xsh[-1][1], zmid) * wxm * h
            load_xp = density(xsh[1][0], xsh[1][1], zmid) * wxp * h
            cum_xm = cum_xm + load_xm
            cum_xp = cum_xp + load_xp
            grad_x = 0.5 * ((cum_xp - 0.5 * load_xp) - (cum_xm - 0.5 * load_xm))
            part[2] = part[2] + time_step * (turning * q[3] - gravity * grad_x)
            part[3] = part[3] + time_step * (-turning * q[2])
            for c in range(4):
                divx_ref[c * layers + k] = part[c]
            carry = (cum_xm, cum_xp)
        return carry

    lax.fori_loop(0, groups, group_body, (zero, zero))


def step_kernel(
    lat_ref, h_ref, inv_h_ref, zmid_ref, inv_sp_ref,
    shore_ref, bottom_ref, flux_ref, t_ref, s_ref, u_ref, v_ref,
    south_ref, north_ref, fold_ref, divx_ref,
    o0_hbm, o1_hbm, o2_hbm, o3_hbm,
    star_scr, r_scr, rs_scr, o0_ref, o1_ref, o2_ref, o3_ref, out_sems,
):
    layers = t_ref.shape[0]
    rows, cols = t_ref.shape[1], t_ref.shape[2]
    groups = layers // GROUP
    lane = lax.broadcasted_iota(jnp.int32, (rows, cols), 1)
    row = lax.broadcasted_iota(jnp.int32, (rows, cols), 0)

    def ys(v, e, s):
        if s == 1:
            return pltpu.roll(jnp.where(row == 0, e, v), rows - 1, 0)
        if s == 2:
            return pltpu.roll(jnp.where(row < 2, e, v), rows - 2, 0)
        if s == -1:
            return pltpu.roll(jnp.where(row == rows - 1, e, v), 1, 0)
        return pltpu.roll(jnp.where(row >= rows - 2, e, v), 2, 0)

    def lat_edge(tile_n, tile_s, c):
        return jnp.where(row < 4, rolled(tile_n, -2 * c, 0), rolled(tile_s, rows - 2 - 2 * c, 0))

    dep = (shore_ref[...] * bottom_ref[...]).astype(jnp.float32)
    dep_lat = lat_edge(north_ref[layers] + fold_ref[layers], south_ref[layers], 0)
    dep_ym = ys(dep, dep_lat, -1)
    dep_yp = ys(dep, dep_lat, 1)
    zero = jnp.zeros((rows, cols), jnp.float32)

    def explicit(k, carry):
        cum_ym, cum_yp = carry
        kf = k.astype(jnp.float32)
        h = h_ref[k]
        zmid = zmid_ref[k]
        w0 = (kf < dep).astype(jnp.float32)
        wym = (kf < dep_ym).astype(jnp.float32)
        wyp = (kf < dep_yp).astype(jnp.float32)
        q = [r[k] * w0 for r in (t_ref, s_ref, u_ref, v_ref)]
        tile_n = north_ref[k] + fold_ref[k]
        tile_s = south_ref[k]
        ey = [lat_edge(tile_n, tile_s, c) for c in range(4)]
        ysh = {s: [ys(q[c], ey[c], s) for c in range(4)] for s in (-2, -1, 1, 2)}
        b_r = 0.5 * (q[3] + ysh[1][3]) * w0 * wyp
        b_l = 0.5 * (ysh[-1][3] + q[3]) * wym * w0
        w_r = face_weights(b_r)
        w_l = face_weights(b_l)
        adv = []
        for c in range(4):
            div_y = flux_divergence(w_r, w_l, ysh[-2][c], ysh[-1][c], q[c], ysh[1][c], ysh[2][c])
            adv.append(divx_ref[c * layers + k] - courant * div_y)
        load_ym = density(ysh[-1][0], ysh[-1][1], zmid) * wym * h
        load_yp = density(ysh[1][0], ysh[1][1], zmid) * wyp * h
        cum_ym = cum_ym + load_ym
        cum_yp = cum_yp + load_yp
        grad_y = 0.5 * ((cum_yp - 0.5 * load_yp) - (cum_ym - 0.5 * load_ym))
        star0 = adv[0] * w0
        star1 = adv[1] * w0
        star2 = adv[2] * w0
        star3 = (adv[3] - time_step * gravity * grad_y) * w0
        for c, val in enumerate((star0, star1, star2, star3)):
            star_scr[c * layers + k] = val
        rs_scr[k] = density(star0, star1, zmid)
        return (cum_ym, cum_yp)

    lag = 3
    carry_e = lax.fori_loop(0, lag, explicit, (zero, zero))

    surface_scale = surface_gain * inv_h_ref[0]
    w_top = (0.0 < dep).astype(jnp.float32)
    for c in range(4):
        star_scr[c * layers] = star_scr[c * layers] + flux_ref[c] * w_top * surface_scale

    def forward(k, carry):
        mix_prev, r_a, r_b, s0, s1, s2, s3 = carry
        kf = k.astype(jnp.float32)
        inv_h = inv_h_ref[k]
        nxt = jnp.minimum(k + 1, layers - 1)
        stratified = (rs_scr[nxt] - rs_scr[k]) * inv_sp_ref[k]
        sig = 1.0 / (1.0 + jnp.exp(stratified * (1.0 / strat_scale)))
        w_next = (kf + 1.0 < dep).astype(jnp.float32)
        mix = (mix_back + mix_conv * sig) * w_next
        mix = jnp.where(k < layers - 1, mix, 0.0)
        low_a = -mix_prev * inv_h
        up_a = -mix * inv_h
        cen_a = 1.0 - low_a - up_a
        low_b = -mix_prev * momentum_mix * inv_h
        up_b = -mix * momentum_mix * inv_h
        floor = (kf == dep - 1.0).astype(jnp.float32)
        cen_b = 1.0 - low_b - up_b + bottom_drag * floor * inv_h
        inv_a = 1.0 / (cen_a - low_a * r_a)
        inv_b = 1.0 / (cen_b - low_b * r_b)
        r_a = up_a * inv_a
        r_b = up_b * inv_b
        r_scr[k] = r_a
        r_scr[layers + k] = r_b
        s0 = (star_scr[k] - low_a * s0) * inv_a
        s1 = (star_scr[layers + k] - low_a * s1) * inv_a
        s2 = (star_scr[2 * layers + k] - low_b * s2) * inv_b
        s3 = (star_scr[3 * layers + k] - low_b * s3) * inv_b
        star_scr[k] = s0
        star_scr[layers + k] = s1
        star_scr[2 * layers + k] = s2
        star_scr[3 * layers + k] = s3
        return (mix, r_a, r_b, s0, s1, s2, s3)

    def fused(k, carry):
        carry_e, carry_f = carry
        return (explicit(k, carry_e), forward(k - lag, carry_f))

    _, carry_f = lax.fori_loop(lag, layers, fused, (carry_e, (zero,) * 7), unroll=9)
    lax.fori_loop(layers - lag, layers, forward, carry_f)

    def backward(i, carry):
        x0, x1, x2, x3 = carry
        k = layers - 1 - i
        r_a = r_scr[k]
        r_b = r_scr[layers + k]
        x0 = star_scr[k] - r_a * x0
        x1 = star_scr[layers + k] - r_a * x1
        x2 = star_scr[2 * layers + k] - r_b * x2
        x3 = star_scr[3 * layers + k] - r_b * x3
        o0_ref[k] = x0
        o1_ref[k] = x1
        o2_ref[k] = x2
        o3_ref[k] = x3
        return (x0, x1, x2, x3)

    pairs = ((o0_ref, o0_hbm), (o1_ref, o1_hbm), (o2_ref, o2_hbm), (o3_ref, o3_hbm))
    writes = []
    carry = (zero,) * 4
    for chunk in range(groups):
        carry = lax.fori_loop(chunk * GROUP, (chunk + 1) * GROUP, backward, carry, unroll=3)
        span = pl.ds(layers - (chunk + 1) * GROUP, GROUP)
        for c, (src, dst) in enumerate(pairs):
            write = pltpu.make_async_copy(src.at[span], dst.at[span], out_sems.at[chunk, c])
            write.start()
            writes.append(write)
    for write in writes:
        write.wait()


def level_tables(layers):
    offsets = np.arange(layers, dtype=np.float32) + np.float32(0.5)
    zmid = offsets / np.float32(layers)
    thickness = np.float32(0.5) + zmid
    inverse = np.float32(1.0) / thickness
    spacing = np.float32(0.5) * (thickness[1:] + thickness[:-1])
    inv_spacing = np.concatenate([np.float32(1.0) / spacing, np.ones((1,), np.float32)])
    return [jnp.asarray(t.astype(np.float32)) for t in (thickness, inverse, zmid, inv_spacing)]


def on_device(
    heat_anomaly,
    brine_anomaly,
    eastward_current,
    northward_current,
    shoreline_indicator,
    bottom_layer_index,
    boundary_fluxes,
):
    layers, rows, cols = heat_anomaly.shape
    fields = (heat_anomaly, brine_anomaly, eastward_current, northward_current)
    groups = layers // GROUP
    n_lat = lax.axis_size("lat")
    n_lon = lax.axis_size("lon")
    lat_idx = lax.axis_index("lat").astype(jnp.int32)
    is_last = (lat_idx == n_lat - 1).astype(jnp.int32).reshape(1)
    lat_info = jnp.stack([lat_idx, jnp.int32(n_lat)])

    smem = pl.BlockSpec(memory_space=pltpu.SMEM)
    vmem = pl.BlockSpec(memory_space=pltpu.VMEM)
    row_tiles = jax.ShapeDtypeStruct((layers + 1, rows, cols), jnp.float32)
    col_tiles = jax.ShapeDtypeStruct((groups + 1, rows, cols), jnp.float32)
    top, bot, right, left = pl.pallas_call(
        pack_kernel,
        out_shape=(row_tiles, row_tiles, col_tiles, col_tiles),
        in_specs=[smem] + [vmem] * 6,
        out_specs=(vmem,) * 4,
    )(is_last, shoreline_indicator, bottom_layer_index, *fields)

    from_south = lax.ppermute(top, "lat", [(i, i + 1) for i in range(n_lat - 1)])
    from_north = lax.ppermute(bot, "lat", [(i + 1, i) for i in range(n_lat - 1)])
    from_west = lax.ppermute(right, "lon", [(i, (i + 1) % n_lon) for i in range(n_lon)])
    from_east = lax.ppermute(left, "lon", [((i + 1) % n_lon, i) for i in range(n_lon)])
    last = (n_lat - 1) * n_lon
    fold = top
    from_fold = lax.ppermute(
        fold, ("lat", "lon"), [(last + x, last + n_lon - 1 - x) for x in range(n_lon)]
    )

    plane = jax.ShapeDtypeStruct((layers, rows, cols), jnp.float32)
    tables = level_tables(layers)
    divx = pl.pallas_call(
        xpart_kernel,
        out_shape=jax.ShapeDtypeStruct((4 * layers, rows, cols), jnp.float32),
        in_specs=[smem] * 3 + [vmem] * 8,
        out_specs=vmem,
        compiler_params=pltpu.CompilerParams(vmem_limit_bytes=16 * 1024 * 1024),
    )(lat_info, tables[0], tables[2], shoreline_indicator, bottom_layer_index, *fields,
      from_west, from_east)
    outs = pl.pallas_call(
        step_kernel,
        out_shape=(plane,) * 4,
        in_specs=[smem] * 5 + [vmem] * 11,
        out_specs=(pl.BlockSpec(memory_space=pl.ANY),) * 4,
        scratch_shapes=[
            pltpu.VMEM((4 * layers, rows, cols), jnp.float32),
            pltpu.VMEM((2 * layers, rows, cols), jnp.float32),
            pltpu.VMEM((layers, rows, cols), jnp.float32),
        ] + [pltpu.VMEM((layers, rows, cols), jnp.float32)] * 4 + [
            pltpu.SemaphoreType.DMA((groups, 4)),
        ],
        compiler_params=pltpu.CompilerParams(vmem_limit_bytes=16 * 1024 * 1024),
    )(
        lat_info, *tables,
        shoreline_indicator, bottom_layer_index, boundary_fluxes, *fields,
        from_south, from_north, from_fold, divx,
    )
    return tuple(outs)


def solution(mesh):
    in_specs = (
        P(None, "lat", "lon"),
        P(None, "lat", "lon"),
        P(None, "lat", "lon"),
        P(None, "lat", "lon"),
        P("lat", "lon"),
        P("lat", "lon"),
        P(None, "lat", "lon"),
    )
    out_specs = (
        P(None, "lat", "lon"),
        P(None, "lat", "lon"),
        P(None, "lat", "lon"),
        P(None, "lat", "lon"),
    )
    return jax.shard_map(
        on_device, mesh=mesh, in_specs=in_specs, out_specs=out_specs, check_vma=False
    )
```

```python
import numpy as np
import jax
import jax.numpy as jnp
from jax import lax
from jax.experimental import pallas as pl
from jax.experimental.pallas import tpu as pltpu
from jax.sharding import PartitionSpec as P

courant = 0.25
time_step = 0.2
gravity = 0.2
coriolis = 0.5
thermal = 0.6
thermal_sq = 0.1
haline = 0.8
mix_back = 5.0
mix_conv = 60.0
strat_scale = 2.0
momentum_mix = 2.0
bottom_drag = 1.0
surface_gain = 0.5

GROUP = 15


def density(warmth, saltiness, depth_column):
    return -thermal * warmth * (1.0 + thermal_sq * warmth + depth_column) + haline * saltiness


def face_weights(face_vel):
    return (
        0.5 * face_vel,
        jnp.maximum(face_vel, 0.0) * (1.0 / 6.0),
        jnp.minimum(face_vel, 0.0) * (1.0 / 6.0),
    )


def flux_divergence(right_w, left_w, m2, m1, q0, p1, p2):
    half_r, pos_r, neg_r = right_w
    half_l, pos_l, neg_l = left_w
    step_r = p1 - q0
    step_l = q0 - m1
    curv_0 = step_r - step_l
    curv_p = (p2 - p1) - step_r
    curv_m = step_l - (m1 - m2)
    flux_r = half_r * (q0 + p1) - (pos_r * curv_0 + neg_r * curv_p)
    flux_l = half_l * (m1 + q0) - (pos_l * curv_m + neg_l * curv_0)
    return flux_r - flux_l


def rolled(x, shift, axis):
    shift %= x.shape[axis]
    return x if shift == 0 else pltpu.roll(x, shift, axis)


def pack_kernel(
    last_ref, shore_ref, bottom_ref, t_ref, s_ref, u_ref, v_ref,
    top_ref, bot_ref, right_ref, left_ref,
):
    layers, rows, cols = t_ref.shape
    groups = layers // GROUP
    lane = lax.broadcasted_iota(jnp.int32, (rows, cols), 1)
    row = lax.broadcasted_iota(jnp.int32, (rows, cols), 0)
    dep = (shore_ref[...] * bottom_ref[...]).astype(jnp.float32)
    zero = jnp.zeros((rows, cols), jnp.float32)

    def pack_rows(vals, first):
        out = zero
        for c, val in enumerate(vals):
            out = jnp.where((row >> 1) == c, rolled(val, 2 * c - first, 0), out)
        return out

    def group_body(g, carry):
        right = zero
        left = zero
        for j in range(GROUP):
            k = g * GROUP + j
            w = (k.astype(jnp.float32) < dep).astype(jnp.float32)
            q = [r[k] * w for r in (t_ref, s_ref, u_ref, v_ref)]
            top_ref[k] = pack_rows(q, rows - 2)
            bot_ref[k] = pack_rows(q, 0)
            for c in range(4):
                m = j * 4 + c
                slot = (lane >> 1) == m
                right = jnp.where(slot, rolled(q[c], 2 * m - (cols - 2), 1), right)
                left = jnp.where(slot, rolled(q[c], 2 * m, 1), left)
        right_ref[g] = right
        left_ref[g] = left
        return carry

    lax.fori_loop(0, groups, group_body, 0)
    top_ref[layers] = pack_rows([dep], rows - 2)
    bot_ref[layers] = pack_rows([dep], 0)
    right_ref[groups] = jnp.where(lane < 2, rolled(dep, 2, 1), zero)
    left_ref[groups] = jnp.where(lane < 2, dep, zero)

    @pl.when(last_ref[0] == 1)
    def _():
        tiles = top_ref[...].reshape((layers + 1) * rows, cols)
        tile_row = lax.broadcasted_iota(jnp.int32, tiles.shape, 0) % rows
        sign = jnp.where(tile_row < 4, 1.0, -1.0)
        swapped = jnp.where(
            (tile_row & 1) == 0, rolled(tiles, -1, 0), rolled(tiles, 1, 0)
        ) * sign
        src_lane = lax.broadcasted_iota(jnp.int32, (cols, cols), 0)
        dst_lane = lax.broadcasted_iota(jnp.int32, (cols, cols), 1)
        reverse = (src_lane + dst_lane == cols - 1).astype(jnp.float32)
        flipped = jnp.dot(
            swapped, reverse, precision=lax.Precision.HIGHEST,
            preferred_element_type=jnp.float32,
        )
        top_ref[...] = flipped.reshape(layers + 1, rows, cols)


def xpart_kernel(
    lat_ref, h_ref, zmid_ref, shore_ref, bottom_ref, t_ref, s_ref, u_ref, v_ref,
    west_ref, east_ref, divx_ref,
):
    layers, rows, cols = t_ref.shape
    groups = layers // GROUP
    lane = lax.broadcasted_iota(jnp.int32, (rows, cols), 1)
    row = lax.broadcasted_iota(jnp.int32, (rows, cols), 0)
    total_rows = rows * lat_ref[1]
    row_ids = (lat_ref[0] * rows + row).astype(jnp.float32)
    turning = coriolis * (2.0 * (row_ids + 0.5) / total_rows.astype(jnp.float32) - 1.0)

    def xs(v, e, s):
        if s == 1:
            return pltpu.roll(jnp.where(lane == 0, e, v), cols - 1, 1)
        if s == 2:
            return pltpu.roll(jnp.where(lane < 2, e, v), cols - 2, 1)
        if s == -1:
            return pltpu.roll(jnp.where(lane == cols - 1, e, v), 1, 1)
        return pltpu.roll(jnp.where(lane >= cols - 2, e, v), 2, 1)

    def lon_edge(tile_e, tile_w, m):
        return jnp.where(lane < 64, rolled(tile_e, -2 * m, 1), rolled(tile_w, cols - 2 - 2 * m, 1))

    dep = (shore_ref[...] * bottom_ref[...]).astype(jnp.float32)
    dep_lon = lon_edge(east_ref[groups], west_ref[groups], 0)
    dep_xm = xs(dep, dep_lon, -1)
    dep_xp = xs(dep, dep_lon, 1)
    zero = jnp.zeros((rows, cols), jnp.float32)

    def group_body(g, carry):
        tile_e = east_ref[g]
        tile_w = west_ref[g]
        for j in range(GROUP):
            cum_xm, cum_xp = carry
            k = g * GROUP + j
            kf = k.astype(jnp.float32)
            h = h_ref[k]
            zmid = zmid_ref[k]
            w0 = (kf < dep).astype(jnp.float32)
            wxm = (kf < dep_xm).astype(jnp.float32)
            wxp = (kf < dep_xp).astype(jnp.float32)
            q = [r[k] * w0 for r in (t_ref, s_ref, u_ref, v_ref)]
            ex = [lon_edge(tile_e, tile_w, j * 4 + c) for c in range(4)]
            xsh = {s: [xs(q[c], ex[c], s) for c in range(4)] for s in (-2, -1, 1, 2)}
            a_r = 0.5 * (q[2] + xsh[1][2]) * w0 * wxp
            a_l = 0.5 * (xsh[-1][2] + q[2]) * wxm * w0
            w_r = face_weights(a_r)
            w_l = face_weights(a_l)
            part = [
                q[c] - courant * flux_divergence(
                    w_r, w_l, xsh[-2][c], xsh[-1][c], q[c], xsh[1][c], xsh[2][c]
                )
                for c in range(4)
            ]
            load_xm = density(xsh[-1][0], xsh[-1][1], zmid) * wxm * h
            load_xp = density(xsh[1][0], xsh[1][1], zmid) * wxp * h
            cum_xm = cum_xm + load_xm
            cum_xp = cum_xp + load_xp
            grad_x = 0.5 * ((cum_xp - 0.5 * load_xp) - (cum_xm - 0.5 * load_xm))
            part[2] = part[2] + time_step * (turning * q[3] - gravity * grad_x)
            part[3] = part[3] + time_step * (-turning * q[2])
            for c in range(4):
                divx_ref[c * layers + k] = part[c]
            carry = (cum_xm, cum_xp)
        return carry

    lax.fori_loop(0, groups, group_body, (zero, zero))


def step_kernel(
    lat_ref, h_ref, inv_h_ref, zmid_ref, inv_sp_ref,
    shore_ref, bottom_ref, flux_ref, t_ref, s_ref, u_ref, v_ref,
    south_ref, north_ref, fold_ref, divx_ref,
    o0_hbm, o1_hbm, o2_hbm, o3_hbm,
    star_scr, r_scr, rs_scr, o0_ref, o1_ref, o2_ref, o3_ref, out_sems,
):
    layers = t_ref.shape[0]
    rows, cols = t_ref.shape[1], t_ref.shape[2]
    groups = layers // GROUP
    lane = lax.broadcasted_iota(jnp.int32, (rows, cols), 1)
    row = lax.broadcasted_iota(jnp.int32, (rows, cols), 0)

    def ys(v, e, s):
        if s == 1:
            return pltpu.roll(jnp.where(row == 0, e, v), rows - 1, 0)
        if s == 2:
            return pltpu.roll(jnp.where(row < 2, e, v), rows - 2, 0)
        if s == -1:
            return pltpu.roll(jnp.where(row == rows - 1, e, v), 1, 0)
        return pltpu.roll(jnp.where(row >= rows - 2, e, v), 2, 0)

    def lat_edge(tile_n, tile_s, c):
        return jnp.where(row < 4, rolled(tile_n, -2 * c, 0), rolled(tile_s, rows - 2 - 2 * c, 0))

    dep = (shore_ref[...] * bottom_ref[...]).astype(jnp.float32)
    dep_lat = lat_edge(north_ref[layers] + fold_ref[layers], south_ref[layers], 0)
    dep_ym = ys(dep, dep_lat, -1)
    dep_yp = ys(dep, dep_lat, 1)
    zero = jnp.zeros((rows, cols), jnp.float32)

    def explicit(k, carry):
        cum_ym, cum_yp = carry
        kf = k.astype(jnp.float32)
        h = h_ref[k]
        zmid = zmid_ref[k]
        w0 = (kf < dep).astype(jnp.float32)
        wym = (kf < dep_ym).astype(jnp.float32)
        wyp = (kf < dep_yp).astype(jnp.float32)
        q = [r[k] * w0 for r in (t_ref, s_ref, u_ref, v_ref)]
        tile_n = north_ref[k] + fold_ref[k]
        tile_s = south_ref[k]
        ey = [lat_edge(tile_n, tile_s, c) for c in range(4)]
        ysh = {s: [ys(q[c], ey[c], s) for c in range(4)] for s in (-2, -1, 1, 2)}
        b_r = 0.5 * (q[3] + ysh[1][3]) * w0 * wyp
        b_l = 0.5 * (ysh[-1][3] + q[3]) * wym * w0
        w_r = face_weights(b_r)
        w_l = face_weights(b_l)
        adv = []
        for c in range(4):
            div_y = flux_divergence(w_r, w_l, ysh[-2][c], ysh[-1][c], q[c], ysh[1][c], ysh[2][c])
            adv.append(divx_ref[c * layers + k] - courant * div_y)
        load_ym = density(ysh[-1][0], ysh[-1][1], zmid) * wym * h
        load_yp = density(ysh[1][0], ysh[1][1], zmid) * wyp * h
        cum_ym = cum_ym + load_ym
        cum_yp = cum_yp + load_yp
        grad_y = 0.5 * ((cum_yp - 0.5 * load_yp) - (cum_ym - 0.5 * load_ym))
        star0 = adv[0] * w0
        star1 = adv[1] * w0
        star2 = adv[2] * w0
        star3 = (adv[3] - time_step * gravity * grad_y) * w0
        for c, val in enumerate((star0, star1, star2, star3)):
            star_scr[c * layers + k] = val
        rs_scr[k] = density(star0, star1, zmid)
        return (cum_ym, cum_yp)

    lag = 3
    carry_e = lax.fori_loop(0, lag, explicit, (zero, zero), unroll=True)

    surface_scale = surface_gain * inv_h_ref[0]
    w_top = (0.0 < dep).astype(jnp.float32)
    for c in range(4):
        star_scr[c * layers] = star_scr[c * layers] + flux_ref[c] * w_top * surface_scale

    def forward(k, carry):
        mix_prev, r_a, r_b, s0, s1, s2, s3 = carry
        kf = k.astype(jnp.float32)
        inv_h = inv_h_ref[k]
        nxt = jnp.minimum(k + 1, layers - 1)
        stratified = (rs_scr[nxt] - rs_scr[k]) * inv_sp_ref[k]
        sig = 1.0 / (1.0 + jnp.exp(stratified * (1.0 / strat_scale)))
        w_next = (kf + 1.0 < dep).astype(jnp.float32)
        mix = (mix_back + mix_conv * sig) * w_next
        mix = jnp.where(k < layers - 1, mix, 0.0)
        low_a = -mix_prev * inv_h
        up_a = -mix * inv_h
        cen_a = 1.0 - low_a - up_a
        low_b = -mix_prev * momentum_mix * inv_h
        up_b = -mix * momentum_mix * inv_h
        floor = (kf == dep - 1.0).astype(jnp.float32)
        cen_b = 1.0 - low_b - up_b + bottom_drag * floor * inv_h
        inv_a = 1.0 / (cen_a - low_a * r_a)
        inv_b = 1.0 / (cen_b - low_b * r_b)
        r_a = up_a * inv_a
        r_b = up_b * inv_b
        r_scr[k] = r_a
        r_scr[layers + k] = r_b
        s0 = (star_scr[k] - low_a * s0) * inv_a
        s1 = (star_scr[layers + k] - low_a * s1) * inv_a
        s2 = (star_scr[2 * layers + k] - low_b * s2) * inv_b
        s3 = (star_scr[3 * layers + k] - low_b * s3) * inv_b
        star_scr[k] = s0
        star_scr[layers + k] = s1
        star_scr[2 * layers + k] = s2
        star_scr[3 * layers + k] = s3
        return (mix, r_a, r_b, s0, s1, s2, s3)

    def fused(k, carry):
        carry_e, carry_f = carry
        return (explicit(k, carry_e), forward(k - lag, carry_f))

    _, carry_f = lax.fori_loop(lag, layers, fused, (carry_e, (zero,) * 7), unroll=9)
    lax.fori_loop(layers - lag, layers, forward, carry_f, unroll=True)

    def backward(i, carry):
        x0, x1, x2, x3 = carry
        k = layers - 1 - i
        r_a = r_scr[k]
        r_b = r_scr[layers + k]
        x0 = star_scr[k] - r_a * x0
        x1 = star_scr[layers + k] - r_a * x1
        x2 = star_scr[2 * layers + k] - r_b * x2
        x3 = star_scr[3 * layers + k] - r_b * x3
        o0_ref[k] = x0
        o1_ref[k] = x1
        o2_ref[k] = x2
        o3_ref[k] = x3
        return (x0, x1, x2, x3)

    pairs = ((o0_ref, o0_hbm), (o1_ref, o1_hbm), (o2_ref, o2_hbm), (o3_ref, o3_hbm))
    writes = []
    carry = (zero,) * 4
    for chunk in range(groups):
        carry = lax.fori_loop(chunk * GROUP, (chunk + 1) * GROUP, backward, carry, unroll=5)
        span = pl.ds(layers - (chunk + 1) * GROUP, GROUP)
        for c, (src, dst) in enumerate(pairs):
            write = pltpu.make_async_copy(src.at[span], dst.at[span], out_sems.at[chunk, c])
            write.start()
            writes.append(write)
    for write in writes:
        write.wait()


def level_tables(layers):
    offsets = np.arange(layers, dtype=np.float32) + np.float32(0.5)
    zmid = offsets / np.float32(layers)
    thickness = np.float32(0.5) + zmid
    inverse = np.float32(1.0) / thickness
    spacing = np.float32(0.5) * (thickness[1:] + thickness[:-1])
    inv_spacing = np.concatenate([np.float32(1.0) / spacing, np.ones((1,), np.float32)])
    return [jnp.asarray(t.astype(np.float32)) for t in (thickness, inverse, zmid, inv_spacing)]


def on_device(
    heat_anomaly,
    brine_anomaly,
    eastward_current,
    northward_current,
    shoreline_indicator,
    bottom_layer_index,
    boundary_fluxes,
):
    layers, rows, cols = heat_anomaly.shape
    fields = (heat_anomaly, brine_anomaly, eastward_current, northward_current)
    groups = layers // GROUP
    n_lat = lax.axis_size("lat")
    n_lon = lax.axis_size("lon")
    lat_idx = lax.axis_index("lat").astype(jnp.int32)
    is_last = (lat_idx == n_lat - 1).astype(jnp.int32).reshape(1)
    lat_info = jnp.stack([lat_idx, jnp.int32(n_lat)])

    smem = pl.BlockSpec(memory_space=pltpu.SMEM)
    vmem = pl.BlockSpec(memory_space=pltpu.VMEM)
    row_tiles = jax.ShapeDtypeStruct((layers + 1, rows, cols), jnp.float32)
    col_tiles = jax.ShapeDtypeStruct((groups + 1, rows, cols), jnp.float32)
    top, bot, right, left = pl.pallas_call(
        pack_kernel,
        out_shape=(row_tiles, row_tiles, col_tiles, col_tiles),
        in_specs=[smem] + [vmem] * 6,
        out_specs=(vmem,) * 4,
    )(is_last, shoreline_indicator, bottom_layer_index, *fields)

    from_south = lax.ppermute(top, "lat", [(i, i + 1) for i in range(n_lat - 1)])
    from_north = lax.ppermute(bot, "lat", [(i + 1, i) for i in range(n_lat - 1)])
    from_west = lax.ppermute(right, "lon", [(i, (i + 1) % n_lon) for i in range(n_lon)])
    from_east = lax.ppermute(left, "lon", [((i + 1) % n_lon, i) for i in range(n_lon)])
    last = (n_lat - 1) * n_lon
    fold, from_west, from_east = lax.optimization_barrier((top, from_west, from_east))
    from_fold = lax.ppermute(
        fold, ("lat", "lon"), [(last + x, last + n_lon - 1 - x) for x in range(n_lon)]
    )

    plane = jax.ShapeDtypeStruct((layers, rows, cols), jnp.float32)
    tables = level_tables(layers)
    divx = pl.pallas_call(
        xpart_kernel,
        out_shape=jax.ShapeDtypeStruct((4 * layers, rows, cols), jnp.float32),
        in_specs=[smem] * 3 + [vmem] * 8,
        out_specs=vmem,
        compiler_params=pltpu.CompilerParams(vmem_limit_bytes=16 * 1024 * 1024),
    )(lat_info, tables[0], tables[2], shoreline_indicator, bottom_layer_index, *fields,
      from_west, from_east)
    outs = pl.pallas_call(
        step_kernel,
        out_shape=(plane,) * 4,
        in_specs=[smem] * 5 + [vmem] * 11,
        out_specs=(pl.BlockSpec(memory_space=pl.ANY),) * 4,
        scratch_shapes=[
            pltpu.VMEM((4 * layers, rows, cols), jnp.float32),
            pltpu.VMEM((2 * layers, rows, cols), jnp.float32),
            pltpu.VMEM((layers, rows, cols), jnp.float32),
        ] + [pltpu.VMEM((layers, rows, cols), jnp.float32)] * 4 + [
            pltpu.SemaphoreType.DMA((groups, 4)),
        ],
        compiler_params=pltpu.CompilerParams(vmem_limit_bytes=16 * 1024 * 1024),
    )(
        lat_info, *tables,
        shoreline_indicator, bottom_layer_index, boundary_fluxes, *fields,
        from_south, from_north, from_fold, divx,
    )
    return tuple(outs)


def solution(mesh):
    in_specs = (
        P(None, "lat", "lon"),
        P(None, "lat", "lon"),
        P(None, "lat", "lon"),
        P(None, "lat", "lon"),
        P("lat", "lon"),
        P("lat", "lon"),
        P(None, "lat", "lon"),
    )
    out_specs = (
        P(None, "lat", "lon"),
        P(None, "lat", "lon"),
        P(None, "lat", "lon"),
        P(None, "lat", "lon"),
    )
    return jax.shard_map(
        on_device, mesh=mesh, in_specs=in_specs, out_specs=out_specs, check_vma=False
    )
```

```python
import numpy as np
import jax
import jax.numpy as jnp
from jax import lax
from jax.experimental import pallas as pl
from jax.experimental.pallas import tpu as pltpu
from jax.sharding import PartitionSpec as P

courant = 0.25
time_step = 0.2
gravity = 0.2
coriolis = 0.5
thermal = 0.6
thermal_sq = 0.1
haline = 0.8
mix_back = 5.0
mix_conv = 60.0
strat_scale = 2.0
momentum_mix = 2.0
bottom_drag = 1.0
surface_gain = 0.5

GROUP = 15


def density(warmth, saltiness, depth_column):
    return -thermal * warmth * (1.0 + thermal_sq * warmth + depth_column) + haline * saltiness


def face_weights(face_vel):
    return (
        0.5 * face_vel,
        jnp.maximum(face_vel, 0.0) * (1.0 / 6.0),
        jnp.minimum(face_vel, 0.0) * (1.0 / 6.0),
    )


def flux_divergence(right_w, left_w, m2, m1, q0, p1, p2):
    half_r, pos_r, neg_r = right_w
    half_l, pos_l, neg_l = left_w
    step_r = p1 - q0
    step_l = q0 - m1
    curv_0 = step_r - step_l
    curv_p = (p2 - p1) - step_r
    curv_m = step_l - (m1 - m2)
    flux_r = half_r * (q0 + p1) - (pos_r * curv_0 + neg_r * curv_p)
    flux_l = half_l * (m1 + q0) - (pos_l * curv_m + neg_l * curv_0)
    return flux_r - flux_l


def rolled(x, shift, axis):
    shift %= x.shape[axis]
    return x if shift == 0 else pltpu.roll(x, shift, axis)


def pack_kernel(
    last_ref, shore_ref, bottom_ref, t_ref, s_ref, u_ref, v_ref,
    top_ref, bot_ref, right_ref, left_ref,
):
    layers, rows, cols = t_ref.shape
    groups = layers // GROUP
    lane = lax.broadcasted_iota(jnp.int32, (rows, cols), 1)
    row = lax.broadcasted_iota(jnp.int32, (rows, cols), 0)
    dep = (shore_ref[...] * bottom_ref[...]).astype(jnp.float32)
    zero = jnp.zeros((rows, cols), jnp.float32)

    def pack_rows(vals, first):
        out = zero
        for c, val in enumerate(vals):
            out = jnp.where((row >> 1) == c, rolled(val, 2 * c - first, 0), out)
        return out

    def group_body(g, carry):
        right = zero
        left = zero
        for j in range(GROUP):
            k = g * GROUP + j
            w = (k.astype(jnp.float32) < dep).astype(jnp.float32)
            q = [r[k] * w for r in (t_ref, s_ref, u_ref, v_ref)]
            top_ref[k] = pack_rows(q, rows - 2)
            bot_ref[k] = pack_rows(q, 0)
            for c in range(4):
                m = j * 4 + c
                slot = (lane >> 1) == m
                right = jnp.where(slot, rolled(q[c], 2 * m - (cols - 2), 1), right)
                left = jnp.where(slot, rolled(q[c], 2 * m, 1), left)
        right_ref[g] = right
        left_ref[g] = left
        return carry

    lax.fori_loop(0, groups, group_body, 0)
    top_ref[layers] = pack_rows([dep], rows - 2)
    bot_ref[layers] = pack_rows([dep], 0)
    right_ref[groups] = jnp.where(lane < 2, rolled(dep, 2, 1), zero)
    left_ref[groups] = jnp.where(lane < 2, dep, zero)

    @pl.when(last_ref[0] == 1)
    def _():
        tiles = top_ref[...].reshape((layers + 1) * rows, cols)
        tile_row = lax.broadcasted_iota(jnp.int32, tiles.shape, 0) % rows
        sign = jnp.where(tile_row < 4, 1.0, -1.0)
        swapped = jnp.where(
            (tile_row & 1) == 0, rolled(tiles, -1, 0), rolled(tiles, 1, 0)
        ) * sign
        src_lane = lax.broadcasted_iota(jnp.int32, (cols, cols), 0)
        dst_lane = lax.broadcasted_iota(jnp.int32, (cols, cols), 1)
        reverse = (src_lane + dst_lane == cols - 1).astype(jnp.float32)
        flipped = jnp.dot(
            swapped, reverse, precision=lax.Precision.HIGHEST,
            preferred_element_type=jnp.float32,
        )
        top_ref[...] = flipped.reshape(layers + 1, rows, cols)


def xpart_kernel(
    lat_ref, h_ref, zmid_ref, shore_ref, bottom_ref, t_ref, s_ref, u_ref, v_ref,
    west_ref, east_ref, divx_ref,
):
    layers, rows, cols = t_ref.shape
    groups = layers // GROUP
    lane = lax.broadcasted_iota(jnp.int32, (rows, cols), 1)
    row = lax.broadcasted_iota(jnp.int32, (rows, cols), 0)
    total_rows = rows * lat_ref[1]
    row_ids = (lat_ref[0] * rows + row).astype(jnp.float32)
    turning = coriolis * (2.0 * (row_ids + 0.5) / total_rows.astype(jnp.float32) - 1.0)

    def xs(v, e, s):
        if s == 1:
            return pltpu.roll(jnp.where(lane == 0, e, v), cols - 1, 1)
        if s == 2:
            return pltpu.roll(jnp.where(lane < 2, e, v), cols - 2, 1)
        if s == -1:
            return pltpu.roll(jnp.where(lane == cols - 1, e, v), 1, 1)
        return pltpu.roll(jnp.where(lane >= cols - 2, e, v), 2, 1)

    def lon_edge(tile_e, tile_w, m):
        return jnp.where(lane < 64, rolled(tile_e, -2 * m, 1), rolled(tile_w, cols - 2 - 2 * m, 1))

    dep = (shore_ref[...] * bottom_ref[...]).astype(jnp.float32)
    dep_lon = lon_edge(east_ref[groups], west_ref[groups], 0)
    dep_xm = xs(dep, dep_lon, -1)
    dep_xp = xs(dep, dep_lon, 1)
    zero = jnp.zeros((rows, cols), jnp.float32)

    def group_body(g, carry):
        tile_e = east_ref[g]
        tile_w = west_ref[g]
        for j in range(GROUP):
            cum_xm, cum_xp = carry
            k = g * GROUP + j
            kf = k.astype(jnp.float32)
            h = h_ref[k]
            zmid = zmid_ref[k]
            w0 = (kf < dep).astype(jnp.float32)
            wxm = (kf < dep_xm).astype(jnp.float32)
            wxp = (kf < dep_xp).astype(jnp.float32)
            q = [r[k] * w0 for r in (t_ref, s_ref, u_ref, v_ref)]
            ex = [lon_edge(tile_e, tile_w, j * 4 + c) for c in range(4)]
            xsh = {s: [xs(q[c], ex[c], s) for c in range(4)] for s in (-2, -1, 1, 2)}
            a_r = 0.5 * (q[2] + xsh[1][2]) * w0 * wxp
            a_l = 0.5 * (xsh[-1][2] + q[2]) * wxm * w0
            w_r = face_weights(a_r)
            w_l = face_weights(a_l)
            part = [
                q[c] - courant * flux_divergence(
                    w_r, w_l, xsh[-2][c], xsh[-1][c], q[c], xsh[1][c], xsh[2][c]
                )
                for c in range(4)
            ]
            load_xm = density(xsh[-1][0], xsh[-1][1], zmid) * wxm * h
            load_xp = density(xsh[1][0], xsh[1][1], zmid) * wxp * h
            cum_xm = cum_xm + load_xm
            cum_xp = cum_xp + load_xp
            grad_x = 0.5 * ((cum_xp - 0.5 * load_xp) - (cum_xm - 0.5 * load_xm))
            part[2] = part[2] + time_step * (turning * q[3] - gravity * grad_x)
            part[3] = part[3] + time_step * (-turning * q[2])
            for c in range(4):
                divx_ref[c * layers + k] = part[c]
            carry = (cum_xm, cum_xp)
        return carry

    lax.fori_loop(0, groups, group_body, (zero, zero))


def step_kernel(
    lat_ref, h_ref, inv_h_ref, zmid_ref, inv_sp_ref,
    shore_ref, bottom_ref, flux_ref, t_ref, s_ref, u_ref, v_ref,
    south_ref, north_ref, fold_ref, divx_ref,
    o0_hbm, o1_hbm, o2_hbm, o3_hbm,
    star_scr, r_scr, rs_scr, o0_ref, o1_ref, o2_ref, o3_ref, out_sems,
):
    layers = t_ref.shape[0]
    rows, cols = t_ref.shape[1], t_ref.shape[2]
    groups = layers // GROUP
    lane = lax.broadcasted_iota(jnp.int32, (rows, cols), 1)
    row = lax.broadcasted_iota(jnp.int32, (rows, cols), 0)

    def ys(v, e, s):
        if s == 1:
            return pltpu.roll(jnp.where(row == 0, e, v), rows - 1, 0)
        if s == 2:
            return pltpu.roll(jnp.where(row < 2, e, v), rows - 2, 0)
        if s == -1:
            return pltpu.roll(jnp.where(row == rows - 1, e, v), 1, 0)
        return pltpu.roll(jnp.where(row >= rows - 2, e, v), 2, 0)

    def lat_edge(tile_n, tile_s, c):
        return jnp.where(row < 4, rolled(tile_n, -2 * c, 0), rolled(tile_s, rows - 2 - 2 * c, 0))

    dep = (shore_ref[...] * bottom_ref[...]).astype(jnp.float32)
    dep_lat = lat_edge(north_ref[layers] + fold_ref[layers], south_ref[layers], 0)
    dep_ym = ys(dep, dep_lat, -1)
    dep_yp = ys(dep, dep_lat, 1)
    zero = jnp.zeros((rows, cols), jnp.float32)

    def explicit(k, carry):
        cum_ym, cum_yp = carry
        kf = k.astype(jnp.float32)
        h = h_ref[k]
        zmid = zmid_ref[k]
        w0 = (kf < dep).astype(jnp.float32)
        wym = (kf < dep_ym).astype(jnp.float32)
        wyp = (kf < dep_yp).astype(jnp.float32)
        q = [r[k] * w0 for r in (t_ref, s_ref, u_ref, v_ref)]
        tile_n = north_ref[k] + fold_ref[k]
        tile_s = south_ref[k]
        ey = [lat_edge(tile_n, tile_s, c) for c in range(4)]
        ysh = {s: [ys(q[c], ey[c], s) for c in range(4)] for s in (-2, -1, 1, 2)}
        b_r = 0.5 * (q[3] + ysh[1][3]) * w0 * wyp
        b_l = 0.5 * (ysh[-1][3] + q[3]) * wym * w0
        w_r = face_weights(b_r)
        w_l = face_weights(b_l)
        adv = []
        for c in range(4):
            div_y = flux_divergence(w_r, w_l, ysh[-2][c], ysh[-1][c], q[c], ysh[1][c], ysh[2][c])
            adv.append(divx_ref[c * layers + k] - courant * div_y)
        load_ym = density(ysh[-1][0], ysh[-1][1], zmid) * wym * h
        load_yp = density(ysh[1][0], ysh[1][1], zmid) * wyp * h
        cum_ym = cum_ym + load_ym
        cum_yp = cum_yp + load_yp
        grad_y = 0.5 * ((cum_yp - 0.5 * load_yp) - (cum_ym - 0.5 * load_ym))
        star0 = adv[0] * w0
        star1 = adv[1] * w0
        star2 = adv[2] * w0
        star3 = (adv[3] - time_step * gravity * grad_y) * w0
        for c, val in enumerate((star0, star1, star2, star3)):
            star_scr[c * layers + k] = val
        rs_scr[k] = density(star0, star1, zmid)
        return (cum_ym, cum_yp)

    lag = 3
    carry_e = lax.fori_loop(0, lag, explicit, (zero, zero), unroll=True)

    surface_scale = surface_gain * inv_h_ref[0]
    w_top = (0.0 < dep).astype(jnp.float32)
    for c in range(4):
        star_scr[c * layers] = star_scr[c * layers] + flux_ref[c] * w_top * surface_scale

    def forward(k, carry):
        mix_prev, r_a, r_b, s0, s1, s2, s3 = carry
        kf = k.astype(jnp.float32)
        inv_h = inv_h_ref[k]
        nxt = jnp.minimum(k + 1, layers - 1)
        stratified = (rs_scr[nxt] - rs_scr[k]) * inv_sp_ref[k]
        sig = 1.0 / (1.0 + jnp.exp(stratified * (1.0 / strat_scale)))
        w_next = (kf + 1.0 < dep).astype(jnp.float32)
        mix = (mix_back + mix_conv * sig) * w_next
        mix = jnp.where(k < layers - 1, mix, 0.0)
        low_a = -mix_prev * inv_h
        up_a = -mix * inv_h
        cen_a = 1.0 - low_a - up_a
        low_b = -mix_prev * momentum_mix * inv_h
        up_b = -mix * momentum_mix * inv_h
        floor = (kf == dep - 1.0).astype(jnp.float32)
        cen_b = 1.0 - low_b - up_b + bottom_drag * floor * inv_h
        inv_a = 1.0 / (cen_a - low_a * r_a)
        inv_b = 1.0 / (cen_b - low_b * r_b)
        r_a = up_a * inv_a
        r_b = up_b * inv_b
        r_scr[k] = r_a
        r_scr[layers + k] = r_b
        s0 = (star_scr[k] - low_a * s0) * inv_a
        s1 = (star_scr[layers + k] - low_a * s1) * inv_a
        s2 = (star_scr[2 * layers + k] - low_b * s2) * inv_b
        s3 = (star_scr[3 * layers + k] - low_b * s3) * inv_b
        star_scr[k] = s0
        star_scr[layers + k] = s1
        star_scr[2 * layers + k] = s2
        star_scr[3 * layers + k] = s3
        return (mix, r_a, r_b, s0, s1, s2, s3)

    def fused(k, carry):
        carry_e, carry_f = carry
        return (explicit(k, carry_e), forward(k - lag, carry_f))

    _, carry_f = lax.fori_loop(lag, layers, fused, (carry_e, (zero,) * 7), unroll=12)
    lax.fori_loop(layers - lag, layers, forward, carry_f, unroll=True)

    def backward(i, carry):
        x0, x1, x2, x3 = carry
        k = layers - 1 - i
        r_a = r_scr[k]
        r_b = r_scr[layers + k]
        x0 = star_scr[k] - r_a * x0
        x1 = star_scr[layers + k] - r_a * x1
        x2 = star_scr[2 * layers + k] - r_b * x2
        x3 = star_scr[3 * layers + k] - r_b * x3
        o0_ref[k] = x0
        o1_ref[k] = x1
        o2_ref[k] = x2
        o3_ref[k] = x3
        return (x0, x1, x2, x3)

    pairs = ((o0_ref, o0_hbm), (o1_ref, o1_hbm), (o2_ref, o2_hbm), (o3_ref, o3_hbm))
    writes = []
    carry = (zero,) * 4
    for chunk in range(groups):
        carry = lax.fori_loop(chunk * GROUP, (chunk + 1) * GROUP, backward, carry, unroll=5)
        span = pl.ds(layers - (chunk + 1) * GROUP, GROUP)
        for c, (src, dst) in enumerate(pairs):
            write = pltpu.make_async_copy(src.at[span], dst.at[span], out_sems.at[chunk, c])
            write.start()
            writes.append(write)
    for write in writes:
        write.wait()


def level_tables(layers):
    offsets = np.arange(layers, dtype=np.float32) + np.float32(0.5)
    zmid = offsets / np.float32(layers)
    thickness = np.float32(0.5) + zmid
    inverse = np.float32(1.0) / thickness
    spacing = np.float32(0.5) * (thickness[1:] + thickness[:-1])
    inv_spacing = np.concatenate([np.float32(1.0) / spacing, np.ones((1,), np.float32)])
    return [jnp.asarray(t.astype(np.float32)) for t in (thickness, inverse, zmid, inv_spacing)]


def on_device(
    heat_anomaly,
    brine_anomaly,
    eastward_current,
    northward_current,
    shoreline_indicator,
    bottom_layer_index,
    boundary_fluxes,
):
    layers, rows, cols = heat_anomaly.shape
    fields = (heat_anomaly, brine_anomaly, eastward_current, northward_current)
    groups = layers // GROUP
    n_lat = lax.axis_size("lat")
    n_lon = lax.axis_size("lon")
    lat_idx = lax.axis_index("lat").astype(jnp.int32)
    is_last = (lat_idx == n_lat - 1).astype(jnp.int32).reshape(1)
    lat_info = jnp.stack([lat_idx, jnp.int32(n_lat)])

    smem = pl.BlockSpec(memory_space=pltpu.SMEM)
    vmem = pl.BlockSpec(memory_space=pltpu.VMEM)
    row_tiles = jax.ShapeDtypeStruct((layers + 1, rows, cols), jnp.float32)
    col_tiles = jax.ShapeDtypeStruct((groups + 1, rows, cols), jnp.float32)
    top, bot, right, left = pl.pallas_call(
        pack_kernel,
        out_shape=(row_tiles, row_tiles, col_tiles, col_tiles),
        in_specs=[smem] + [vmem] * 6,
        out_specs=(vmem,) * 4,
    )(is_last, shoreline_indicator, bottom_layer_index, *fields)

    from_south = lax.ppermute(top, "lat", [(i, i + 1) for i in range(n_lat - 1)])
    from_north = lax.ppermute(bot, "lat", [(i + 1, i) for i in range(n_lat - 1)])
    from_west = lax.ppermute(right, "lon", [(i, (i + 1) % n_lon) for i in range(n_lon)])
    from_east = lax.ppermute(left, "lon", [((i + 1) % n_lon, i) for i in range(n_lon)])
    last = (n_lat - 1) * n_lon
    fold, from_west, from_east = lax.optimization_barrier((top, from_west, from_east))
    from_fold = lax.ppermute(
        fold, ("lat", "lon"), [(last + x, last + n_lon - 1 - x) for x in range(n_lon)]
    )

    plane = jax.ShapeDtypeStruct((layers, rows, cols), jnp.float32)
    tables = level_tables(layers)
    divx = pl.pallas_call(
        xpart_kernel,
        out_shape=jax.ShapeDtypeStruct((4 * layers, rows, cols), jnp.float32),
        in_specs=[smem] * 3 + [vmem] * 8,
        out_specs=vmem,
        compiler_params=pltpu.CompilerParams(vmem_limit_bytes=16 * 1024 * 1024),
    )(lat_info, tables[0], tables[2], shoreline_indicator, bottom_layer_index, *fields,
      from_west, from_east)
    outs = pl.pallas_call(
        step_kernel,
        out_shape=(plane,) * 4,
        in_specs=[smem] * 5 + [vmem] * 11,
        out_specs=(pl.BlockSpec(memory_space=pl.ANY),) * 4,
        scratch_shapes=[
            pltpu.VMEM((4 * layers, rows, cols), jnp.float32),
            pltpu.VMEM((2 * layers, rows, cols), jnp.float32),
            pltpu.VMEM((layers, rows, cols), jnp.float32),
        ] + [pltpu.VMEM((layers, rows, cols), jnp.float32)] * 4 + [
            pltpu.SemaphoreType.DMA((groups, 4)),
        ],
        compiler_params=pltpu.CompilerParams(vmem_limit_bytes=16 * 1024 * 1024),
    )(
        lat_info, *tables,
        shoreline_indicator, bottom_layer_index, boundary_fluxes, *fields,
        from_south, from_north, from_fold, divx,
    )
    return tuple(outs)


def solution(mesh):
    in_specs = (
        P(None, "lat", "lon"),
        P(None, "lat", "lon"),
        P(None, "lat", "lon"),
        P(None, "lat", "lon"),
        P("lat", "lon"),
        P("lat", "lon"),
        P(None, "lat", "lon"),
    )
    out_specs = (
        P(None, "lat", "lon"),
        P(None, "lat", "lon"),
        P(None, "lat", "lon"),
        P(None, "lat", "lon"),
    )
    return jax.shard_map(
        on_device, mesh=mesh, in_specs=in_specs, out_specs=out_specs, check_vma=False
    )
```

```python
import numpy as np
import jax
import jax.numpy as jnp
from jax import lax
from jax.experimental import pallas as pl
from jax.experimental.pallas import tpu as pltpu
from jax.sharding import PartitionSpec as P

courant = 0.25
time_step = 0.2
gravity = 0.2
coriolis = 0.5
thermal = 0.6
thermal_sq = 0.1
haline = 0.8
mix_back = 5.0
mix_conv = 60.0
strat_scale = 2.0
momentum_mix = 2.0
bottom_drag = 1.0
surface_gain = 0.5

GROUP = 15


def density(warmth, saltiness, depth_column):
    return -thermal * warmth * (1.0 + thermal_sq * warmth + depth_column) + haline * saltiness


def face_weights(face_vel):
    return (
        0.5 * face_vel,
        jnp.maximum(face_vel, 0.0) * (1.0 / 6.0),
        jnp.minimum(face_vel, 0.0) * (1.0 / 6.0),
    )


def flux_divergence(right_w, left_w, m2, m1, q0, p1, p2):
    half_r, pos_r, neg_r = right_w
    half_l, pos_l, neg_l = left_w
    step_r = p1 - q0
    step_l = q0 - m1
    curv_0 = step_r - step_l
    curv_p = (p2 - p1) - step_r
    curv_m = step_l - (m1 - m2)
    flux_r = half_r * (q0 + p1) - (pos_r * curv_0 + neg_r * curv_p)
    flux_l = half_l * (m1 + q0) - (pos_l * curv_m + neg_l * curv_0)
    return flux_r - flux_l


def rolled(x, shift, axis):
    shift %= x.shape[axis]
    return x if shift == 0 else pltpu.roll(x, shift, axis)


def pack_kernel(
    last_ref, shore_ref, bottom_ref, t_ref, s_ref, u_ref, v_ref,
    top_ref, bot_ref, right_ref, left_ref,
):
    layers, rows, cols = t_ref.shape
    groups = layers // GROUP
    lane = lax.broadcasted_iota(jnp.int32, (rows, cols), 1)
    row = lax.broadcasted_iota(jnp.int32, (rows, cols), 0)
    dep = (shore_ref[...] * bottom_ref[...]).astype(jnp.float32)
    zero = jnp.zeros((rows, cols), jnp.float32)

    def pack_rows(vals, first):
        out = zero
        for c, val in enumerate(vals):
            out = jnp.where((row >> 1) == c, rolled(val, 2 * c - first, 0), out)
        return out

    def group_body(g, carry):
        right = zero
        left = zero
        for j in range(GROUP):
            k = g * GROUP + j
            w = (k.astype(jnp.float32) < dep).astype(jnp.float32)
            q = [r[k] * w for r in (t_ref, s_ref, u_ref, v_ref)]
            top_ref[k] = pack_rows(q, rows - 2)
            bot_ref[k] = pack_rows(q, 0)
            for c in range(4):
                m = j * 4 + c
                slot = (lane >> 1) == m
                right = jnp.where(slot, rolled(q[c], 2 * m - (cols - 2), 1), right)
                left = jnp.where(slot, rolled(q[c], 2 * m, 1), left)
        right_ref[g] = right
        left_ref[g] = left
        return carry

    lax.fori_loop(0, groups, group_body, 0, unroll=True)
    top_ref[layers] = pack_rows([dep], rows - 2)
    bot_ref[layers] = pack_rows([dep], 0)
    right_ref[groups] = jnp.where(lane < 2, rolled(dep, 2, 1), zero)
    left_ref[groups] = jnp.where(lane < 2, dep, zero)

    @pl.when(last_ref[0] == 1)
    def _():
        tiles = top_ref[...].reshape((layers + 1) * rows, cols)
        tile_row = lax.broadcasted_iota(jnp.int32, tiles.shape, 0) % rows
        sign = jnp.where(tile_row < 4, 1.0, -1.0)
        swapped = jnp.where(
            (tile_row & 1) == 0, rolled(tiles, -1, 0), rolled(tiles, 1, 0)
        ) * sign
        src_lane = lax.broadcasted_iota(jnp.int32, (cols, cols), 0)
        dst_lane = lax.broadcasted_iota(jnp.int32, (cols, cols), 1)
        reverse = (src_lane + dst_lane == cols - 1).astype(jnp.float32)
        flipped = jnp.dot(
            swapped, reverse, precision=lax.Precision.HIGHEST,
            preferred_element_type=jnp.float32,
        )
        top_ref[...] = flipped.reshape(layers + 1, rows, cols)


def xpart_kernel(
    lat_ref, h_ref, zmid_ref, shore_ref, bottom_ref, t_ref, s_ref, u_ref, v_ref,
    west_ref, east_ref, divx_ref,
):
    layers, rows, cols = t_ref.shape
    groups = layers // GROUP
    lane = lax.broadcasted_iota(jnp.int32, (rows, cols), 1)
    row = lax.broadcasted_iota(jnp.int32, (rows, cols), 0)
    total_rows = rows * lat_ref[1]
    row_ids = (lat_ref[0] * rows + row).astype(jnp.float32)
    turning = coriolis * (2.0 * (row_ids + 0.5) / total_rows.astype(jnp.float32) - 1.0)

    def xs(v, e, s):
        if s == 1:
            return pltpu.roll(jnp.where(lane == 0, e, v), cols - 1, 1)
        if s == 2:
            return pltpu.roll(jnp.where(lane < 2, e, v), cols - 2, 1)
        if s == -1:
            return pltpu.roll(jnp.where(lane == cols - 1, e, v), 1, 1)
        return pltpu.roll(jnp.where(lane >= cols - 2, e, v), 2, 1)

    def lon_edge(tile_e, tile_w, m):
        return jnp.where(lane < 64, rolled(tile_e, -2 * m, 1), rolled(tile_w, cols - 2 - 2 * m, 1))

    dep = (shore_ref[...] * bottom_ref[...]).astype(jnp.float32)
    dep_lon = lon_edge(east_ref[groups], west_ref[groups], 0)
    dep_xm = xs(dep, dep_lon, -1)
    dep_xp = xs(dep, dep_lon, 1)
    zero = jnp.zeros((rows, cols), jnp.float32)

    def group_body(g, carry):
        tile_e = east_ref[g]
        tile_w = west_ref[g]
        for j in range(GROUP):
            cum_xm, cum_xp = carry
            k = g * GROUP + j
            kf = k.astype(jnp.float32)
            h = h_ref[k]
            zmid = zmid_ref[k]
            w0 = (kf < dep).astype(jnp.float32)
            wxm = (kf < dep_xm).astype(jnp.float32)
            wxp = (kf < dep_xp).astype(jnp.float32)
            q = [r[k] * w0 for r in (t_ref, s_ref, u_ref, v_ref)]
            ex = [lon_edge(tile_e, tile_w, j * 4 + c) for c in range(4)]
            xsh = {s: [xs(q[c], ex[c], s) for c in range(4)] for s in (-2, -1, 1, 2)}
            a_r = 0.5 * (q[2] + xsh[1][2]) * w0 * wxp
            a_l = 0.5 * (xsh[-1][2] + q[2]) * wxm * w0
            w_r = face_weights(a_r)
            w_l = face_weights(a_l)
            part = [
                q[c] - courant * flux_divergence(
                    w_r, w_l, xsh[-2][c], xsh[-1][c], q[c], xsh[1][c], xsh[2][c]
                )
                for c in range(4)
            ]
            load_xm = density(xsh[-1][0], xsh[-1][1], zmid) * wxm * h
            load_xp = density(xsh[1][0], xsh[1][1], zmid) * wxp * h
            cum_xm = cum_xm + load_xm
            cum_xp = cum_xp + load_xp
            grad_x = 0.5 * ((cum_xp - 0.5 * load_xp) - (cum_xm - 0.5 * load_xm))
            part[2] = part[2] + time_step * (turning * q[3] - gravity * grad_x)
            part[3] = part[3] + time_step * (-turning * q[2])
            for c in range(4):
                divx_ref[c * layers + k] = part[c]
            carry = (cum_xm, cum_xp)
        return carry

    lax.fori_loop(0, groups, group_body, (zero, zero))


def step_kernel(
    lat_ref, h_ref, inv_h_ref, zmid_ref, inv_sp_ref,
    shore_ref, bottom_ref, flux_ref, t_ref, s_ref, u_ref, v_ref,
    south_ref, north_ref, fold_ref, divx_ref,
    o0_hbm, o1_hbm, o2_hbm, o3_hbm,
    star_scr, r_scr, rs_scr, o0_ref, o1_ref, o2_ref, o3_ref, out_sems,
):
    layers = t_ref.shape[0]
    rows, cols = t_ref.shape[1], t_ref.shape[2]
    groups = layers // GROUP
    lane = lax.broadcasted_iota(jnp.int32, (rows, cols), 1)
    row = lax.broadcasted_iota(jnp.int32, (rows, cols), 0)

    def ys(v, e, s):
        if s == 1:
            return pltpu.roll(jnp.where(row == 0, e, v), rows - 1, 0)
        if s == 2:
            return pltpu.roll(jnp.where(row < 2, e, v), rows - 2, 0)
        if s == -1:
            return pltpu.roll(jnp.where(row == rows - 1, e, v), 1, 0)
        return pltpu.roll(jnp.where(row >= rows - 2, e, v), 2, 0)

    def lat_edge(tile_n, tile_s, c):
        return jnp.where(row < 4, rolled(tile_n, -2 * c, 0), rolled(tile_s, rows - 2 - 2 * c, 0))

    dep = (shore_ref[...] * bottom_ref[...]).astype(jnp.float32)
    dep_lat = lat_edge(north_ref[layers] + fold_ref[layers], south_ref[layers], 0)
    dep_ym = ys(dep, dep_lat, -1)
    dep_yp = ys(dep, dep_lat, 1)
    zero = jnp.zeros((rows, cols), jnp.float32)

    def explicit(k, carry):
        cum_ym, cum_yp = carry
        kf = k.astype(jnp.float32)
        h = h_ref[k]
        zmid = zmid_ref[k]
        w0 = (kf < dep).astype(jnp.float32)
        wym = (kf < dep_ym).astype(jnp.float32)
        wyp = (kf < dep_yp).astype(jnp.float32)
        q = [r[k] * w0 for r in (t_ref, s_ref, u_ref, v_ref)]
        tile_n = north_ref[k] + fold_ref[k]
        tile_s = south_ref[k]
        ey = [lat_edge(tile_n, tile_s, c) for c in range(4)]
        ysh = {s: [ys(q[c], ey[c], s) for c in range(4)] for s in (-2, -1, 1, 2)}
        b_r = 0.5 * (q[3] + ysh[1][3]) * w0 * wyp
        b_l = 0.5 * (ysh[-1][3] + q[3]) * wym * w0
        w_r = face_weights(b_r)
        w_l = face_weights(b_l)
        adv = []
        for c in range(4):
            div_y = flux_divergence(w_r, w_l, ysh[-2][c], ysh[-1][c], q[c], ysh[1][c], ysh[2][c])
            adv.append(divx_ref[c * layers + k] - courant * div_y)
        load_ym = density(ysh[-1][0], ysh[-1][1], zmid) * wym * h
        load_yp = density(ysh[1][0], ysh[1][1], zmid) * wyp * h
        cum_ym = cum_ym + load_ym
        cum_yp = cum_yp + load_yp
        grad_y = 0.5 * ((cum_yp - 0.5 * load_yp) - (cum_ym - 0.5 * load_ym))
        star0 = adv[0] * w0
        star1 = adv[1] * w0
        star2 = adv[2] * w0
        star3 = (adv[3] - time_step * gravity * grad_y) * w0
        for c, val in enumerate((star0, star1, star2, star3)):
            star_scr[c * layers + k] = val
        rs_scr[k] = density(star0, star1, zmid)
        return (cum_ym, cum_yp)

    lag = 3
    carry_e = lax.fori_loop(0, lag, explicit, (zero, zero), unroll=True)

    surface_scale = surface_gain * inv_h_ref[0]
    w_top = (0.0 < dep).astype(jnp.float32)
    for c in range(4):
        star_scr[c * layers] = star_scr[c * layers] + flux_ref[c] * w_top * surface_scale

    def forward(k, carry):
        mix_prev, r_a, r_b, s0, s1, s2, s3 = carry
        kf = k.astype(jnp.float32)
        inv_h = inv_h_ref[k]
        nxt = jnp.minimum(k + 1, layers - 1)
        stratified = (rs_scr[nxt] - rs_scr[k]) * inv_sp_ref[k]
        sig = 1.0 / (1.0 + jnp.exp(stratified * (1.0 / strat_scale)))
        w_next = (kf + 1.0 < dep).astype(jnp.float32)
        mix = (mix_back + mix_conv * sig) * w_next
        mix = jnp.where(k < layers - 1, mix, 0.0)
        low_a = -mix_prev * inv_h
        up_a = -mix * inv_h
        cen_a = 1.0 - low_a - up_a
        low_b = -mix_prev * momentum_mix * inv_h
        up_b = -mix * momentum_mix * inv_h
        floor = (kf == dep - 1.0).astype(jnp.float32)
        cen_b = 1.0 - low_b - up_b + bottom_drag * floor * inv_h
        inv_a = 1.0 / (cen_a - low_a * r_a)
        inv_b = 1.0 / (cen_b - low_b * r_b)
        r_a = up_a * inv_a
        r_b = up_b * inv_b
        r_scr[k] = r_a
        r_scr[layers + k] = r_b
        s0 = (star_scr[k] - low_a * s0) * inv_a
        s1 = (star_scr[layers + k] - low_a * s1) * inv_a
        s2 = (star_scr[2 * layers + k] - low_b * s2) * inv_b
        s3 = (star_scr[3 * layers + k] - low_b * s3) * inv_b
        star_scr[k] = s0
        star_scr[layers + k] = s1
        star_scr[2 * layers + k] = s2
        star_scr[3 * layers + k] = s3
        return (mix, r_a, r_b, s0, s1, s2, s3)

    def fused(k, carry):
        carry_e, carry_f = carry
        return (explicit(k, carry_e), forward(k - lag, carry_f))

    _, carry_f = lax.fori_loop(lag, layers, fused, (carry_e, (zero,) * 7), unroll=9)
    lax.fori_loop(layers - lag, layers, forward, carry_f, unroll=True)

    def backward(i, carry):
        x0, x1, x2, x3 = carry
        k = layers - 1 - i
        r_a = r_scr[k]
        r_b = r_scr[layers + k]
        x0 = star_scr[k] - r_a * x0
        x1 = star_scr[layers + k] - r_a * x1
        x2 = star_scr[2 * layers + k] - r_b * x2
        x3 = star_scr[3 * layers + k] - r_b * x3
        o0_ref[k] = x0
        o1_ref[k] = x1
        o2_ref[k] = x2
        o3_ref[k] = x3
        return (x0, x1, x2, x3)

    pairs = ((o0_ref, o0_hbm), (o1_ref, o1_hbm), (o2_ref, o2_hbm), (o3_ref, o3_hbm))
    writes = []
    carry = (zero,) * 4
    for chunk in range(groups):
        carry = lax.fori_loop(chunk * GROUP, (chunk + 1) * GROUP, backward, carry, unroll=5)
        span = pl.ds(layers - (chunk + 1) * GROUP, GROUP)
        for c, (src, dst) in enumerate(pairs):
            write = pltpu.make_async_copy(src.at[span], dst.at[span], out_sems.at[chunk, c])
            write.start()
            writes.append(write)
    for write in writes:
        write.wait()


def level_tables(layers):
    offsets = np.arange(layers, dtype=np.float32) + np.float32(0.5)
    zmid = offsets / np.float32(layers)
    thickness = np.float32(0.5) + zmid
    inverse = np.float32(1.0) / thickness
    spacing = np.float32(0.5) * (thickness[1:] + thickness[:-1])
    inv_spacing = np.concatenate([np.float32(1.0) / spacing, np.ones((1,), np.float32)])
    return [jnp.asarray(t.astype(np.float32)) for t in (thickness, inverse, zmid, inv_spacing)]


def on_device(
    heat_anomaly,
    brine_anomaly,
    eastward_current,
    northward_current,
    shoreline_indicator,
    bottom_layer_index,
    boundary_fluxes,
):
    layers, rows, cols = heat_anomaly.shape
    fields = (heat_anomaly, brine_anomaly, eastward_current, northward_current)
    groups = layers // GROUP
    n_lat = lax.axis_size("lat")
    n_lon = lax.axis_size("lon")
    lat_idx = lax.axis_index("lat").astype(jnp.int32)
    is_last = (lat_idx == n_lat - 1).astype(jnp.int32).reshape(1)
    lat_info = jnp.stack([lat_idx, jnp.int32(n_lat)])

    smem = pl.BlockSpec(memory_space=pltpu.SMEM)
    vmem = pl.BlockSpec(memory_space=pltpu.VMEM)
    row_tiles = jax.ShapeDtypeStruct((layers + 1, rows, cols), jnp.float32)
    col_tiles = jax.ShapeDtypeStruct((groups + 1, rows, cols), jnp.float32)
    top, bot, right, left = pl.pallas_call(
        pack_kernel,
        out_shape=(row_tiles, row_tiles, col_tiles, col_tiles),
        in_specs=[smem] + [vmem] * 6,
        out_specs=(vmem,) * 4,
    )(is_last, shoreline_indicator, bottom_layer_index, *fields)

    from_south = lax.ppermute(top, "lat", [(i, i + 1) for i in range(n_lat - 1)])
    from_north = lax.ppermute(bot, "lat", [(i + 1, i) for i in range(n_lat - 1)])
    from_west = lax.ppermute(right, "lon", [(i, (i + 1) % n_lon) for i in range(n_lon)])
    from_east = lax.ppermute(left, "lon", [((i + 1) % n_lon, i) for i in range(n_lon)])
    last = (n_lat - 1) * n_lon
    fold, from_west, from_east = lax.optimization_barrier((top, from_west, from_east))
    from_fold = lax.ppermute(
        fold, ("lat", "lon"), [(last + x, last + n_lon - 1 - x) for x in range(n_lon)]
    )

    plane = jax.ShapeDtypeStruct((layers, rows, cols), jnp.float32)
    tables = level_tables(layers)
    divx = pl.pallas_call(
        xpart_kernel,
        out_shape=jax.ShapeDtypeStruct((4 * layers, rows, cols), jnp.float32),
        in_specs=[smem] * 3 + [vmem] * 8,
        out_specs=vmem,
        compiler_params=pltpu.CompilerParams(vmem_limit_bytes=16 * 1024 * 1024),
    )(lat_info, tables[0], tables[2], shoreline_indicator, bottom_layer_index, *fields,
      from_west, from_east)
    outs = pl.pallas_call(
        step_kernel,
        out_shape=(plane,) * 4,
        in_specs=[smem] * 5 + [vmem] * 11,
        out_specs=(pl.BlockSpec(memory_space=pl.ANY),) * 4,
        scratch_shapes=[
            pltpu.VMEM((4 * layers, rows, cols), jnp.float32),
            pltpu.VMEM((2 * layers, rows, cols), jnp.float32),
            pltpu.VMEM((layers, rows, cols), jnp.float32),
        ] + [pltpu.VMEM((layers, rows, cols), jnp.float32)] * 4 + [
            pltpu.SemaphoreType.DMA((groups, 4)),
        ],
        compiler_params=pltpu.CompilerParams(vmem_limit_bytes=16 * 1024 * 1024),
    )(
        lat_info, *tables,
        shoreline_indicator, bottom_layer_index, boundary_fluxes, *fields,
        from_south, from_north, from_fold, divx,
    )
    return tuple(outs)


def solution(mesh):
    in_specs = (
        P(None, "lat", "lon"),
        P(None, "lat", "lon"),
        P(None, "lat", "lon"),
        P(None, "lat", "lon"),
        P("lat", "lon"),
        P("lat", "lon"),
        P(None, "lat", "lon"),
    )
    out_specs = (
        P(None, "lat", "lon"),
        P(None, "lat", "lon"),
        P(None, "lat", "lon"),
        P(None, "lat", "lon"),
    )
    return jax.shard_map(
        on_device, mesh=mesh, in_specs=in_specs, out_specs=out_specs, check_vma=False
    )
```
